256 devices in a mesh: grid: 16 (over y_hi, z), states: 16 (over y_lo, x, core).
Axes of the slice: x: 4, y: 4 (y_hi: 2, y_lo: 2; y = y_hi * 2 + y_lo), z: 8, core: 2. Of those that a mesh axis runs over, the one named last changes fastest.
Arguments:
- states_in: float32 [16, 256, 32, 128], P('states', 'grid'), may hold values from -10 to 10
- potential: float32 [256, 32, 128], P('grid'), may hold values from -2 to 0.5
- projectors: bfloat16 [16, 32, 8, 4096], P('grid', 'states'), may hold values from -0.0625 to 0.0625
- proj_gains: bfloat16 [16, 32, 8], P('grid', 'states'), may hold values from 1 to 6
- atom_owner: int32 [160], P('grid'), may hold values from 0 to 15, as said below
- atom_rows: int32 [160, 32], P('grid'), may hold values from -1 to 8191, as said below
- wrap_rows: int32 [32], replicated, may hold values from 0 to 31, as said below
Outputs:
- filtered: float32 [16, 256, 32, 128], P('states', 'grid')
The draws below stay inside these ranges and needn't reach their ends.
Inputs may be any that keep to these rules, and one draw needn't show every extreme that they name: `atom_owner`: atom a belongs to tile a // 10. At most 2 atoms of one tile share an owner, and one owner takes exactly 2 atoms of every tile. `atom_rows`: A row r is the line of cells at x = r // 32, y = r % 32. Each list holds distinct rows whose x lies in the atom's own tile of 16 planes, followed by -1 entries; each list has 16 rows or more, and the first atom of every tile fills all 32. wrap_rows[y] = (y + t) mod 32 for one t of 1 to 31.
All inputs are finite; a program needn't handle non-finite values.
Results may differ from the reference program's by a relative error of at most 0.00082.
Values may be sent and summed in bfloat16 or wider, within the bound.
No kernel may reach another device: no remote copies, remote signals or barrier semaphores. Data moves between devices by JAX's collectives and lax.ppermute only.
A program may use at most 64 MiB of HBM per device.

```python
import math
import jax
import jax.numpy as jnp
from jax import lax

STATES_DEV = 1
CX = 16
NY = 32
NZ = 128
RADIUS = 6
NPROJ = 8
BLK = 32
HOME_ATOMS = 10
PAIR_CAP = 2
NSTATES = 16
NX = 256
OWNERS = 16
ATOMS = 160
SLOTS = 32
N_STATES = 16


def draw_atom_owner(key, part):
    subkeys = jax.random.split(jax.random.fold_in(key, 11), 2)
    busy_owner = jax.random.randint(subkeys[0], (), 0, OWNERS)

    def one_home(home_key):
        key_a, key_b, key_c = jax.random.split(home_key, 3)
        others = jax.random.permutation(key_a, OWNERS - 1)
        others = others + (others >= busy_owner).astype(jnp.int32)
        offset_flip = jax.random.randint(key_b, (), 0, 2)
        slot_order = jnp.arange(HOME_ATOMS, dtype=jnp.int32)
        other_index = jnp.maximum(slot_order - 2 + offset_flip, 0) // 2
        owner_list = jnp.where(slot_order < 2, busy_owner, others[other_index])
        return jax.random.permutation(key_c, owner_list)
    homes = jax.vmap(one_home)(jax.random.split(subkeys[1], OWNERS))
    return homes.reshape(-1).astype(jnp.int32)


def draw_atom_rows(key, part):
    tile_lines = CX * NY
    atom_ids = jnp.arange(ATOMS, dtype=jnp.int32)

    def one_atom(atom_key, atom_id):
        key_a, key_b = jax.random.split(atom_key)
        chosen = jax.random.permutation(key_a, tile_lines)[:BLK]
        live_count = jax.random.randint(key_b, (), BLK // 2, BLK + 1)
        live_count = jnp.where(atom_id % HOME_ATOMS == 0, BLK, live_count)
        row_list = atom_id // HOME_ATOMS * tile_lines + chosen
        return jnp.where(jnp.arange(BLK) < live_count, row_list, -1).astype(jnp.int32)
    return jax.vmap(one_atom)(jax.random.split(jax.random.fold_in(key, 23), ATOMS), atom_ids)


def draw_wrap_rows(key, part):
    skew_shift = jax.random.randint(jax.random.fold_in(key, 37), (), 1, NY)
    return ((jnp.arange(NY, dtype=jnp.int32) + skew_shift) % NY).astype(jnp.int32)


def projector_values(key):
    scale_factor = (BLK * NZ) ** (-0.5)
    full_shape = (OWNERS, SLOTS, NPROJ, BLK * NZ)
    proj_key = jax.random.fold_in(key, 41)
    raw_values = jax.random.truncated_normal(proj_key, -4.0, 4.0, full_shape, jnp.float32)
    return raw_values * scale_factor


def draw_projectors(key, part):
    return projector_values(key).astype(jnp.bfloat16)


def draw_states_in(key, part):
    spread = 0.25 * (BLK * NZ) ** 0.5
    owner_table = draw_atom_owner(key, part).reshape(OWNERS, HOME_ATOMS)
    row_lists = draw_atom_rows(key, part)
    home_order = jnp.arange(HOME_ATOMS, dtype=jnp.int32)
    same_owner = (owner_table[:, :, None] == owner_table[:, None, :]) & (home_order[None, None, :] < home_order[None, :, None])
    owner_rank = jnp.sum(same_owner.astype(jnp.int32), axis=2)
    home_index = jnp.arange(OWNERS, dtype=jnp.int32)[:, None]
    slot_index = (owner_table * SLOTS + home_index * PAIR_CAP + owner_rank).reshape(-1).astype(jnp.int32)
    atom_proj = jnp.take(projector_values(key).reshape(OWNERS * SLOTS, NPROJ, BLK * NZ), slot_index, axis=0)
    safe_rows = jnp.where(row_lists >= 0, row_lists, NX * NY).reshape(-1).astype(jnp.int32)
    noise_key = jax.random.fold_in(key, 53)
    mixing_key = jax.random.fold_in(key, 59)
    line_shape = (NSTATES, NX * NY, NZ)
    mixing_shape = (NSTATES, ATOMS, NPROJ)
    base_lines = jax.random.truncated_normal(noise_key, -4.0, 4.0, line_shape, jnp.float32)
    mixing = jax.random.truncated_normal(mixing_key, -3.0, 3.0, mixing_shape, jnp.float32) * spread

    def one_state(state_pair):
        line_values, state_mixing = state_pair
        aligned = jnp.zeros((ATOMS, BLK * NZ), jnp.float32)
        for proj_index in range(NPROJ):
            aligned = aligned + atom_proj[:, proj_index] * state_mixing[:, proj_index][:, None]
        return line_values.at[safe_rows].add(aligned.reshape(ATOMS * BLK, NZ), mode='drop')
    states = lax.map(one_state, (base_lines, mixing))
    return jnp.clip(states, -10.0, 10.0).reshape(NSTATES, NX, NY, NZ)


def block_levels(rng, shape, cuts, least, high):
    factor_of, own = 1.0, jax.random.fold_in(rng, 6)
    for axis_at, parts in cuts:
        steps = jnp.exp(jax.random.uniform(jax.random.fold_in(own, axis_at), (parts,), jnp.float32, least / len(cuts), high / len(cuts)))
        factor_of = factor_of * jnp.repeat(steps, shape[axis_at] // parts).reshape([-1 if axis == axis_at else 1 for axis in range(len(shape))])
    return factor_of


def setup_inputs(seed: int = 0) -> dict:
    keys = jax.random.split(jax.random.key(seed), 8)
    states_in = draw_states_in(jax.random.fold_in(keys[7], 71), 0)
    potential = jnp.clip(-2.0 + 2.5 * jax.random.uniform(keys[1], (NX, NY, NZ), jnp.float32) ** block_levels(keys[1], (NX, NY, NZ), ((0, 16),), -0.2, 0.2), -2.0, 0.5)
    projectors = draw_projectors(jax.random.fold_in(keys[7], 71), 0)
    proj_gains = jnp.clip(1.0 + 5.0 * jax.random.uniform(keys[3], (OWNERS, SLOTS, NPROJ), jnp.float32) ** block_levels(keys[3], (OWNERS, SLOTS, NPROJ), ((0, 16), (1, 16)), -0.2, 0.2), 1.0, 6.0).astype(jnp.bfloat16)
    atom_owner = draw_atom_owner(jax.random.fold_in(keys[7], 71), 0)
    atom_rows = draw_atom_rows(jax.random.fold_in(keys[7], 71), 0)
    wrap_rows = draw_wrap_rows(jax.random.fold_in(keys[7], 71), 0)
    return dict(states_in=states_in, potential=potential, projectors=projectors, proj_gains=proj_gains, atom_owner=atom_owner, atom_rows=atom_rows, wrap_rows=wrap_rows)


MIXED_WEIGHT = 0.7
CENTER = 12.0
HALF_WIDTH = 8.0


def second_table(radius):
    weights = [-2.0 * sum(1.0 / (k * k) for k in range(1, radius + 1))]
    for k in range(1, radius + 1):
        weights.append(2.0 * (-1) ** (k + 1) * math.factorial(radius) ** 2 / (k * k * math.factorial(radius - k) * math.factorial(radius + k)))
    return weights


def first_table(radius):
    weights = [0.0]
    for k in range(1, radius + 1):
        weights.append((-1) ** (k + 1) * math.factorial(radius) ** 2 / (k * math.factorial(radius - k) * math.factorial(radius + k)))
    return weights


def laplacian(padded, plane_count):
    second_weights = second_table(RADIUS)
    first_weights = first_table(RADIUS)
    interior = padded[:, RADIUS:RADIUS + plane_count]
    line_depth = interior.shape[3]
    z_padded = jnp.pad(interior, ((0, 0), (0, 0), (0, 0), (RADIUS, RADIUS)))
    summed = 3.0 * second_weights[0] * interior
    y_slope = jnp.zeros_like(padded)
    for k in range(1, RADIUS + 1):
        summed = summed + second_weights[k] * (padded[:, RADIUS + k:RADIUS + k + plane_count] + padded[:, RADIUS - k:RADIUS - k + plane_count])
        summed = summed + second_weights[k] * (jnp.roll(interior, -k, 2) + jnp.roll(interior, k, 2))
        summed = summed + second_weights[k] * (z_padded[:, :, :, RADIUS + k:RADIUS + k + line_depth] + z_padded[:, :, :, RADIUS - k:RADIUS - k + line_depth])
        y_slope = y_slope + first_weights[k] * (jnp.roll(padded, -k, 2) - jnp.roll(padded, k, 2))
    cross_term = jnp.zeros_like(interior)
    for k in range(1, RADIUS + 1):
        cross_term = cross_term + first_weights[k] * (y_slope[:, RADIUS + k:RADIUS + k + plane_count] - y_slope[:, RADIUS - k:RADIUS - k + plane_count])
    return summed + MIXED_WEIGHT * cross_term


def extend(grid_field, wrap_rows, unwrap_rows):
    low_rim = jnp.take(grid_field[:, NX - RADIUS:], wrap_rows, axis=2)
    high_rim = jnp.take(grid_field[:, :RADIUS], unwrap_rows, axis=2)
    return jnp.concatenate([low_rim, grid_field, high_rim], axis=1)


def atom_tables(projectors, proj_gains, atom_owner, atom_rows):
    owners = atom_owner.reshape(OWNERS, HOME_ATOMS)
    row_order = jnp.arange(HOME_ATOMS, dtype=jnp.int32)
    same_owner = (owners[:, :, None] == owners[:, None, :]) & (row_order[None, None, :] < row_order[None, :, None])
    owner_rank = jnp.sum(same_owner.astype(jnp.int32), axis=2)
    home_index = jnp.arange(OWNERS, dtype=jnp.int32)[:, None]
    slot_index = (owners * SLOTS + home_index * PAIR_CAP + owner_rank).reshape(-1).astype(jnp.int32)
    atom_proj = jnp.take(projectors.reshape(OWNERS * SLOTS, NPROJ, BLK * NZ), slot_index, axis=0)
    atom_gain = jnp.take(proj_gains.reshape(OWNERS * SLOTS, NPROJ), slot_index, axis=0)
    safe_rows = jnp.where(atom_rows >= 0, atom_rows, NX * NY).astype(jnp.int32)
    return atom_proj, atom_gain, safe_rows


def nonlocal_term(grid_field, atom_proj, atom_gain, safe_rows):
    state_count = grid_field.shape[0]
    tile_lines = grid_field.reshape(state_count, NX * NY, NZ)
    picked = jnp.take(tile_lines, safe_rows, axis=1, mode="fill", fill_value=0.0).astype(jnp.bfloat16)
    picked = picked.reshape(state_count, ATOMS, BLK * NZ)
    coefficients = jnp.einsum("ajc,sac->saj", atom_proj.astype(jnp.float32), picked.astype(jnp.float32))
    scaled = (coefficients * atom_gain.astype(jnp.float32)[None]).astype(jnp.bfloat16)
    projected = jnp.einsum("ajc,saj->sac", atom_proj.astype(jnp.float32), scaled.astype(jnp.float32)).astype(jnp.bfloat16)
    pieces = projected.reshape(state_count, ATOMS, BLK, NZ).astype(jnp.float32)
    summed = jnp.zeros((state_count, NX * NY, NZ), jnp.float32).at[:, safe_rows].add(pieces, mode="drop")
    return summed.reshape(state_count, NX, NY, NZ)


def reference(states_in, potential, projectors, proj_gains, atom_owner, atom_rows, wrap_rows):
    row_order = jnp.arange(NY, dtype=jnp.int32)
    unwrap_rows = jnp.sum(row_order[None, :] * (wrap_rows[None, :] == row_order[:, None]).astype(jnp.int32), axis=1).astype(jnp.int32)
    atom_proj, atom_gain, safe_rows = atom_tables(projectors, proj_gains, atom_owner, atom_rows)

    def operate(grid_field):
        padded = extend(grid_field, wrap_rows, unwrap_rows)
        return -0.5 * laplacian(padded, NX) + potential[None] * grid_field + nonlocal_term(grid_field, atom_proj, atom_gain, safe_rows)

    def shifted(grid_field):
        return (operate(grid_field) - CENTER * grid_field) / HALF_WIDTH

    def filter_group(state_group):
        first_term = shifted(state_group)
        second_term = 2.0 * shifted(first_term) - state_group
        return 2.0 * shifted(second_term) - first_term

    groups = states_in.reshape(N_STATES, STATES_DEV, NX, NY, NZ)
    return lax.map(filter_group, groups).reshape(NSTATES, NX, NY, NZ)
```

```python
import math

import jax
import jax.numpy as jnp
from jax import lax
from jax.sharding import PartitionSpec as P

RADIUS = 6
PAIR_CAP = 2


MIXED_WEIGHT = 0.7
CENTER = 12.0
HALF_WIDTH = 8.0


def padded_2(shard, sides, width):
    for axis, dim in sides:
        count, length = (lax.axis_size(axis), shard.shape[dim])
        up = [(i, (i + 1) % count) for i in range(count)]
        down = [(j, i) for i, j in up]
        last = lax.slice_in_dim(shard, length - width, length, axis=dim)
        initial = lax.slice_in_dim(shard, 0, width, axis=dim)
        before = lax.ppermute(last, axis, up)
        after = lax.ppermute(initial, axis, down)
        shard = jnp.concatenate([before, shard, after], axis=dim)
    return shard


def second_table(radius):
    weights = [-2.0 * sum((1.0 / (k * k) for k in range(1, radius + 1)))]
    for k in range(1, radius + 1):
        weights.append(
            2.0
            * (-1) ** (k + 1)
            * math.factorial(radius) ** 2
            / (k * k * math.factorial(radius - k) * math.factorial(radius + k))
        )
    return weights


def first_table(radius):
    weights = [0.0]
    for k in range(1, radius + 1):
        weights.append(
            (-1) ** (k + 1)
            * math.factorial(radius) ** 2
            / (k * math.factorial(radius - k) * math.factorial(radius + k))
        )
    return weights


def laplacian(padded, plane_count):
    second_weights = second_table(RADIUS)
    first_weights = first_table(RADIUS)
    interior = padded[:, RADIUS : RADIUS + plane_count]
    line_depth = interior.shape[3]
    z_padded = jnp.pad(interior, ((0, 0), (0, 0), (0, 0), (RADIUS, RADIUS)))
    summed = 3.0 * second_weights[0] * interior
    y_slope = jnp.zeros_like(padded)
    for k in range(1, RADIUS + 1):
        summed = summed + second_weights[k] * (
            padded[:, RADIUS + k : RADIUS + k + plane_count]
            + padded[:, RADIUS - k : RADIUS - k + plane_count]
        )
        summed = summed + second_weights[k] * (jnp.roll(interior, -k, 2) + jnp.roll(interior, k, 2))
        summed = summed + second_weights[k] * (
            z_padded[:, :, :, RADIUS + k : RADIUS + k + line_depth]
            + z_padded[:, :, :, RADIUS - k : RADIUS - k + line_depth]
        )
        y_slope = y_slope + first_weights[k] * (jnp.roll(padded, -k, 2) - jnp.roll(padded, k, 2))
    cross_term = jnp.zeros_like(interior)
    for k in range(1, RADIUS + 1):
        cross_term = cross_term + first_weights[k] * (
            y_slope[:, RADIUS + k : RADIUS + k + plane_count]
            - y_slope[:, RADIUS - k : RADIUS - k + plane_count]
        )
    return summed + MIXED_WEIGHT * cross_term


def shards(states_in, potential, projectors, proj_gains, atom_owner, atom_rows, wrap_rows):
    state_count, tile_width, breadth, line_depth = states_in.shape
    n_grid = lax.axis_size("grid")
    n_states = lax.axis_size("states")
    tile_index = lax.axis_index("grid")
    tile_lines = tile_width * breadth
    block_rows = atom_rows.shape[1]
    line_span = block_rows * line_depth
    proj_count = projectors.shape[2]
    home_count = atom_owner.shape[0]
    slot_pairs = projectors.shape[1]
    row_order = jnp.arange(breadth, dtype=jnp.int32)
    unwrap_rows = jnp.sum(
        row_order[None, :] * (wrap_rows[None, :] == row_order[:, None]).astype(jnp.int32), axis=1
    )
    atom_order = jnp.arange(home_count, dtype=jnp.int32)
    same_owner = (atom_owner[:, None] == atom_owner[None, :]) & (
        atom_order[None, :] < atom_order[:, None]
    )
    owner_rank = jnp.sum(same_owner.astype(jnp.int32), axis=1)
    atom_slot = atom_owner * PAIR_CAP + owner_rank
    local_rows = jnp.where(atom_rows >= 0, atom_rows - tile_index * tile_lines, tile_lines)

    gain_lanes = jnp.zeros((1, slot_pairs, proj_count, 128), jnp.bfloat16)
    gain_lanes = gain_lanes.at[..., 0].set(proj_gains)
    packed = jnp.concatenate([projectors, gain_lanes], axis=3)
    pairs = [(o * n_states + t, t * n_states + o) for o in range(n_grid) for t in range(n_states)]
    packed = lax.ppermute(packed, ("grid", "states"), pairs)
    gathered = lax.all_gather(packed[0], "states", axis=0, tiled=True)
    gathered = gathered.reshape(n_states * slot_pairs, proj_count, line_span + 128)
    atom_pack = jnp.take(gathered, atom_slot, axis=0)
    atom_proj = atom_pack[:, :, :line_span]
    atom_gain = atom_pack[:, :, line_span].astype(jnp.float32)

    def extended(grid_field):
        padded = padded_2(grid_field, (("grid", 1),), RADIUS)
        low_rim = padded[:, :RADIUS]
        high_rim = padded[:, RADIUS + tile_width :]
        low_rim = jnp.where(tile_index == 0, jnp.take(low_rim, wrap_rows, axis=2), low_rim)
        high_rim = jnp.where(
            tile_index == n_grid - 1, jnp.take(high_rim, unwrap_rows, axis=2), high_rim
        )
        return jnp.concatenate([low_rim, padded[:, RADIUS : RADIUS + tile_width], high_rim], axis=1)

    def nonlocal_part(grid_field):
        lines_here = grid_field.reshape(state_count, tile_lines, line_depth)
        picked = jnp.take(lines_here, local_rows, axis=1, mode="fill", fill_value=0.0).astype(
            jnp.bfloat16
        )
        picked = picked.reshape(state_count, home_count, line_span)
        coefficients = jnp.einsum(
            "ajc,sac->saj", atom_proj, picked, preferred_element_type=jnp.float32
        )
        scaled = (coefficients * atom_gain[None]).astype(jnp.bfloat16)
        projected = jnp.einsum(
            "ajc,saj->sac", atom_proj, scaled, preferred_element_type=jnp.float32
        ).astype(jnp.bfloat16)
        pieces = projected.reshape(state_count, home_count, block_rows, line_depth).astype(
            jnp.float32
        )
        summed = (
            jnp.zeros((state_count, tile_lines, line_depth), jnp.float32)
            .at[:, local_rows]
            .add(pieces, mode="drop")
        )
        return summed.reshape(state_count, tile_width, breadth, line_depth)

    def operate(grid_field):
        padded = extended(grid_field)
        return (
            -0.5 * laplacian(padded, tile_width)
            + potential[None] * grid_field
            + nonlocal_part(grid_field)
        )

    def shifted(grid_field):
        return (operate(grid_field) - CENTER * grid_field) / HALF_WIDTH

    first_term = shifted(states_in)
    second_term = 2.0 * shifted(first_term) - states_in
    return 2.0 * shifted(second_term) - first_term


def solution(mesh):
    in_specs = (
        P("states", "grid", None, None),
        P("grid", None, None),
        P("grid", "states", None, None),
        P("grid", "states", None),
        P("grid"),
        P("grid", None),
        P(),
    )
    out_specs = P("states", "grid", None, None)
    return jax.shard_map(shards, mesh=mesh, in_specs=in_specs, out_specs=out_specs, check_vma=False)
```

```python
import math

import jax
import jax.numpy as jnp
from jax import lax
from jax.sharding import PartitionSpec as P

RADIUS = 6
PAIR_CAP = 2


MIXED_WEIGHT = 0.7
CENTER = 12.0
HALF_WIDTH = 8.0


def padded_2(shard, sides, width):
    for axis, dim in sides:
        count, length = (lax.axis_size(axis), shard.shape[dim])
        up = [(i, (i + 1) % count) for i in range(count)]
        down = [(j, i) for i, j in up]
        last = lax.slice_in_dim(shard, length - width, length, axis=dim)
        initial = lax.slice_in_dim(shard, 0, width, axis=dim)
        before = lax.ppermute(last, axis, up)
        after = lax.ppermute(initial, axis, down)
        shard = jnp.concatenate([before, shard, after], axis=dim)
    return shard


def second_table(radius):
    weights = [-2.0 * sum((1.0 / (k * k) for k in range(1, radius + 1)))]
    for k in range(1, radius + 1):
        weights.append(
            2.0
            * (-1) ** (k + 1)
            * math.factorial(radius) ** 2
            / (k * k * math.factorial(radius - k) * math.factorial(radius + k))
        )
    return weights


def first_table(radius):
    weights = [0.0]
    for k in range(1, radius + 1):
        weights.append(
            (-1) ** (k + 1)
            * math.factorial(radius) ** 2
            / (k * math.factorial(radius - k) * math.factorial(radius + k))
        )
    return weights


def laplacian(padded, plane_count):
    second_weights = second_table(RADIUS)
    first_weights = first_table(RADIUS)
    interior = padded[:, RADIUS : RADIUS + plane_count]
    line_depth = interior.shape[3]
    z_padded = jnp.pad(interior, ((0, 0), (0, 0), (0, 0), (RADIUS, RADIUS)))
    summed = 3.0 * second_weights[0] * interior
    y_slope = jnp.zeros_like(padded)
    for k in range(1, RADIUS + 1):
        summed = summed + second_weights[k] * (
            padded[:, RADIUS + k : RADIUS + k + plane_count]
            + padded[:, RADIUS - k : RADIUS - k + plane_count]
        )
        summed = summed + second_weights[k] * (jnp.roll(interior, -k, 2) + jnp.roll(interior, k, 2))
        summed = summed + second_weights[k] * (
            z_padded[:, :, :, RADIUS + k : RADIUS + k + line_depth]
            + z_padded[:, :, :, RADIUS - k : RADIUS - k + line_depth]
        )
        y_slope = y_slope + first_weights[k] * (jnp.roll(padded, -k, 2) - jnp.roll(padded, k, 2))
    cross_term = jnp.zeros_like(interior)
    for k in range(1, RADIUS + 1):
        cross_term = cross_term + first_weights[k] * (
            y_slope[:, RADIUS + k : RADIUS + k + plane_count]
            - y_slope[:, RADIUS - k : RADIUS - k + plane_count]
        )
    return summed + MIXED_WEIGHT * cross_term


def shards(states_in, potential, projectors, proj_gains, atom_owner, atom_rows, wrap_rows):
    state_count, tile_width, breadth, line_depth = states_in.shape
    n_grid = lax.axis_size("grid")
    n_states = lax.axis_size("states")
    tile_index = lax.axis_index("grid")
    tile_lines = tile_width * breadth
    block_rows = atom_rows.shape[1]
    line_span = block_rows * line_depth
    proj_count = projectors.shape[2]
    home_count = atom_owner.shape[0]
    slot_pairs = projectors.shape[1]
    row_order = jnp.arange(breadth, dtype=jnp.int32)
    unwrap_rows = jnp.sum(
        row_order[None, :] * (wrap_rows[None, :] == row_order[:, None]).astype(jnp.int32), axis=1
    )
    atom_order = jnp.arange(home_count, dtype=jnp.int32)
    same_owner = (atom_owner[:, None] == atom_owner[None, :]) & (
        atom_order[None, :] < atom_order[:, None]
    )
    owner_rank = jnp.sum(same_owner.astype(jnp.int32), axis=1)
    atom_slot = atom_owner * PAIR_CAP + owner_rank
    local_rows = jnp.where(atom_rows >= 0, atom_rows - tile_index * tile_lines, tile_lines)

    gain_lanes = jnp.zeros((1, slot_pairs, proj_count, 128), jnp.bfloat16)
    gain_lanes = gain_lanes.at[..., 0].set(proj_gains)
    packed = jnp.concatenate([projectors, gain_lanes], axis=3)
    pairs = [(o * n_states + t, t * n_states + o) for o in range(n_grid) for t in range(n_states)]
    packed = lax.ppermute(packed, ("grid", "states"), pairs)
    gathered = lax.all_gather(packed[0], "states", axis=0, tiled=True)
    gathered = gathered.reshape(n_states * slot_pairs, proj_count, line_span + 128)
    atom_pack = jnp.take(gathered, atom_slot, axis=0)
    proj_rows = atom_pack[:, :, :line_span].reshape(home_count * proj_count, line_span)
    atom_gain = atom_pack[:, :, line_span].astype(jnp.float32)
    selector = (
        local_rows.reshape(-1)[:, None] == jnp.arange(tile_lines, dtype=jnp.int32)[None, :]
    ).astype(jnp.bfloat16)
    atom_eye = jnp.eye(home_count, dtype=jnp.float32)

    def extended(grid_field):
        padded = padded_2(grid_field, (("grid", 1),), RADIUS)
        low_rim = padded[:, :RADIUS]
        high_rim = padded[:, RADIUS + tile_width :]
        low_rim = jnp.where(tile_index == 0, jnp.take(low_rim, wrap_rows, axis=2), low_rim)
        high_rim = jnp.where(
            tile_index == n_grid - 1, jnp.take(high_rim, unwrap_rows, axis=2), high_rim
        )
        return jnp.concatenate([low_rim, padded[:, RADIUS : RADIUS + tile_width], high_rim], axis=1)

    def nonlocal_part(grid_field):
        lines_here = grid_field.reshape(tile_lines, line_depth).astype(jnp.bfloat16)
        picked = jnp.dot(selector, lines_here, preferred_element_type=jnp.float32)
        picked = picked.astype(jnp.bfloat16).reshape(home_count, line_span)
        every_pair = lax.dot_general(
            proj_rows, picked, (((1,), (1,)), ((), ())), preferred_element_type=jnp.float32
        ).reshape(home_count, proj_count, home_count)
        coefficients = jnp.sum(every_pair * atom_eye[:, None, :], axis=2)
        scaled = (coefficients * atom_gain).astype(jnp.bfloat16)
        block_scaled = (atom_eye.astype(jnp.bfloat16)[:, :, None] * scaled[None, :, :]).reshape(
            home_count, home_count * proj_count
        )
        projected = jnp.dot(block_scaled, proj_rows, preferred_element_type=jnp.float32)
        projected = projected.astype(jnp.bfloat16).reshape(home_count * block_rows, line_depth)
        summed = lax.dot_general(
            selector, projected, (((0,), (0,)), ((), ())), preferred_element_type=jnp.float32
        )
        return summed.reshape(state_count, tile_width, breadth, line_depth)

    def operate(grid_field):
        padded = extended(grid_field)
        return (
            -0.5 * laplacian(padded, tile_width)
            + potential[None] * grid_field
            + nonlocal_part(grid_field)
        )

    def shifted(grid_field):
        return (operate(grid_field) - CENTER * grid_field) / HALF_WIDTH

    first_term = shifted(states_in)
    second_term = 2.0 * shifted(first_term) - states_in
    return 2.0 * shifted(second_term) - first_term


def solution(mesh):
    in_specs = (
        P("states", "grid", None, None),
        P("grid", None, None),
        P("grid", "states", None, None),
        P("grid", "states", None),
        P("grid"),
        P("grid", None),
        P(),
    )
    out_specs = P("states", "grid", None, None)
    return jax.shard_map(shards, mesh=mesh, in_specs=in_specs, out_specs=out_specs, check_vma=False)
```

```python
import math

import jax
import jax.numpy as jnp
from jax import lax
from jax.sharding import PartitionSpec as P

RADIUS = 6
PAIR_CAP = 2


MIXED_WEIGHT = 0.7
CENTER = 12.0
HALF_WIDTH = 8.0


def padded_2(shard, sides, width):
    for axis, dim in sides:
        count, length = (lax.axis_size(axis), shard.shape[dim])
        up = [(i, (i + 1) % count) for i in range(count)]
        down = [(j, i) for i, j in up]
        last = lax.slice_in_dim(shard, length - width, length, axis=dim)
        initial = lax.slice_in_dim(shard, 0, width, axis=dim)
        before = lax.ppermute(last, axis, up)
        after = lax.ppermute(initial, axis, down)
        shard = jnp.concatenate([before, shard, after], axis=dim)
    return shard


def second_table(radius):
    weights = [-2.0 * sum((1.0 / (k * k) for k in range(1, radius + 1)))]
    for k in range(1, radius + 1):
        weights.append(
            2.0
            * (-1) ** (k + 1)
            * math.factorial(radius) ** 2
            / (k * k * math.factorial(radius - k) * math.factorial(radius + k))
        )
    return weights


def first_table(radius):
    weights = [0.0]
    for k in range(1, radius + 1):
        weights.append(
            (-1) ** (k + 1)
            * math.factorial(radius) ** 2
            / (k * math.factorial(radius - k) * math.factorial(radius + k))
        )
    return weights


def laplacian(padded, plane_count):
    second_weights = second_table(RADIUS)
    first_weights = first_table(RADIUS)
    interior = padded[:, RADIUS : RADIUS + plane_count]
    line_depth = interior.shape[3]
    z_padded = jnp.pad(interior, ((0, 0), (0, 0), (0, 0), (RADIUS, RADIUS)))
    summed = 3.0 * second_weights[0] * interior
    y_slope = jnp.zeros_like(padded)
    for k in range(1, RADIUS + 1):
        summed = summed + second_weights[k] * (
            padded[:, RADIUS + k : RADIUS + k + plane_count]
            + padded[:, RADIUS - k : RADIUS - k + plane_count]
        )
        summed = summed + second_weights[k] * (jnp.roll(interior, -k, 2) + jnp.roll(interior, k, 2))
        summed = summed + second_weights[k] * (
            z_padded[:, :, :, RADIUS + k : RADIUS + k + line_depth]
            + z_padded[:, :, :, RADIUS - k : RADIUS - k + line_depth]
        )
        y_slope = y_slope + first_weights[k] * (jnp.roll(padded, -k, 2) - jnp.roll(padded, k, 2))
    cross_term = jnp.zeros_like(interior)
    for k in range(1, RADIUS + 1):
        cross_term = cross_term + first_weights[k] * (
            y_slope[:, RADIUS + k : RADIUS + k + plane_count]
            - y_slope[:, RADIUS - k : RADIUS - k + plane_count]
        )
    return summed + MIXED_WEIGHT * cross_term


def shards(states_in, potential, projectors, proj_gains, atom_owner, atom_rows, wrap_rows):
    state_count, tile_width, breadth, line_depth = states_in.shape
    n_grid = lax.axis_size("grid")
    n_states = lax.axis_size("states")
    tile_index = lax.axis_index("grid")
    tile_lines = tile_width * breadth
    block_rows = atom_rows.shape[1]
    line_span = block_rows * line_depth
    proj_count = projectors.shape[2]
    home_count = atom_owner.shape[0]
    slot_pairs = projectors.shape[1]
    row_order = jnp.arange(breadth, dtype=jnp.int32)
    unwrap_rows = jnp.sum(
        row_order[None, :] * (wrap_rows[None, :] == row_order[:, None]).astype(jnp.int32), axis=1
    )
    atom_order = jnp.arange(home_count, dtype=jnp.int32)
    same_owner = (atom_owner[:, None] == atom_owner[None, :]) & (
        atom_order[None, :] < atom_order[:, None]
    )
    owner_rank = jnp.sum(same_owner.astype(jnp.int32), axis=1)
    atom_slot = atom_owner * PAIR_CAP + owner_rank
    local_rows = jnp.where(atom_rows >= 0, atom_rows - tile_index * tile_lines, tile_lines)

    gain_lanes = jnp.zeros((1, slot_pairs, proj_count, 128), jnp.bfloat16)
    gain_lanes = gain_lanes.at[..., 0].set(proj_gains)
    packed = jnp.concatenate([projectors, gain_lanes], axis=3)
    pairs = [(o * n_states + t, t * n_states + o) for o in range(n_grid) for t in range(n_states)]
    packed = lax.ppermute(packed, ("grid", "states"), pairs)
    mine = atom_owner == lax.axis_index("states")
    atom_pack = jnp.where(
        mine[:, None, None], jnp.take(packed[0], owner_rank, axis=0), jnp.zeros((), jnp.bfloat16)
    )
    atom_pack = lax.psum(atom_pack, "states")
    proj_rows = atom_pack[:, :, :line_span].reshape(home_count * proj_count, line_span)
    atom_gain = atom_pack[:, :, line_span].astype(jnp.float32)
    selector = (
        local_rows.reshape(-1)[:, None] == jnp.arange(tile_lines, dtype=jnp.int32)[None, :]
    ).astype(jnp.bfloat16)
    atom_eye = jnp.eye(home_count, dtype=jnp.float32)

    def extended(grid_field):
        padded = padded_2(grid_field, (("grid", 1),), RADIUS)
        low_rim = padded[:, :RADIUS]
        high_rim = padded[:, RADIUS + tile_width :]
        low_rim = jnp.where(tile_index == 0, jnp.take(low_rim, wrap_rows, axis=2), low_rim)
        high_rim = jnp.where(
            tile_index == n_grid - 1, jnp.take(high_rim, unwrap_rows, axis=2), high_rim
        )
        return jnp.concatenate([low_rim, padded[:, RADIUS : RADIUS + tile_width], high_rim], axis=1)

    def nonlocal_part(grid_field):
        lines_here = grid_field.reshape(tile_lines, line_depth).astype(jnp.bfloat16)
        picked = jnp.dot(selector, lines_here, preferred_element_type=jnp.float32)
        picked = picked.astype(jnp.bfloat16).reshape(home_count, line_span)
        every_pair = lax.dot_general(
            proj_rows, picked, (((1,), (1,)), ((), ())), preferred_element_type=jnp.float32
        ).reshape(home_count, proj_count, home_count)
        coefficients = jnp.sum(every_pair * atom_eye[:, None, :], axis=2)
        scaled = (coefficients * atom_gain).astype(jnp.bfloat16)
        block_scaled = (atom_eye.astype(jnp.bfloat16)[:, :, None] * scaled[None, :, :]).reshape(
            home_count, home_count * proj_count
        )
        projected = jnp.dot(block_scaled, proj_rows, preferred_element_type=jnp.float32)
        projected = projected.astype(jnp.bfloat16).reshape(home_count * block_rows, line_depth)
        summed = lax.dot_general(
            selector, projected, (((0,), (0,)), ((), ())), preferred_element_type=jnp.float32
        )
        return summed.reshape(state_count, tile_width, breadth, line_depth)

    def operate(grid_field):
        padded = extended(grid_field)
        return (
            -0.5 * laplacian(padded, tile_width)
            + potential[None] * grid_field
            + nonlocal_part(grid_field)
        )

    def shifted(grid_field):
        return (operate(grid_field) - CENTER * grid_field) / HALF_WIDTH

    first_term = shifted(states_in)
    second_term = 2.0 * shifted(first_term) - states_in
    return 2.0 * shifted(second_term) - first_term


def solution(mesh):
    in_specs = (
        P("states", "grid", None, None),
        P("grid", None, None),
        P("grid", "states", None, None),
        P("grid", "states", None),
        P("grid"),
        P("grid", None),
        P(),
    )
    out_specs = P("states", "grid", None, None)
    return jax.shard_map(shards, mesh=mesh, in_specs=in_specs, out_specs=out_specs, check_vma=False)
```

```python
import math

import jax
import jax.numpy as jnp
from jax import lax
from jax.sharding import PartitionSpec as P

RADIUS = 6
PAIR_CAP = 2


MIXED_WEIGHT = 0.7
CENTER = 12.0
HALF_WIDTH = 8.0


def padded_2(shard, sides, width):
    for axis, dim in sides:
        count, length = (lax.axis_size(axis), shard.shape[dim])
        up = [(i, (i + 1) % count) for i in range(count)]
        down = [(j, i) for i, j in up]
        last = lax.slice_in_dim(shard, length - width, length, axis=dim)
        initial = lax.slice_in_dim(shard, 0, width, axis=dim)
        before = lax.ppermute(last, axis, up)
        after = lax.ppermute(initial, axis, down)
        shard = jnp.concatenate([before, shard, after], axis=dim)
    return shard


def second_table(radius):
    weights = [-2.0 * sum((1.0 / (k * k) for k in range(1, radius + 1)))]
    for k in range(1, radius + 1):
        weights.append(
            2.0
            * (-1) ** (k + 1)
            * math.factorial(radius) ** 2
            / (k * k * math.factorial(radius - k) * math.factorial(radius + k))
        )
    return weights


def first_table(radius):
    weights = [0.0]
    for k in range(1, radius + 1):
        weights.append(
            (-1) ** (k + 1)
            * math.factorial(radius) ** 2
            / (k * math.factorial(radius - k) * math.factorial(radius + k))
        )
    return weights


def laplacian(padded, plane_count):
    second_weights = second_table(RADIUS)
    first_weights = first_table(RADIUS)
    interior = padded[:, RADIUS : RADIUS + plane_count]
    line_depth = interior.shape[3]
    z_padded = jnp.pad(interior, ((0, 0), (0, 0), (0, 0), (RADIUS, RADIUS)))
    summed = 3.0 * second_weights[0] * interior
    y_slope = jnp.zeros_like(padded)
    for k in range(1, RADIUS + 1):
        summed = summed + second_weights[k] * (
            padded[:, RADIUS + k : RADIUS + k + plane_count]
            + padded[:, RADIUS - k : RADIUS - k + plane_count]
        )
        summed = summed + second_weights[k] * (jnp.roll(interior, -k, 2) + jnp.roll(interior, k, 2))
        summed = summed + second_weights[k] * (
            z_padded[:, :, :, RADIUS + k : RADIUS + k + line_depth]
            + z_padded[:, :, :, RADIUS - k : RADIUS - k + line_depth]
        )
        y_slope = y_slope + first_weights[k] * (jnp.roll(padded, -k, 2) - jnp.roll(padded, k, 2))
    cross_term = jnp.zeros_like(interior)
    for k in range(1, RADIUS + 1):
        cross_term = cross_term + first_weights[k] * (
            y_slope[:, RADIUS + k : RADIUS + k + plane_count]
            - y_slope[:, RADIUS - k : RADIUS - k + plane_count]
        )
    return summed + MIXED_WEIGHT * cross_term


def shards(states_in, potential, projectors, proj_gains, atom_owner, atom_rows, wrap_rows):
    state_count, tile_width, breadth, line_depth = states_in.shape
    n_grid = lax.axis_size("grid")
    n_states = lax.axis_size("states")
    tile_index = lax.axis_index("grid")
    tile_lines = tile_width * breadth
    block_rows = atom_rows.shape[1]
    line_span = block_rows * line_depth
    proj_count = projectors.shape[2]
    home_count = atom_owner.shape[0]
    slot_pairs = projectors.shape[1]
    row_order = jnp.arange(breadth, dtype=jnp.int32)
    unwrap_rows = jnp.sum(
        row_order[None, :] * (wrap_rows[None, :] == row_order[:, None]).astype(jnp.int32), axis=1
    )
    atom_order = jnp.arange(home_count, dtype=jnp.int32)
    same_owner = (atom_owner[:, None] == atom_owner[None, :]) & (
        atom_order[None, :] < atom_order[:, None]
    )
    owner_rank = jnp.sum(same_owner.astype(jnp.int32), axis=1)
    atom_slot = atom_owner * PAIR_CAP + owner_rank
    local_rows = jnp.where(atom_rows >= 0, atom_rows - tile_index * tile_lines, tile_lines)

    gain_lanes = jnp.zeros((1, slot_pairs, proj_count, 128), jnp.bfloat16)
    gain_lanes = gain_lanes.at[..., 0].set(proj_gains)
    packed = jnp.concatenate([projectors, gain_lanes], axis=3)
    pairs = [(o * n_states + t, t * n_states + o) for o in range(n_grid) for t in range(n_states)]
    packed = lax.ppermute(packed, ("grid", "states"), pairs)
    packed, states_held = lax.optimization_barrier((packed, states_in))
    gathered = lax.all_gather(packed[0], "states", axis=0, tiled=True)
    gathered = gathered.reshape(n_states * slot_pairs, proj_count, line_span + 128)
    atom_pack = jnp.take(gathered, atom_slot, axis=0)
    proj_rows = atom_pack[:, :, :line_span].reshape(home_count * proj_count, line_span)
    atom_gain = atom_pack[:, :, line_span].astype(jnp.float32)
    selector = (
        local_rows.reshape(-1)[:, None] == jnp.arange(tile_lines, dtype=jnp.int32)[None, :]
    ).astype(jnp.bfloat16)
    atom_eye = jnp.eye(home_count, dtype=jnp.float32)

    def extended(grid_field):
        padded = padded_2(grid_field, (("grid", 1),), RADIUS)
        low_rim = padded[:, :RADIUS]
        high_rim = padded[:, RADIUS + tile_width :]
        low_rim = jnp.where(tile_index == 0, jnp.take(low_rim, wrap_rows, axis=2), low_rim)
        high_rim = jnp.where(
            tile_index == n_grid - 1, jnp.take(high_rim, unwrap_rows, axis=2), high_rim
        )
        return jnp.concatenate([low_rim, padded[:, RADIUS : RADIUS + tile_width], high_rim], axis=1)

    def nonlocal_part(grid_field):
        lines_here = grid_field.reshape(tile_lines, line_depth).astype(jnp.bfloat16)
        picked = jnp.dot(selector, lines_here, preferred_element_type=jnp.float32)
        picked = picked.astype(jnp.bfloat16).reshape(home_count, line_span)
        every_pair = lax.dot_general(
            proj_rows, picked, (((1,), (1,)), ((), ())), preferred_element_type=jnp.float32
        ).reshape(home_count, proj_count, home_count)
        coefficients = jnp.sum(every_pair * atom_eye[:, None, :], axis=2)
        scaled = (coefficients * atom_gain).astype(jnp.bfloat16)
        block_scaled = (atom_eye.astype(jnp.bfloat16)[:, :, None] * scaled[None, :, :]).reshape(
            home_count, home_count * proj_count
        )
        projected = jnp.dot(block_scaled, proj_rows, preferred_element_type=jnp.float32)
        projected = projected.astype(jnp.bfloat16).reshape(home_count * block_rows, line_depth)
        summed = lax.dot_general(
            selector, projected, (((0,), (0,)), ((), ())), preferred_element_type=jnp.float32
        )
        return summed.reshape(state_count, tile_width, breadth, line_depth)

    def operate(grid_field, interior):
        padded = extended(grid_field)
        padded = jnp.concatenate(
            [padded[:, :RADIUS], interior, padded[:, RADIUS + tile_width :]], axis=1
        )
        return (
            -0.5 * laplacian(padded, tile_width)
            + potential[None] * interior
            + nonlocal_part(interior)
        )

    def shifted(grid_field, interior=None):
        interior = grid_field if interior is None else interior
        return (operate(grid_field, interior) - CENTER * interior) / HALF_WIDTH

    first_term = shifted(states_in, states_held)
    second_term = 2.0 * shifted(first_term) - states_in
    return 2.0 * shifted(second_term) - first_term


def solution(mesh):
    in_specs = (
        P("states", "grid", None, None),
        P("grid", None, None),
        P("grid", "states", None, None),
        P("grid", "states", None),
        P("grid"),
        P("grid", None),
        P(),
    )
    out_specs = P("states", "grid", None, None)
    return jax.shard_map(shards, mesh=mesh, in_specs=in_specs, out_specs=out_specs, check_vma=False)
```

```python
import math

import jax
import jax.numpy as jnp
from jax import lax
from jax.experimental import pallas as pl
from jax.experimental.pallas import tpu as pltpu
from jax.sharding import PartitionSpec as P

RADIUS = 6
PAIR_CAP = 2


MIXED_WEIGHT = 0.7
CENTER = 12.0
HALF_WIDTH = 8.0


def padded_2(shard, sides, width):
    for axis, dim in sides:
        count, length = (lax.axis_size(axis), shard.shape[dim])
        up = [(i, (i + 1) % count) for i in range(count)]
        down = [(j, i) for i, j in up]
        last = lax.slice_in_dim(shard, length - width, length, axis=dim)
        initial = lax.slice_in_dim(shard, 0, width, axis=dim)
        before = lax.ppermute(last, axis, up)
        after = lax.ppermute(initial, axis, down)
        shard = jnp.concatenate([before, shard, after], axis=dim)
    return shard


def second_table(radius):
    weights = [-2.0 * sum((1.0 / (k * k) for k in range(1, radius + 1)))]
    for k in range(1, radius + 1):
        weights.append(
            2.0
            * (-1) ** (k + 1)
            * math.factorial(radius) ** 2
            / (k * k * math.factorial(radius - k) * math.factorial(radius + k))
        )
    return weights


def first_table(radius):
    weights = [0.0]
    for k in range(1, radius + 1):
        weights.append(
            (-1) ** (k + 1)
            * math.factorial(radius) ** 2
            / (k * math.factorial(radius - k) * math.factorial(radius + k))
        )
    return weights


def laplacian(padded, plane_count):
    second_weights = second_table(RADIUS)
    first_weights = first_table(RADIUS)
    interior = padded[:, RADIUS : RADIUS + plane_count]
    line_depth = interior.shape[3]
    z_padded = jnp.pad(interior, ((0, 0), (0, 0), (0, 0), (RADIUS, RADIUS)))
    summed = 3.0 * second_weights[0] * interior
    y_slope = jnp.zeros_like(padded)
    for k in range(1, RADIUS + 1):
        summed = summed + second_weights[k] * (
            padded[:, RADIUS + k : RADIUS + k + plane_count]
            + padded[:, RADIUS - k : RADIUS - k + plane_count]
        )
        summed = summed + second_weights[k] * (jnp.roll(interior, -k, 2) + jnp.roll(interior, k, 2))
        summed = summed + second_weights[k] * (
            z_padded[:, :, :, RADIUS + k : RADIUS + k + line_depth]
            + z_padded[:, :, :, RADIUS - k : RADIUS - k + line_depth]
        )
        y_slope = y_slope + first_weights[k] * (jnp.roll(padded, -k, 2) - jnp.roll(padded, k, 2))
    cross_term = jnp.zeros_like(interior)
    for k in range(1, RADIUS + 1):
        cross_term = cross_term + first_weights[k] * (
            y_slope[:, RADIUS + k : RADIUS + k + plane_count]
            - y_slope[:, RADIUS - k : RADIUS - k + plane_count]
        )
    return summed + MIXED_WEIGHT * cross_term


def make_kernel(scale, with_prev):
    sw = second_table(RADIUS); fw = first_table(RADIUS)
    def kernel(lo_ref, v_ref, hi_ref, pot_ref, nl_ref, *rest):
        if with_prev:
            prev_ref, out_ref, pad_ref = rest
        else:
            out_ref, pad_ref = rest
        planes, breadth, depth = v_ref.shape
        v = v_ref[...]
        pad_ref[0:RADIUS] = lo_ref[...]
        pad_ref[RADIUS:RADIUS + planes] = v
        pad_ref[RADIUS + planes:] = hi_ref[...]
        lane = jax.lax.broadcasted_iota(jnp.int32, v.shape, 2)
        summed = (3.0 * sw[0]) * v
        for k in range(1, RADIUS + 1):
            xs = pad_ref[RADIUS + k:RADIUS + k + planes] + pad_ref[RADIUS - k:RADIUS - k + planes]
            ys = pltpu.roll(v, breadth - k, 1) + pltpu.roll(v, k, 1)
            zs = (jnp.where(lane < depth - k, pltpu.roll(v, depth - k, 2), 0.0)
                  + jnp.where(lane >= k, pltpu.roll(v, k, 2), 0.0))
            summed = summed + sw[k] * xs + sw[k] * ys + sw[k] * zs
        padded = pad_ref[...]
        slope = fw[1] * (pltpu.roll(padded, breadth - 1, 1) - pltpu.roll(padded, 1, 1))
        for k in range(2, RADIUS + 1):
            slope = slope + fw[k] * (pltpu.roll(padded, breadth - k, 1) - pltpu.roll(padded, k, 1))
        cross = fw[1] * (slope[RADIUS + 1:RADIUS + 1 + planes] - slope[RADIUS - 1:RADIUS - 1 + planes])
        for k in range(2, RADIUS + 1):
            cross = cross + fw[k] * (slope[RADIUS + k:RADIUS + k + planes] - slope[RADIUS - k:RADIUS - k + planes])
        lap = summed + 0.7 * cross
        hv = -0.5 * lap + pot_ref[...] * v + nl_ref[...]
        kv = (hv - 12.0 * v) / 8.0
        if with_prev:
            out_ref[...] = scale * kv - prev_ref[...]
        else:
            out_ref[...] = kv
    return kernel

def apply_op(lo, v, hi, pot, nl, prev=None, scale=1.0):
    planes, breadth, depth = v.shape
    args = [lo, v, hi, pot, nl] + ([prev] if prev is not None else [])
    return pl.pallas_call(
        make_kernel(scale, prev is not None),
        out_shape=jax.ShapeDtypeStruct(v.shape, jnp.float32),
        scratch_shapes=[pltpu.VMEM((planes + 2 * RADIUS, breadth, depth), jnp.float32)],
    )(*args)

def shards(states_in, potential, projectors, proj_gains, atom_owner, atom_rows, wrap_rows):
    state_count, tile_width, breadth, line_depth = states_in.shape
    n_grid = lax.axis_size("grid")
    n_states = lax.axis_size("states")
    tile_index = lax.axis_index("grid")
    tile_lines = tile_width * breadth
    block_rows = atom_rows.shape[1]
    line_span = block_rows * line_depth
    proj_count = projectors.shape[2]
    home_count = atom_owner.shape[0]
    slot_pairs = projectors.shape[1]
    row_order = jnp.arange(breadth, dtype=jnp.int32)
    unwrap_rows = jnp.sum(
        row_order[None, :] * (wrap_rows[None, :] == row_order[:, None]).astype(jnp.int32), axis=1
    )
    atom_order = jnp.arange(home_count, dtype=jnp.int32)
    same_owner = (atom_owner[:, None] == atom_owner[None, :]) & (
        atom_order[None, :] < atom_order[:, None]
    )
    owner_rank = jnp.sum(same_owner.astype(jnp.int32), axis=1)
    atom_slot = atom_owner * PAIR_CAP + owner_rank
    local_rows = jnp.where(atom_rows >= 0, atom_rows - tile_index * tile_lines, tile_lines)

    gain_lanes = jnp.zeros((1, slot_pairs, proj_count, 128), jnp.bfloat16)
    gain_lanes = gain_lanes.at[..., 0].set(proj_gains)
    packed = jnp.concatenate([projectors, gain_lanes], axis=3)
    pairs = [(o * n_states + t, t * n_states + o) for o in range(n_grid) for t in range(n_states)]
    packed = lax.ppermute(packed, ("grid", "states"), pairs)
    gathered = lax.all_gather(packed[0], "states", axis=0, tiled=True)
    gathered = gathered.reshape(n_states * slot_pairs, proj_count, line_span + 128)
    atom_pack = jnp.take(gathered, atom_slot, axis=0)
    proj_rows = atom_pack[:, :, :line_span].reshape(home_count * proj_count, line_span)
    atom_gain = atom_pack[:, :, line_span].astype(jnp.float32)
    selector = (
        local_rows.reshape(-1)[:, None] == jnp.arange(tile_lines, dtype=jnp.int32)[None, :]
    ).astype(jnp.bfloat16)
    atom_eye = jnp.eye(home_count, dtype=jnp.float32)

    def rims(grid_field):
        padded = padded_2(grid_field, (("grid", 1),), RADIUS)
        low_rim = padded[:, :RADIUS]
        high_rim = padded[:, RADIUS + tile_width :]
        low_rim = jnp.where(tile_index == 0, jnp.take(low_rim, wrap_rows, axis=2), low_rim)
        high_rim = jnp.where(
            tile_index == n_grid - 1, jnp.take(high_rim, unwrap_rows, axis=2), high_rim
        )
        return low_rim[0], high_rim[0]

    def nonlocal_part(grid_field):
        lines_here = grid_field.reshape(tile_lines, line_depth).astype(jnp.bfloat16)
        picked = jnp.dot(selector, lines_here, preferred_element_type=jnp.float32)
        picked = picked.astype(jnp.bfloat16).reshape(home_count, line_span)
        every_pair = lax.dot_general(
            proj_rows, picked, (((1,), (1,)), ((), ())), preferred_element_type=jnp.float32
        ).reshape(home_count, proj_count, home_count)
        coefficients = jnp.sum(every_pair * atom_eye[:, None, :], axis=2)
        scaled = (coefficients * atom_gain).astype(jnp.bfloat16)
        block_scaled = (atom_eye.astype(jnp.bfloat16)[:, :, None] * scaled[None, :, :]).reshape(
            home_count, home_count * proj_count
        )
        projected = jnp.dot(block_scaled, proj_rows, preferred_element_type=jnp.float32)
        projected = projected.astype(jnp.bfloat16).reshape(home_count * block_rows, line_depth)
        summed = lax.dot_general(
            selector, projected, (((0,), (0,)), ((), ())), preferred_element_type=jnp.float32
        )
        return summed.reshape(state_count, tile_width, breadth, line_depth)

    def step(grid_field, prev=None, scale=1.0):
        low_rim, high_rim = rims(grid_field)
        nonlocal_lines = nonlocal_part(grid_field)[0]
        out = apply_op(
            low_rim, grid_field[0], high_rim, potential, nonlocal_lines, prev, scale
        )
        return out[None]

    first_term = step(states_in)
    second_term = step(first_term, states_in[0], 2.0)
    return step(second_term, first_term[0], 2.0)


def solution(mesh):
    in_specs = (
        P("states", "grid", None, None),
        P("grid", None, None),
        P("grid", "states", None, None),
        P("grid", "states", None),
        P("grid"),
        P("grid", None),
        P(),
    )
    out_specs = P("states", "grid", None, None)
    return jax.shard_map(shards, mesh=mesh, in_specs=in_specs, out_specs=out_specs, check_vma=False)
```

```python
import math

import jax
import jax.numpy as jnp
from jax import lax
from jax.experimental import pallas as pl
from jax.experimental.pallas import tpu as pltpu
from jax.sharding import PartitionSpec as P

RADIUS = 6
PAIR_CAP = 2


MIXED_WEIGHT = 0.7
CENTER = 12.0
HALF_WIDTH = 8.0


def padded_2(shard, sides, width):
    for axis, dim in sides:
        count, length = (lax.axis_size(axis), shard.shape[dim])
        up = [(i, (i + 1) % count) for i in range(count)]
        down = [(j, i) for i, j in up]
        last = lax.slice_in_dim(shard, length - width, length, axis=dim)
        initial = lax.slice_in_dim(shard, 0, width, axis=dim)
        before = lax.ppermute(last, axis, up)
        after = lax.ppermute(initial, axis, down)
        shard = jnp.concatenate([before, shard, after], axis=dim)
    return shard


def second_table(radius):
    weights = [-2.0 * sum((1.0 / (k * k) for k in range(1, radius + 1)))]
    for k in range(1, radius + 1):
        weights.append(
            2.0
            * (-1) ** (k + 1)
            * math.factorial(radius) ** 2
            / (k * k * math.factorial(radius - k) * math.factorial(radius + k))
        )
    return weights


def first_table(radius):
    weights = [0.0]
    for k in range(1, radius + 1):
        weights.append(
            (-1) ** (k + 1)
            * math.factorial(radius) ** 2
            / (k * math.factorial(radius - k) * math.factorial(radius + k))
        )
    return weights


def laplacian(padded, plane_count):
    second_weights = second_table(RADIUS)
    first_weights = first_table(RADIUS)
    interior = padded[:, RADIUS : RADIUS + plane_count]
    line_depth = interior.shape[3]
    z_padded = jnp.pad(interior, ((0, 0), (0, 0), (0, 0), (RADIUS, RADIUS)))
    summed = 3.0 * second_weights[0] * interior
    y_slope = jnp.zeros_like(padded)
    for k in range(1, RADIUS + 1):
        summed = summed + second_weights[k] * (
            padded[:, RADIUS + k : RADIUS + k + plane_count]
            + padded[:, RADIUS - k : RADIUS - k + plane_count]
        )
        summed = summed + second_weights[k] * (jnp.roll(interior, -k, 2) + jnp.roll(interior, k, 2))
        summed = summed + second_weights[k] * (
            z_padded[:, :, :, RADIUS + k : RADIUS + k + line_depth]
            + z_padded[:, :, :, RADIUS - k : RADIUS - k + line_depth]
        )
        y_slope = y_slope + first_weights[k] * (jnp.roll(padded, -k, 2) - jnp.roll(padded, k, 2))
    cross_term = jnp.zeros_like(interior)
    for k in range(1, RADIUS + 1):
        cross_term = cross_term + first_weights[k] * (
            y_slope[:, RADIUS + k : RADIUS + k + plane_count]
            - y_slope[:, RADIUS - k : RADIUS - k + plane_count]
        )
    return summed + MIXED_WEIGHT * cross_term


def make_kernel(scale, with_prev):
    sw = second_table(RADIUS); fw = first_table(RADIUS)
    def kernel(lo_ref, v_ref, hi_ref, pot_ref, nl_ref, *rest):
        if with_prev:
            prev_ref, out_ref, pad_ref = rest
        else:
            out_ref, pad_ref = rest
        planes, breadth, depth = v_ref.shape
        v = v_ref[...]
        pad_ref[0:RADIUS] = lo_ref[...]
        pad_ref[RADIUS:RADIUS + planes] = v
        pad_ref[RADIUS + planes:] = hi_ref[...]
        lane = jax.lax.broadcasted_iota(jnp.int32, v.shape, 2)
        summed = (3.0 * sw[0]) * v
        for k in range(1, RADIUS + 1):
            xs = pad_ref[RADIUS + k:RADIUS + k + planes] + pad_ref[RADIUS - k:RADIUS - k + planes]
            ys = pltpu.roll(v, breadth - k, 1) + pltpu.roll(v, k, 1)
            zs = (jnp.where(lane < depth - k, pltpu.roll(v, depth - k, 2), 0.0)
                  + jnp.where(lane >= k, pltpu.roll(v, k, 2), 0.0))
            summed = summed + sw[k] * xs + sw[k] * ys + sw[k] * zs
        padded = pad_ref[...]
        slope = fw[1] * (pltpu.roll(padded, breadth - 1, 1) - pltpu.roll(padded, 1, 1))
        for k in range(2, RADIUS + 1):
            slope = slope + fw[k] * (pltpu.roll(padded, breadth - k, 1) - pltpu.roll(padded, k, 1))
        cross = fw[1] * (slope[RADIUS + 1:RADIUS + 1 + planes] - slope[RADIUS - 1:RADIUS - 1 + planes])
        for k in range(2, RADIUS + 1):
            cross = cross + fw[k] * (slope[RADIUS + k:RADIUS + k + planes] - slope[RADIUS - k:RADIUS - k + planes])
        lap = summed + 0.7 * cross
        hv = -0.5 * lap + pot_ref[...] * v + nl_ref[...]
        kv = (hv - 12.0 * v) / 8.0
        if with_prev:
            out_ref[...] = scale * kv - prev_ref[...]
        else:
            out_ref[...] = kv
    return kernel

def apply_op(lo, v, hi, pot, nl, prev=None, scale=1.0):
    planes, breadth, depth = v.shape
    args = [lo, v, hi, pot, nl] + ([prev] if prev is not None else [])
    return pl.pallas_call(
        make_kernel(scale, prev is not None),
        out_shape=jax.ShapeDtypeStruct(v.shape, jnp.float32),
        scratch_shapes=[pltpu.VMEM((planes + 2 * RADIUS, breadth, depth), jnp.float32)],
    )(*args)

def shards(states_in, potential, projectors, proj_gains, atom_owner, atom_rows, wrap_rows):
    state_count, tile_width, breadth, line_depth = states_in.shape
    n_grid = lax.axis_size("grid")
    n_states = lax.axis_size("states")
    tile_index = lax.axis_index("grid")
    tile_lines = tile_width * breadth
    block_rows = atom_rows.shape[1]
    line_span = block_rows * line_depth
    proj_count = projectors.shape[2]
    home_count = atom_owner.shape[0]
    slot_pairs = projectors.shape[1]
    row_order = jnp.arange(breadth, dtype=jnp.int32)
    unwrap_rows = jnp.sum(
        row_order[None, :] * (wrap_rows[None, :] == row_order[:, None]).astype(jnp.int32), axis=1
    )
    atom_order = jnp.arange(home_count, dtype=jnp.int32)
    same_owner = (atom_owner[:, None] == atom_owner[None, :]) & (
        atom_order[None, :] < atom_order[:, None]
    )
    owner_rank = jnp.sum(same_owner.astype(jnp.int32), axis=1)
    atom_slot = atom_owner * PAIR_CAP + owner_rank
    local_rows = jnp.where(atom_rows >= 0, atom_rows - tile_index * tile_lines, tile_lines)

    gain_lanes = jnp.zeros((1, slot_pairs, proj_count, 128), jnp.bfloat16)
    gain_lanes = gain_lanes.at[..., 0].set(proj_gains)
    packed = jnp.concatenate([projectors, gain_lanes], axis=3)
    pairs = [(o * n_states + t, t * n_states + o) for o in range(n_grid) for t in range(n_states)]
    packed = lax.ppermute(packed, ("grid", "states"), pairs)
    def flip_y(s):
        return s ^ 8

    def flip_x(s):
        return s ^ 2

    def mirror_x(s):
        x = (s // 2) % 4
        return s + (3 - x - x) * 2

    def flip_core(s):
        return s ^ 1

    exchanges = (flip_y, flip_x, mirror_x, flip_core)

    def origins(me, done):
        if not done:
            return [me]
        return origins(me, done[:-1]) + origins(done[-1](me), done[:-1])

    gathered = packed[0]
    for exchange in exchanges:
        partner = lax.ppermute(
            gathered, "states", [(s, exchange(s)) for s in range(n_states)]
        )
        gathered = jnp.concatenate([gathered, partner], axis=0)
    block_owner = jnp.stack(origins(lax.axis_index("states"), exchanges))
    owner_block = jnp.argmax(block_owner[None, :] == atom_owner[:, None], axis=1)
    gathered = gathered.reshape(n_states * slot_pairs, proj_count, line_span + 128)
    atom_slot = owner_block * PAIR_CAP + owner_rank
    atom_pack = jnp.take(gathered, atom_slot, axis=0)
    proj_rows = atom_pack[:, :, :line_span].reshape(home_count * proj_count, line_span)
    atom_gain = atom_pack[:, :, line_span].astype(jnp.float32)
    selector = (
        local_rows.reshape(-1)[:, None] == jnp.arange(tile_lines, dtype=jnp.int32)[None, :]
    ).astype(jnp.bfloat16)
    atom_eye = jnp.eye(home_count, dtype=jnp.float32)

    def rims(grid_field):
        padded = padded_2(grid_field, (("grid", 1),), RADIUS)
        low_rim = padded[:, :RADIUS]
        high_rim = padded[:, RADIUS + tile_width :]
        low_rim = jnp.where(tile_index == 0, jnp.take(low_rim, wrap_rows, axis=2), low_rim)
        high_rim = jnp.where(
            tile_index == n_grid - 1, jnp.take(high_rim, unwrap_rows, axis=2), high_rim
        )
        return low_rim[0], high_rim[0]

    def nonlocal_part(grid_field):
        lines_here = grid_field.reshape(tile_lines, line_depth).astype(jnp.bfloat16)
        picked = jnp.dot(selector, lines_here, preferred_element_type=jnp.float32)
        picked = picked.astype(jnp.bfloat16).reshape(home_count, line_span)
        every_pair = lax.dot_general(
            proj_rows, picked, (((1,), (1,)), ((), ())), preferred_element_type=jnp.float32
        ).reshape(home_count, proj_count, home_count)
        coefficients = jnp.sum(every_pair * atom_eye[:, None, :], axis=2)
        scaled = (coefficients * atom_gain).astype(jnp.bfloat16)
        block_scaled = (atom_eye.astype(jnp.bfloat16)[:, :, None] * scaled[None, :, :]).reshape(
            home_count, home_count * proj_count
        )
        projected = jnp.dot(block_scaled, proj_rows, preferred_element_type=jnp.float32)
        projected = projected.astype(jnp.bfloat16).reshape(home_count * block_rows, line_depth)
        summed = lax.dot_general(
            selector, projected, (((0,), (0,)), ((), ())), preferred_element_type=jnp.float32
        )
        return summed.reshape(state_count, tile_width, breadth, line_depth)

    def step(grid_field, prev=None, scale=1.0):
        low_rim, high_rim = rims(grid_field)
        nonlocal_lines = nonlocal_part(grid_field)[0]
        out = apply_op(
            low_rim, grid_field[0], high_rim, potential, nonlocal_lines, prev, scale
        )
        return out[None]

    first_term = step(states_in)
    second_term = step(first_term, states_in[0], 2.0)
    return step(second_term, first_term[0], 2.0)


def solution(mesh):
    in_specs = (
        P("states", "grid", None, None),
        P("grid", None, None),
        P("grid", "states", None, None),
        P("grid", "states", None),
        P("grid"),
        P("grid", None),
        P(),
    )
    out_specs = P("states", "grid", None, None)
    return jax.shard_map(shards, mesh=mesh, in_specs=in_specs, out_specs=out_specs, check_vma=False)
```

```python
import math

import jax
import jax.numpy as jnp
from jax import lax
from jax.experimental import pallas as pl
from jax.experimental.pallas import tpu as pltpu
from jax.sharding import PartitionSpec as P

RADIUS = 6
PAIR_CAP = 2


MIXED_WEIGHT = 0.7
CENTER = 12.0
HALF_WIDTH = 8.0


def padded_2(shard, sides, width):
    for axis, dim in sides:
        count, length = (lax.axis_size(axis), shard.shape[dim])
        up = [(i, (i + 1) % count) for i in range(count)]
        down = [(j, i) for i, j in up]
        last = lax.slice_in_dim(shard, length - width, length, axis=dim)
        initial = lax.slice_in_dim(shard, 0, width, axis=dim)
        before = lax.ppermute(last, axis, up)
        after = lax.ppermute(initial, axis, down)
        shard = jnp.concatenate([before, shard, after], axis=dim)
    return shard


def second_table(radius):
    weights = [-2.0 * sum((1.0 / (k * k) for k in range(1, radius + 1)))]
    for k in range(1, radius + 1):
        weights.append(
            2.0
            * (-1) ** (k + 1)
            * math.factorial(radius) ** 2
            / (k * k * math.factorial(radius - k) * math.factorial(radius + k))
        )
    return weights


def first_table(radius):
    weights = [0.0]
    for k in range(1, radius + 1):
        weights.append(
            (-1) ** (k + 1)
            * math.factorial(radius) ** 2
            / (k * math.factorial(radius - k) * math.factorial(radius + k))
        )
    return weights


def laplacian(padded, plane_count):
    second_weights = second_table(RADIUS)
    first_weights = first_table(RADIUS)
    interior = padded[:, RADIUS : RADIUS + plane_count]
    line_depth = interior.shape[3]
    z_padded = jnp.pad(interior, ((0, 0), (0, 0), (0, 0), (RADIUS, RADIUS)))
    summed = 3.0 * second_weights[0] * interior
    y_slope = jnp.zeros_like(padded)
    for k in range(1, RADIUS + 1):
        summed = summed + second_weights[k] * (
            padded[:, RADIUS + k : RADIUS + k + plane_count]
            + padded[:, RADIUS - k : RADIUS - k + plane_count]
        )
        summed = summed + second_weights[k] * (jnp.roll(interior, -k, 2) + jnp.roll(interior, k, 2))
        summed = summed + second_weights[k] * (
            z_padded[:, :, :, RADIUS + k : RADIUS + k + line_depth]
            + z_padded[:, :, :, RADIUS - k : RADIUS - k + line_depth]
        )
        y_slope = y_slope + first_weights[k] * (jnp.roll(padded, -k, 2) - jnp.roll(padded, k, 2))
    cross_term = jnp.zeros_like(interior)
    for k in range(1, RADIUS + 1):
        cross_term = cross_term + first_weights[k] * (
            y_slope[:, RADIUS + k : RADIUS + k + plane_count]
            - y_slope[:, RADIUS - k : RADIUS - k + plane_count]
        )
    return summed + MIXED_WEIGHT * cross_term


def make_kernel(scale, with_prev):
    sw = second_table(RADIUS); fw = first_table(RADIUS)
    def kernel(lo_ref, v_ref, hi_ref, pot_ref, nl_ref, *rest):
        if with_prev:
            prev_ref, out_ref, pad_ref = rest
        else:
            out_ref, pad_ref = rest
        planes, breadth, depth = v_ref.shape
        v = v_ref[...]
        pad_ref[0:RADIUS] = lo_ref[...]
        pad_ref[RADIUS:RADIUS + planes] = v
        pad_ref[RADIUS + planes:] = hi_ref[...]
        lane = jax.lax.broadcasted_iota(jnp.int32, v.shape, 2)
        summed = (3.0 * sw[0]) * v
        for k in range(1, RADIUS + 1):
            xs = pad_ref[RADIUS + k:RADIUS + k + planes] + pad_ref[RADIUS - k:RADIUS - k + planes]
            ys = pltpu.roll(v, breadth - k, 1) + pltpu.roll(v, k, 1)
            zs = (jnp.where(lane < depth - k, pltpu.roll(v, depth - k, 2), 0.0)
                  + jnp.where(lane >= k, pltpu.roll(v, k, 2), 0.0))
            summed = summed + sw[k] * xs + sw[k] * ys + sw[k] * zs
        padded = pad_ref[...]
        slope = fw[1] * (pltpu.roll(padded, breadth - 1, 1) - pltpu.roll(padded, 1, 1))
        for k in range(2, RADIUS + 1):
            slope = slope + fw[k] * (pltpu.roll(padded, breadth - k, 1) - pltpu.roll(padded, k, 1))
        cross = fw[1] * (slope[RADIUS + 1:RADIUS + 1 + planes] - slope[RADIUS - 1:RADIUS - 1 + planes])
        for k in range(2, RADIUS + 1):
            cross = cross + fw[k] * (slope[RADIUS + k:RADIUS + k + planes] - slope[RADIUS - k:RADIUS - k + planes])
        lap = summed + 0.7 * cross
        hv = -0.5 * lap + pot_ref[...] * v + nl_ref[...]
        kv = (hv - 12.0 * v) / 8.0
        if with_prev:
            out_ref[...] = scale * kv - prev_ref[...]
        else:
            out_ref[...] = kv
    return kernel

def apply_op(lo, v, hi, pot, nl, prev=None, scale=1.0):
    planes, breadth, depth = v.shape
    args = [lo, v, hi, pot, nl] + ([prev] if prev is not None else [])
    return pl.pallas_call(
        make_kernel(scale, prev is not None),
        out_shape=jax.ShapeDtypeStruct(v.shape, jnp.float32),
        scratch_shapes=[pltpu.VMEM((planes + 2 * RADIUS, breadth, depth), jnp.float32)],
    )(*args)

def shards(states_in, potential, projectors, proj_gains, atom_owner, atom_rows, wrap_rows):
    state_count, tile_width, breadth, line_depth = states_in.shape
    n_grid = lax.axis_size("grid")
    n_states = lax.axis_size("states")
    tile_index = lax.axis_index("grid")
    tile_lines = tile_width * breadth
    block_rows = atom_rows.shape[1]
    line_span = block_rows * line_depth
    proj_count = projectors.shape[2]
    home_count = atom_owner.shape[0]
    slot_pairs = projectors.shape[1]
    row_order = jnp.arange(breadth, dtype=jnp.int32)
    unwrap_rows = jnp.sum(
        row_order[None, :] * (wrap_rows[None, :] == row_order[:, None]).astype(jnp.int32), axis=1
    )
    atom_order = jnp.arange(home_count, dtype=jnp.int32)
    same_owner = (atom_owner[:, None] == atom_owner[None, :]) & (
        atom_order[None, :] < atom_order[:, None]
    )
    owner_rank = jnp.sum(same_owner.astype(jnp.int32), axis=1)
    atom_slot = atom_owner * PAIR_CAP + owner_rank
    local_rows = jnp.where(atom_rows >= 0, atom_rows - tile_index * tile_lines, tile_lines)

    gain_lanes = jnp.zeros((1, slot_pairs, proj_count, 128), jnp.bfloat16)
    gain_lanes = gain_lanes.at[..., 0].set(proj_gains)
    packed = jnp.concatenate([projectors, gain_lanes], axis=3)
    pairs = [(o * n_states + t, t * n_states + o) for o in range(n_grid) for t in range(n_states)]
    packed = lax.ppermute(packed, ("grid", "states"), pairs)
    packed, states_in = lax.optimization_barrier((packed, states_in))
    def flip_y(s):
        return s ^ 8

    def flip_x(s):
        return s ^ 2

    def mirror_x(s):
        x = (s // 2) % 4
        return s + (3 - x - x) * 2

    def flip_core(s):
        return s ^ 1

    exchanges = (flip_y, flip_x, mirror_x, flip_core)

    def origins(me, done):
        if not done:
            return [me]
        return origins(me, done[:-1]) + origins(done[-1](me), done[:-1])

    gathered = packed[0]
    for exchange in exchanges:
        partner = lax.ppermute(
            gathered, "states", [(s, exchange(s)) for s in range(n_states)]
        )
        gathered = jnp.concatenate([gathered, partner], axis=0)
    block_owner = jnp.stack(origins(lax.axis_index("states"), exchanges))
    owner_block = jnp.argmax(block_owner[None, :] == atom_owner[:, None], axis=1)
    gathered = gathered.reshape(n_states * slot_pairs, proj_count, line_span + 128)
    atom_slot = owner_block * PAIR_CAP + owner_rank
    atom_pack = jnp.take(gathered, atom_slot, axis=0)
    proj_rows = atom_pack[:, :, :line_span].reshape(home_count * proj_count, line_span)
    atom_gain = atom_pack[:, :, line_span].astype(jnp.float32)
    selector = (
        local_rows.reshape(-1)[:, None] == jnp.arange(tile_lines, dtype=jnp.int32)[None, :]
    ).astype(jnp.bfloat16)
    atom_eye = jnp.eye(home_count, dtype=jnp.float32)

    def rims(grid_field):
        padded = padded_2(grid_field, (("grid", 1),), RADIUS)
        low_rim = padded[:, :RADIUS]
        high_rim = padded[:, RADIUS + tile_width :]
        low_rim = jnp.where(tile_index == 0, jnp.take(low_rim, wrap_rows, axis=2), low_rim)
        high_rim = jnp.where(
            tile_index == n_grid - 1, jnp.take(high_rim, unwrap_rows, axis=2), high_rim
        )
        return low_rim[0], high_rim[0]

    def nonlocal_part(grid_field):
        lines_here = grid_field.reshape(tile_lines, line_depth).astype(jnp.bfloat16)
        picked = jnp.dot(selector, lines_here, preferred_element_type=jnp.float32)
        picked = picked.astype(jnp.bfloat16).reshape(home_count, line_span)
        every_pair = lax.dot_general(
            proj_rows, picked, (((1,), (1,)), ((), ())), preferred_element_type=jnp.float32
        ).reshape(home_count, proj_count, home_count)
        coefficients = jnp.sum(every_pair * atom_eye[:, None, :], axis=2)
        scaled = (coefficients * atom_gain).astype(jnp.bfloat16)
        block_scaled = (atom_eye.astype(jnp.bfloat16)[:, :, None] * scaled[None, :, :]).reshape(
            home_count, home_count * proj_count
        )
        projected = jnp.dot(block_scaled, proj_rows, preferred_element_type=jnp.float32)
        projected = projected.astype(jnp.bfloat16).reshape(home_count * block_rows, line_depth)
        summed = lax.dot_general(
            selector, projected, (((0,), (0,)), ((), ())), preferred_element_type=jnp.float32
        )
        return summed.reshape(state_count, tile_width, breadth, line_depth)

    def step(grid_field, prev=None, scale=1.0):
        low_rim, high_rim = rims(grid_field)
        nonlocal_lines = nonlocal_part(grid_field)[0]
        out = apply_op(
            low_rim, grid_field[0], high_rim, potential, nonlocal_lines, prev, scale
        )
        return out[None]

    first_term = step(states_in)
    second_term = step(first_term, states_in[0], 2.0)
    return step(second_term, first_term[0], 2.0)


def solution(mesh):
    in_specs = (
        P("states", "grid", None, None),
        P("grid", None, None),
        P("grid", "states", None, None),
        P("grid", "states", None),
        P("grid"),
        P("grid", None),
        P(),
    )
    out_specs = P("states", "grid", None, None)
    return jax.shard_map(shards, mesh=mesh, in_specs=in_specs, out_specs=out_specs, check_vma=False)
```

```python
import math

import jax
import jax.numpy as jnp
from jax import lax
from jax.experimental import pallas as pl
from jax.experimental.pallas import tpu as pltpu
from jax.sharding import PartitionSpec as P

RADIUS = 6
PAIR_CAP = 2


MIXED_WEIGHT = 0.7
CENTER = 12.0
HALF_WIDTH = 8.0


def padded_2(shard, sides, width):
    for axis, dim in sides:
        count, length = (lax.axis_size(axis), shard.shape[dim])
        up = [(i, (i + 1) % count) for i in range(count)]
        down = [(j, i) for i, j in up]
        last = lax.slice_in_dim(shard, length - width, length, axis=dim)
        initial = lax.slice_in_dim(shard, 0, width, axis=dim)
        before = lax.ppermute(last, axis, up)
        after = lax.ppermute(initial, axis, down)
        shard = jnp.concatenate([before, shard, after], axis=dim)
    return shard


def second_table(radius):
    weights = [-2.0 * sum((1.0 / (k * k) for k in range(1, radius + 1)))]
    for k in range(1, radius + 1):
        weights.append(
            2.0
            * (-1) ** (k + 1)
            * math.factorial(radius) ** 2
            / (k * k * math.factorial(radius - k) * math.factorial(radius + k))
        )
    return weights


def first_table(radius):
    weights = [0.0]
    for k in range(1, radius + 1):
        weights.append(
            (-1) ** (k + 1)
            * math.factorial(radius) ** 2
            / (k * math.factorial(radius - k) * math.factorial(radius + k))
        )
    return weights


def laplacian(padded, plane_count):
    second_weights = second_table(RADIUS)
    first_weights = first_table(RADIUS)
    interior = padded[:, RADIUS : RADIUS + plane_count]
    line_depth = interior.shape[3]
    z_padded = jnp.pad(interior, ((0, 0), (0, 0), (0, 0), (RADIUS, RADIUS)))
    summed = 3.0 * second_weights[0] * interior
    y_slope = jnp.zeros_like(padded)
    for k in range(1, RADIUS + 1):
        summed = summed + second_weights[k] * (
            padded[:, RADIUS + k : RADIUS + k + plane_count]
            + padded[:, RADIUS - k : RADIUS - k + plane_count]
        )
        summed = summed + second_weights[k] * (jnp.roll(interior, -k, 2) + jnp.roll(interior, k, 2))
        summed = summed + second_weights[k] * (
            z_padded[:, :, :, RADIUS + k : RADIUS + k + line_depth]
            + z_padded[:, :, :, RADIUS - k : RADIUS - k + line_depth]
        )
        y_slope = y_slope + first_weights[k] * (jnp.roll(padded, -k, 2) - jnp.roll(padded, k, 2))
    cross_term = jnp.zeros_like(interior)
    for k in range(1, RADIUS + 1):
        cross_term = cross_term + first_weights[k] * (
            y_slope[:, RADIUS + k : RADIUS + k + plane_count]
            - y_slope[:, RADIUS - k : RADIUS - k + plane_count]
        )
    return summed + MIXED_WEIGHT * cross_term


def make_kernel(scale, with_prev, home_count, proj_count, block_rows):
    sw = second_table(RADIUS)
    fw = first_table(RADIUS)

    def kernel(shift_ref, lo_ref, v_ref, hi_ref, pot_ref, pick_ref, place_ref, proj_ref, gain_ref, *rest):
        if with_prev:
            prev_ref, out_ref, pad_ref, rows_ref = rest
        else:
            out_ref, pad_ref, rows_ref = rest
        planes, breadth, depth = v_ref.shape
        v = v_ref[...]
        pad_ref[0:RADIUS] = pltpu.roll(lo_ref[...], shift_ref[0], 1)
        pad_ref[RADIUS:RADIUS + planes] = v
        pad_ref[RADIUS + planes:] = pltpu.roll(hi_ref[...], shift_ref[1], 1)

        lines = v.reshape(planes * breadth, depth).astype(jnp.bfloat16)
        picked = jnp.dot(pick_ref[...], lines, preferred_element_type=jnp.float32)

        def one_atom(a, carry):
            base = pl.multiple_of(a * block_rows, block_rows)
            here = picked_ref_load(base)
            acc = jnp.zeros((block_rows, depth), jnp.float32)
            for j in range(proj_count):
                proj = proj_ref[a * proj_count + j].astype(jnp.float32)
                coef = jnp.sum(jnp.sum(proj * here, axis=0, keepdims=True), axis=1, keepdims=True)
                gain = gain_ref[a * proj_count + j]
                scaled = (coef * gain).astype(jnp.bfloat16).astype(jnp.float32)
                acc = acc + proj * scaled
            rows_ref[pl.ds(base, block_rows), :] = acc.astype(jnp.bfloat16)
            return carry

        rows_ref[...] = picked.astype(jnp.bfloat16)

        def picked_ref_load(base):
            return rows_ref[pl.ds(base, block_rows), :].astype(jnp.float32)

        lax.fori_loop(0, home_count, one_atom, 0)
        nonlocal_lines = jnp.dot(place_ref[...], rows_ref[...], preferred_element_type=jnp.float32)
        nonlocal_lines = nonlocal_lines.reshape(planes, breadth, depth)

        lane = lax.broadcasted_iota(jnp.int32, v.shape, 2)
        summed = (3.0 * sw[0]) * v
        for k in range(1, RADIUS + 1):
            xs = pad_ref[RADIUS + k:RADIUS + k + planes] + pad_ref[RADIUS - k:RADIUS - k + planes]
            ys = pltpu.roll(v, breadth - k, 1) + pltpu.roll(v, k, 1)
            zs = (jnp.where(lane < depth - k, pltpu.roll(v, depth - k, 2), 0.0)
                  + jnp.where(lane >= k, pltpu.roll(v, k, 2), 0.0))
            summed = summed + sw[k] * xs + sw[k] * ys + sw[k] * zs
        padded = pad_ref[...]
        slope = fw[1] * (pltpu.roll(padded, breadth - 1, 1) - pltpu.roll(padded, 1, 1))
        for k in range(2, RADIUS + 1):
            slope = slope + fw[k] * (pltpu.roll(padded, breadth - k, 1) - pltpu.roll(padded, k, 1))
        cross = fw[1] * (slope[RADIUS + 1:RADIUS + 1 + planes] - slope[RADIUS - 1:RADIUS - 1 + planes])
        for k in range(2, RADIUS + 1):
            cross = cross + fw[k] * (slope[RADIUS + k:RADIUS + k + planes] - slope[RADIUS - k:RADIUS - k + planes])
        lap = summed + 0.7 * cross
        hv = -0.5 * lap + pot_ref[...] * v + nonlocal_lines
        kv = (hv - 12.0 * v) / 8.0
        if with_prev:
            out_ref[...] = scale * kv - prev_ref[...]
        else:
            out_ref[...] = kv

    return kernel


def apply_op(shifts, lo, v, hi, pot, pick, place, proj, gain, prev=None, scale=1.0):
    planes, breadth, depth = v.shape
    picked_rows = pick.shape[0]
    home_count = proj.shape[0] // 8
    block_rows = picked_rows // home_count
    args = [shifts, lo, v, hi, pot, pick, place, proj, gain] + ([prev] if prev is not None else [])
    vspec = pl.BlockSpec(memory_space=pltpu.VMEM)
    in_specs = [pl.BlockSpec(memory_space=pltpu.SMEM)] + [vspec] * (len(args) - 1)
    return pl.pallas_call(
        make_kernel(scale, prev is not None, home_count, proj.shape[0] // home_count, block_rows),
        out_shape=jax.ShapeDtypeStruct(v.shape, jnp.float32),
        in_specs=in_specs,
        out_specs=vspec,
        scratch_shapes=[
            pltpu.VMEM((planes + 2 * RADIUS, breadth, depth), jnp.float32),
            pltpu.VMEM((picked_rows, depth), jnp.bfloat16),
        ],
    )(*args)


def shards(states_in, potential, projectors, proj_gains, atom_owner, atom_rows, wrap_rows):
    state_count, tile_width, breadth, line_depth = states_in.shape
    n_grid = lax.axis_size("grid")
    n_states = lax.axis_size("states")
    tile_index = lax.axis_index("grid")
    tile_lines = tile_width * breadth
    block_rows = atom_rows.shape[1]
    line_span = block_rows * line_depth
    proj_count = projectors.shape[2]
    home_count = atom_owner.shape[0]
    slot_pairs = projectors.shape[1]
    row_order = jnp.arange(breadth, dtype=jnp.int32)
    unwrap_rows = jnp.sum(
        row_order[None, :] * (wrap_rows[None, :] == row_order[:, None]).astype(jnp.int32), axis=1
    )
    atom_order = jnp.arange(home_count, dtype=jnp.int32)
    same_owner = (atom_owner[:, None] == atom_owner[None, :]) & (
        atom_order[None, :] < atom_order[:, None]
    )
    owner_rank = jnp.sum(same_owner.astype(jnp.int32), axis=1)
    atom_slot = atom_owner * PAIR_CAP + owner_rank
    local_rows = jnp.where(atom_rows >= 0, atom_rows - tile_index * tile_lines, tile_lines)

    gain_lanes = jnp.zeros((1, slot_pairs, proj_count, 128), jnp.bfloat16)
    gain_lanes = gain_lanes.at[..., 0].set(proj_gains)
    packed = jnp.concatenate([projectors, gain_lanes], axis=3)
    pairs = [(o * n_states + t, t * n_states + o) for o in range(n_grid) for t in range(n_states)]
    packed = lax.ppermute(packed, ("grid", "states"), pairs)
    def flip_y(s):
        return s ^ 8

    def flip_x(s):
        return s ^ 2

    def mirror_x(s):
        x = (s // 2) % 4
        return s + (3 - x - x) * 2

    def flip_core(s):
        return s ^ 1

    exchanges = (flip_y, flip_x, mirror_x, flip_core)

    def origins(me, done):
        if not done:
            return [me]
        return origins(me, done[:-1]) + origins(done[-1](me), done[:-1])

    gathered = packed[0]
    for exchange in exchanges:
        partner = lax.ppermute(
            gathered, "states", [(s, exchange(s)) for s in range(n_states)]
        )
        gathered = jnp.concatenate([gathered, partner], axis=0)
    block_owner = jnp.stack(origins(lax.axis_index("states"), exchanges))
    owner_block = jnp.argmax(block_owner[None, :] == atom_owner[:, None], axis=1)
    gathered = gathered.reshape(n_states * slot_pairs, proj_count, line_span + 128)
    atom_slot = owner_block * PAIR_CAP + owner_rank
    atom_pack = jnp.take(gathered, atom_slot, axis=0)
    proj_rows = atom_pack[:, :, :line_span].reshape(home_count * proj_count, line_span)
    atom_gain = atom_pack[:, :, line_span].astype(jnp.float32)
    pick = (
        local_rows.reshape(-1)[:, None] == jnp.arange(tile_lines, dtype=jnp.int32)[None, :]
    ).astype(jnp.bfloat16)
    place = pick.T
    proj_in = proj_rows.reshape(home_count * proj_count, breadth, line_depth)
    gain_in = jnp.broadcast_to(
        atom_gain.reshape(home_count * proj_count, 1, 1), (home_count * proj_count, 1, line_depth)
    )
    skew = wrap_rows[0]
    shifts = jnp.stack(
        [
            jnp.where(tile_index == 0, (breadth - skew) % breadth, 0),
            jnp.where(tile_index == n_grid - 1, skew, 0),
            jnp.zeros((), jnp.int32),
            jnp.zeros((), jnp.int32),
        ]
    ).astype(jnp.int32)
    up = [(i, (i + 1) % n_grid) for i in range(n_grid)]
    down = [(j, i) for i, j in up]

    def step(grid_field, prev=None, scale=1.0):
        field = grid_field[0]
        low_rim = lax.ppermute(field[tile_width - RADIUS :], "grid", up)
        high_rim = lax.ppermute(field[:RADIUS], "grid", down)
        out = apply_op(
            shifts, low_rim, field, high_rim, potential, pick, place, proj_in, gain_in, prev, scale
        )
        return out[None]

    first_term = step(states_in)
    second_term = step(first_term, states_in[0], 2.0)
    return step(second_term, first_term[0], 2.0)


def solution(mesh):
    in_specs = (
        P("states", "grid", None, None),
        P("grid", None, None),
        P("grid", "states", None, None),
        P("grid", "states", None),
        P("grid"),
        P("grid", None),
        P(),
    )
    out_specs = P("states", "grid", None, None)
    return jax.shard_map(shards, mesh=mesh, in_specs=in_specs, out_specs=out_specs, check_vma=False)
```

```python
import math

import jax
import jax.numpy as jnp
from jax import lax
from jax.experimental import pallas as pl
from jax.experimental.pallas import tpu as pltpu
from jax.sharding import PartitionSpec as P

RADIUS = 6
PAIR_CAP = 2


MIXED_WEIGHT = 0.7
CENTER = 12.0
HALF_WIDTH = 8.0


def padded_2(shard, sides, width):
    for axis, dim in sides:
        count, length = (lax.axis_size(axis), shard.shape[dim])
        up = [(i, (i + 1) % count) for i in range(count)]
        down = [(j, i) for i, j in up]
        last = lax.slice_in_dim(shard, length - width, length, axis=dim)
        initial = lax.slice_in_dim(shard, 0, width, axis=dim)
        before = lax.ppermute(last, axis, up)
        after = lax.ppermute(initial, axis, down)
        shard = jnp.concatenate([before, shard, after], axis=dim)
    return shard


def second_table(radius):
    weights = [-2.0 * sum((1.0 / (k * k) for k in range(1, radius + 1)))]
    for k in range(1, radius + 1):
        weights.append(
            2.0
            * (-1) ** (k + 1)
            * math.factorial(radius) ** 2
            / (k * k * math.factorial(radius - k) * math.factorial(radius + k))
        )
    return weights


def first_table(radius):
    weights = [0.0]
    for k in range(1, radius + 1):
        weights.append(
            (-1) ** (k + 1)
            * math.factorial(radius) ** 2
            / (k * math.factorial(radius - k) * math.factorial(radius + k))
        )
    return weights


def laplacian(padded, plane_count):
    second_weights = second_table(RADIUS)
    first_weights = first_table(RADIUS)
    interior = padded[:, RADIUS : RADIUS + plane_count]
    line_depth = interior.shape[3]
    z_padded = jnp.pad(interior, ((0, 0), (0, 0), (0, 0), (RADIUS, RADIUS)))
    summed = 3.0 * second_weights[0] * interior
    y_slope = jnp.zeros_like(padded)
    for k in range(1, RADIUS + 1):
        summed = summed + second_weights[k] * (
            padded[:, RADIUS + k : RADIUS + k + plane_count]
            + padded[:, RADIUS - k : RADIUS - k + plane_count]
        )
        summed = summed + second_weights[k] * (jnp.roll(interior, -k, 2) + jnp.roll(interior, k, 2))
        summed = summed + second_weights[k] * (
            z_padded[:, :, :, RADIUS + k : RADIUS + k + line_depth]
            + z_padded[:, :, :, RADIUS - k : RADIUS - k + line_depth]
        )
        y_slope = y_slope + first_weights[k] * (jnp.roll(padded, -k, 2) - jnp.roll(padded, k, 2))
    cross_term = jnp.zeros_like(interior)
    for k in range(1, RADIUS + 1):
        cross_term = cross_term + first_weights[k] * (
            y_slope[:, RADIUS + k : RADIUS + k + plane_count]
            - y_slope[:, RADIUS - k : RADIUS - k + plane_count]
        )
    return summed + MIXED_WEIGHT * cross_term


def make_kernel(scale, with_prev, home_count, proj_count, block_rows):
    sw = second_table(RADIUS)
    fw = first_table(RADIUS)

    def kernel(shift_ref, lo_ref, v_ref, hi_ref, pot_ref, pick_ref, place_ref, proj_ref, gain_ref, *rest):
        if with_prev:
            prev_ref, out_ref, pad_ref, rows_ref = rest
        else:
            out_ref, pad_ref, rows_ref = rest
        planes, breadth, depth = v_ref.shape
        v = v_ref[...]
        pad_ref[0:RADIUS] = pltpu.roll(lo_ref[...], shift_ref[0], 1)
        pad_ref[RADIUS:RADIUS + planes] = v
        pad_ref[RADIUS + planes:] = pltpu.roll(hi_ref[...], shift_ref[1], 1)

        lines = v.reshape(planes * breadth, depth).astype(jnp.bfloat16)
        picked = jnp.dot(pick_ref[...], lines, preferred_element_type=jnp.float32)

        def one_atom(a, carry):
            base = pl.multiple_of(a * block_rows, block_rows)
            here = picked_ref_load(base)
            acc = jnp.zeros((block_rows, depth), jnp.float32)
            for j in range(proj_count):
                proj = proj_ref[a * proj_count + j].astype(jnp.float32)
                coef = jnp.sum(jnp.sum(proj * here, axis=0, keepdims=True), axis=1, keepdims=True)
                gain = gain_ref[a * proj_count + j]
                scaled = (coef * gain).astype(jnp.bfloat16).astype(jnp.float32)
                acc = acc + proj * scaled
            rows_ref[pl.ds(base, block_rows), :] = acc.astype(jnp.bfloat16)
            return carry

        rows_ref[...] = picked.astype(jnp.bfloat16)

        def picked_ref_load(base):
            return rows_ref[pl.ds(base, block_rows), :].astype(jnp.float32)

        lax.fori_loop(0, home_count, one_atom, 0)
        nonlocal_lines = jnp.dot(place_ref[...], rows_ref[...], preferred_element_type=jnp.float32)
        nonlocal_lines = nonlocal_lines.reshape(planes, breadth, depth)

        lane = lax.broadcasted_iota(jnp.int32, v.shape, 2)
        summed = (3.0 * sw[0]) * v
        for k in range(1, RADIUS + 1):
            xs = pad_ref[RADIUS + k:RADIUS + k + planes] + pad_ref[RADIUS - k:RADIUS - k + planes]
            ys = pltpu.roll(v, breadth - k, 1) + pltpu.roll(v, k, 1)
            zs = (jnp.where(lane < depth - k, pltpu.roll(v, depth - k, 2), 0.0)
                  + jnp.where(lane >= k, pltpu.roll(v, k, 2), 0.0))
            summed = summed + sw[k] * xs + sw[k] * ys + sw[k] * zs
        padded = pad_ref[...]
        slope = fw[1] * (pltpu.roll(padded, breadth - 1, 1) - pltpu.roll(padded, 1, 1))
        for k in range(2, RADIUS + 1):
            slope = slope + fw[k] * (pltpu.roll(padded, breadth - k, 1) - pltpu.roll(padded, k, 1))
        cross = fw[1] * (slope[RADIUS + 1:RADIUS + 1 + planes] - slope[RADIUS - 1:RADIUS - 1 + planes])
        for k in range(2, RADIUS + 1):
            cross = cross + fw[k] * (slope[RADIUS + k:RADIUS + k + planes] - slope[RADIUS - k:RADIUS - k + planes])
        lap = summed + 0.7 * cross
        hv = -0.5 * lap + pot_ref[...] * v + nonlocal_lines
        kv = (hv - 12.0 * v) / 8.0
        if with_prev:
            out_ref[...] = scale * kv - prev_ref[...]
        else:
            out_ref[...] = kv

    return kernel


def apply_op(shifts, lo, v, hi, pot, pick, place, proj, gain, prev=None, scale=1.0):
    planes, breadth, depth = v.shape
    picked_rows = pick.shape[0]
    home_count = proj.shape[0] // 8
    block_rows = picked_rows // home_count
    args = [shifts, lo, v, hi, pot, pick, place, proj, gain] + ([prev] if prev is not None else [])
    vspec = pl.BlockSpec(memory_space=pltpu.VMEM)
    in_specs = [pl.BlockSpec(memory_space=pltpu.SMEM)] + [vspec] * (len(args) - 1)
    return pl.pallas_call(
        make_kernel(scale, prev is not None, home_count, proj.shape[0] // home_count, block_rows),
        out_shape=jax.ShapeDtypeStruct(v.shape, jnp.float32),
        in_specs=in_specs,
        out_specs=vspec,
        scratch_shapes=[
            pltpu.VMEM((planes + 2 * RADIUS, breadth, depth), jnp.float32),
            pltpu.VMEM((picked_rows, depth), jnp.bfloat16),
        ],
    )(*args)


def shards(states_in, potential, projectors, proj_gains, atom_owner, atom_rows, wrap_rows):
    state_count, tile_width, breadth, line_depth = states_in.shape
    n_grid = lax.axis_size("grid")
    n_states = lax.axis_size("states")
    tile_index = lax.axis_index("grid")
    tile_lines = tile_width * breadth
    block_rows = atom_rows.shape[1]
    line_span = block_rows * line_depth
    proj_count = projectors.shape[2]
    home_count = atom_owner.shape[0]
    slot_pairs = projectors.shape[1]
    row_order = jnp.arange(breadth, dtype=jnp.int32)
    unwrap_rows = jnp.sum(
        row_order[None, :] * (wrap_rows[None, :] == row_order[:, None]).astype(jnp.int32), axis=1
    )
    atom_order = jnp.arange(home_count, dtype=jnp.int32)
    same_owner = (atom_owner[:, None] == atom_owner[None, :]) & (
        atom_order[None, :] < atom_order[:, None]
    )
    owner_rank = jnp.sum(same_owner.astype(jnp.int32), axis=1)
    atom_slot = atom_owner * PAIR_CAP + owner_rank
    local_rows = jnp.where(atom_rows >= 0, atom_rows - tile_index * tile_lines, tile_lines)

    gain_lanes = jnp.zeros((1, slot_pairs, proj_count, 128), jnp.bfloat16)
    gain_lanes = gain_lanes.at[..., 0].set(proj_gains)
    packed = jnp.concatenate([projectors, gain_lanes], axis=3)
    pairs = [(o * n_states + t, t * n_states + o) for o in range(n_grid) for t in range(n_states)]
    packed = lax.ppermute(packed, ("grid", "states"), pairs)
    me = lax.axis_index("states")
    blocks = [packed[0]]
    for d in range(1, n_states):
        blocks.append(lax.ppermute(packed[0], "states", [(s, s ^ d) for s in range(n_states)]))
    gathered = jnp.concatenate(blocks, axis=0)
    gathered = gathered.reshape(n_states * slot_pairs, proj_count, line_span + 128)
    atom_slot = (atom_owner ^ me) * PAIR_CAP + owner_rank
    atom_pack = jnp.take(gathered, atom_slot, axis=0)
    proj_rows = atom_pack[:, :, :line_span].reshape(home_count * proj_count, line_span)
    atom_gain = atom_pack[:, :, line_span].astype(jnp.float32)
    pick = (
        local_rows.reshape(-1)[:, None] == jnp.arange(tile_lines, dtype=jnp.int32)[None, :]
    ).astype(jnp.bfloat16)
    place = pick.T
    proj_in = proj_rows.reshape(home_count * proj_count, breadth, line_depth)
    gain_in = jnp.broadcast_to(
        atom_gain.reshape(home_count * proj_count, 1, 1), (home_count * proj_count, 1, line_depth)
    )
    skew = wrap_rows[0]
    shifts = jnp.stack(
        [
            jnp.where(tile_index == 0, (breadth - skew) % breadth, 0),
            jnp.where(tile_index == n_grid - 1, skew, 0),
            jnp.zeros((), jnp.int32),
            jnp.zeros((), jnp.int32),
        ]
    ).astype(jnp.int32)
    up = [(i, (i + 1) % n_grid) for i in range(n_grid)]
    down = [(j, i) for i, j in up]

    def step(grid_field, prev=None, scale=1.0):
        field = grid_field[0]
        low_rim = lax.ppermute(field[tile_width - RADIUS :], "grid", up)
        high_rim = lax.ppermute(field[:RADIUS], "grid", down)
        out = apply_op(
            shifts, low_rim, field, high_rim, potential, pick, place, proj_in, gain_in, prev, scale
        )
        return out[None]

    first_term = step(states_in)
    second_term = step(first_term, states_in[0], 2.0)
    return step(second_term, first_term[0], 2.0)


def solution(mesh):
    in_specs = (
        P("states", "grid", None, None),
        P("grid", None, None),
        P("grid", "states", None, None),
        P("grid", "states", None),
        P("grid"),
        P("grid", None),
        P(),
    )
    out_specs = P("states", "grid", None, None)
    return jax.shard_map(shards, mesh=mesh, in_specs=in_specs, out_specs=out_specs, check_vma=False)
```

```python
import math

import jax
import jax.numpy as jnp
from jax import lax
from jax.experimental import pallas as pl
from jax.experimental.pallas import tpu as pltpu
from jax.sharding import PartitionSpec as P

RADIUS = 6
PAIR_CAP = 2


MIXED_WEIGHT = 0.7
CENTER = 12.0
HALF_WIDTH = 8.0


def padded_2(shard, sides, width):
    for axis, dim in sides:
        count, length = (lax.axis_size(axis), shard.shape[dim])
        up = [(i, (i + 1) % count) for i in range(count)]
        down = [(j, i) for i, j in up]
        last = lax.slice_in_dim(shard, length - width, length, axis=dim)
        initial = lax.slice_in_dim(shard, 0, width, axis=dim)
        before = lax.ppermute(last, axis, up)
        after = lax.ppermute(initial, axis, down)
        shard = jnp.concatenate([before, shard, after], axis=dim)
    return shard


def second_table(radius):
    weights = [-2.0 * sum((1.0 / (k * k) for k in range(1, radius + 1)))]
    for k in range(1, radius + 1):
        weights.append(
            2.0
            * (-1) ** (k + 1)
            * math.factorial(radius) ** 2
            / (k * k * math.factorial(radius - k) * math.factorial(radius + k))
        )
    return weights


def first_table(radius):
    weights = [0.0]
    for k in range(1, radius + 1):
        weights.append(
            (-1) ** (k + 1)
            * math.factorial(radius) ** 2
            / (k * math.factorial(radius - k) * math.factorial(radius + k))
        )
    return weights


def laplacian(padded, plane_count):
    second_weights = second_table(RADIUS)
    first_weights = first_table(RADIUS)
    interior = padded[:, RADIUS : RADIUS + plane_count]
    line_depth = interior.shape[3]
    z_padded = jnp.pad(interior, ((0, 0), (0, 0), (0, 0), (RADIUS, RADIUS)))
    summed = 3.0 * second_weights[0] * interior
    y_slope = jnp.zeros_like(padded)
    for k in range(1, RADIUS + 1):
        summed = summed + second_weights[k] * (
            padded[:, RADIUS + k : RADIUS + k + plane_count]
            + padded[:, RADIUS - k : RADIUS - k + plane_count]
        )
        summed = summed + second_weights[k] * (jnp.roll(interior, -k, 2) + jnp.roll(interior, k, 2))
        summed = summed + second_weights[k] * (
            z_padded[:, :, :, RADIUS + k : RADIUS + k + line_depth]
            + z_padded[:, :, :, RADIUS - k : RADIUS - k + line_depth]
        )
        y_slope = y_slope + first_weights[k] * (jnp.roll(padded, -k, 2) - jnp.roll(padded, k, 2))
    cross_term = jnp.zeros_like(interior)
    for k in range(1, RADIUS + 1):
        cross_term = cross_term + first_weights[k] * (
            y_slope[:, RADIUS + k : RADIUS + k + plane_count]
            - y_slope[:, RADIUS - k : RADIUS - k + plane_count]
        )
    return summed + MIXED_WEIGHT * cross_term


def make_kernel(scale, with_prev, home_count, proj_count, block_rows):
    sw = second_table(RADIUS)
    fw = first_table(RADIUS)

    def kernel(shift_ref, lo_ref, v_ref, hi_ref, pot_ref, pick_ref, place_ref, proj_ref, gain_ref, *rest):
        if with_prev:
            prev_ref, out_ref, pad_ref, rows_ref = rest
        else:
            out_ref, pad_ref, rows_ref = rest
        planes, breadth, depth = v_ref.shape
        v = v_ref[...]
        pad_ref[0:RADIUS] = pltpu.roll(lo_ref[...], shift_ref[0], 1)
        pad_ref[RADIUS:RADIUS + planes] = v
        pad_ref[RADIUS + planes:] = pltpu.roll(hi_ref[...], shift_ref[1], 1)

        lines = v.reshape(planes * breadth, depth).astype(jnp.bfloat16)
        picked = jnp.dot(pick_ref[...], lines, preferred_element_type=jnp.float32)

        def one_atom(a, carry):
            base = pl.multiple_of(a * block_rows, block_rows)
            here = picked_ref_load(base)
            acc = jnp.zeros((block_rows, depth), jnp.float32)
            for j in range(proj_count):
                proj = proj_ref[a * proj_count + j].astype(jnp.float32)
                coef = jnp.sum(jnp.sum(proj * here, axis=0, keepdims=True), axis=1, keepdims=True)
                gain = gain_ref[a * proj_count + j]
                scaled = (coef * gain).astype(jnp.bfloat16).astype(jnp.float32)
                acc = acc + proj * scaled
            rows_ref[pl.ds(base, block_rows), :] = acc.astype(jnp.bfloat16)
            return carry

        rows_ref[...] = picked.astype(jnp.bfloat16)

        def picked_ref_load(base):
            return rows_ref[pl.ds(base, block_rows), :].astype(jnp.float32)

        lax.fori_loop(0, home_count, one_atom, 0)
        nonlocal_lines = jnp.dot(place_ref[...], rows_ref[...], preferred_element_type=jnp.float32)
        nonlocal_lines = nonlocal_lines.reshape(planes, breadth, depth)

        lane = lax.broadcasted_iota(jnp.int32, v.shape, 2)
        summed = (3.0 * sw[0]) * v
        for k in range(1, RADIUS + 1):
            xs = pad_ref[RADIUS + k:RADIUS + k + planes] + pad_ref[RADIUS - k:RADIUS - k + planes]
            ys = pltpu.roll(v, breadth - k, 1) + pltpu.roll(v, k, 1)
            zs = (jnp.where(lane < depth - k, pltpu.roll(v, depth - k, 2), 0.0)
                  + jnp.where(lane >= k, pltpu.roll(v, k, 2), 0.0))
            summed = summed + sw[k] * xs + sw[k] * ys + sw[k] * zs
        padded = pad_ref[...]
        slope = fw[1] * (pltpu.roll(padded, breadth - 1, 1) - pltpu.roll(padded, 1, 1))
        for k in range(2, RADIUS + 1):
            slope = slope + fw[k] * (pltpu.roll(padded, breadth - k, 1) - pltpu.roll(padded, k, 1))
        cross = fw[1] * (slope[RADIUS + 1:RADIUS + 1 + planes] - slope[RADIUS - 1:RADIUS - 1 + planes])
        for k in range(2, RADIUS + 1):
            cross = cross + fw[k] * (slope[RADIUS + k:RADIUS + k + planes] - slope[RADIUS - k:RADIUS - k + planes])
        lap = summed + 0.7 * cross
        hv = -0.5 * lap + pot_ref[...] * v + nonlocal_lines
        kv = (hv - 12.0 * v) / 8.0
        if with_prev:
            out_ref[...] = scale * kv - prev_ref[...]
        else:
            out_ref[...] = kv

    return kernel


def apply_op(shifts, lo, v, hi, pot, pick, place, proj, gain, prev=None, scale=1.0):
    planes, breadth, depth = v.shape
    picked_rows = pick.shape[0]
    home_count = proj.shape[0] // 8
    block_rows = picked_rows // home_count
    args = [shifts, lo, v, hi, pot, pick, place, proj, gain] + ([prev] if prev is not None else [])
    vspec = pl.BlockSpec(memory_space=pltpu.VMEM)
    in_specs = [pl.BlockSpec(memory_space=pltpu.SMEM)] + [vspec] * (len(args) - 1)
    return pl.pallas_call(
        make_kernel(scale, prev is not None, home_count, proj.shape[0] // home_count, block_rows),
        out_shape=jax.ShapeDtypeStruct(v.shape, jnp.float32),
        in_specs=in_specs,
        out_specs=vspec,
        scratch_shapes=[
            pltpu.VMEM((planes + 2 * RADIUS, breadth, depth), jnp.float32),
            pltpu.VMEM((picked_rows, depth), jnp.bfloat16),
        ],
    )(*args)


def shards(states_in, potential, projectors, proj_gains, atom_owner, atom_rows, wrap_rows):
    state_count, tile_width, breadth, line_depth = states_in.shape
    n_grid = lax.axis_size("grid")
    n_states = lax.axis_size("states")
    tile_index = lax.axis_index("grid")
    tile_lines = tile_width * breadth
    block_rows = atom_rows.shape[1]
    line_span = block_rows * line_depth
    proj_count = projectors.shape[2]
    home_count = atom_owner.shape[0]
    slot_pairs = projectors.shape[1]
    row_order = jnp.arange(breadth, dtype=jnp.int32)
    unwrap_rows = jnp.sum(
        row_order[None, :] * (wrap_rows[None, :] == row_order[:, None]).astype(jnp.int32), axis=1
    )
    atom_order = jnp.arange(home_count, dtype=jnp.int32)
    same_owner = (atom_owner[:, None] == atom_owner[None, :]) & (
        atom_order[None, :] < atom_order[:, None]
    )
    owner_rank = jnp.sum(same_owner.astype(jnp.int32), axis=1)
    atom_slot = atom_owner * PAIR_CAP + owner_rank
    local_rows = jnp.where(atom_rows >= 0, atom_rows - tile_index * tile_lines, tile_lines)

    gain_lanes = jnp.zeros((1, slot_pairs, proj_count, 128), jnp.bfloat16)
    gain_lanes = gain_lanes.at[..., 0].set(proj_gains)
    packed = jnp.concatenate([projectors, gain_lanes], axis=3)
    pairs = [(o * n_states + t, t * n_states + o) for o in range(n_grid) for t in range(n_states)]
    pairs_far = [
        (o * n_states + t, t * n_states + (o ^ 8)) for o in range(n_grid) for t in range(n_states)
    ]
    packed_far = lax.ppermute(packed, ("grid", "states"), pairs_far)
    packed = lax.ppermute(packed, ("grid", "states"), pairs)
    def flip_y(s):
        return s ^ 8

    def flip_x(s):
        return s ^ 2

    def mirror_x(s):
        x = (s // 2) % 4
        return s + (3 - x - x) * 2

    def flip_core(s):
        return s ^ 1

    exchanges = (flip_x, mirror_x, flip_core)

    def origins(me, done):
        if not done:
            return [me, flip_y(me)]
        return origins(me, done[:-1]) + origins(done[-1](me), done[:-1])

    gathered = jnp.concatenate([packed[0], packed_far[0]], axis=0)
    for exchange in exchanges:
        partner = lax.ppermute(
            gathered, "states", [(s, exchange(s)) for s in range(n_states)]
        )
        gathered = jnp.concatenate([gathered, partner], axis=0)
    block_owner = jnp.stack(origins(lax.axis_index("states"), exchanges))
    owner_block = jnp.argmax(block_owner[None, :] == atom_owner[:, None], axis=1)
    gathered = gathered.reshape(n_states * slot_pairs, proj_count, line_span + 128)
    atom_slot = owner_block * PAIR_CAP + owner_rank
    atom_pack = jnp.take(gathered, atom_slot, axis=0)
    proj_rows = atom_pack[:, :, :line_span].reshape(home_count * proj_count, line_span)
    atom_gain = atom_pack[:, :, line_span].astype(jnp.float32)
    pick = (
        local_rows.reshape(-1)[:, None] == jnp.arange(tile_lines, dtype=jnp.int32)[None, :]
    ).astype(jnp.bfloat16)
    place = pick.T
    proj_in = proj_rows.reshape(home_count * proj_count, breadth, line_depth)
    gain_in = jnp.broadcast_to(
        atom_gain.reshape(home_count * proj_count, 1, 1), (home_count * proj_count, 1, line_depth)
    )
    skew = wrap_rows[0]
    shifts = jnp.stack(
        [
            jnp.where(tile_index == 0, (breadth - skew) % breadth, 0),
            jnp.where(tile_index == n_grid - 1, skew, 0),
            jnp.zeros((), jnp.int32),
            jnp.zeros((), jnp.int32),
        ]
    ).astype(jnp.int32)
    up = [(i, (i + 1) % n_grid) for i in range(n_grid)]
    down = [(j, i) for i, j in up]

    def step(grid_field, prev=None, scale=1.0):
        field = grid_field[0]
        low_rim = lax.ppermute(field[tile_width - RADIUS :], "grid", up)
        high_rim = lax.ppermute(field[:RADIUS], "grid", down)
        out = apply_op(
            shifts, low_rim, field, high_rim, potential, pick, place, proj_in, gain_in, prev, scale
        )
        return out[None]

    first_term = step(states_in)
    second_term = step(first_term, states_in[0], 2.0)
    return step(second_term, first_term[0], 2.0)


def solution(mesh):
    in_specs = (
        P("states", "grid", None, None),
        P("grid", None, None),
        P("grid", "states", None, None),
        P("grid", "states", None),
        P("grid"),
        P("grid", None),
        P(),
    )
    out_specs = P("states", "grid", None, None)
    return jax.shard_map(shards, mesh=mesh, in_specs=in_specs, out_specs=out_specs, check_vma=False)
```

```python
import math

import jax
import jax.numpy as jnp
from jax import lax
from jax.experimental import pallas as pl
from jax.experimental.pallas import tpu as pltpu
from jax.sharding import PartitionSpec as P

RADIUS = 6
PAIR_CAP = 2


MIXED_WEIGHT = 0.7
CENTER = 12.0
HALF_WIDTH = 8.0


def padded_2(shard, sides, width):
    for axis, dim in sides:
        count, length = (lax.axis_size(axis), shard.shape[dim])
        up = [(i, (i + 1) % count) for i in range(count)]
        down = [(j, i) for i, j in up]
        last = lax.slice_in_dim(shard, length - width, length, axis=dim)
        initial = lax.slice_in_dim(shard, 0, width, axis=dim)
        before = lax.ppermute(last, axis, up)
        after = lax.ppermute(initial, axis, down)
        shard = jnp.concatenate([before, shard, after], axis=dim)
    return shard


def second_table(radius):
    weights = [-2.0 * sum((1.0 / (k * k) for k in range(1, radius + 1)))]
    for k in range(1, radius + 1):
        weights.append(
            2.0
            * (-1) ** (k + 1)
            * math.factorial(radius) ** 2
            / (k * k * math.factorial(radius - k) * math.factorial(radius + k))
        )
    return weights


def first_table(radius):
    weights = [0.0]
    for k in range(1, radius + 1):
        weights.append(
            (-1) ** (k + 1)
            * math.factorial(radius) ** 2
            / (k * math.factorial(radius - k) * math.factorial(radius + k))
        )
    return weights


def laplacian(padded, plane_count):
    second_weights = second_table(RADIUS)
    first_weights = first_table(RADIUS)
    interior = padded[:, RADIUS : RADIUS + plane_count]
    line_depth = interior.shape[3]
    z_padded = jnp.pad(interior, ((0, 0), (0, 0), (0, 0), (RADIUS, RADIUS)))
    summed = 3.0 * second_weights[0] * interior
    y_slope = jnp.zeros_like(padded)
    for k in range(1, RADIUS + 1):
        summed = summed + second_weights[k] * (
            padded[:, RADIUS + k : RADIUS + k + plane_count]
            + padded[:, RADIUS - k : RADIUS - k + plane_count]
        )
        summed = summed + second_weights[k] * (jnp.roll(interior, -k, 2) + jnp.roll(interior, k, 2))
        summed = summed + second_weights[k] * (
            z_padded[:, :, :, RADIUS + k : RADIUS + k + line_depth]
            + z_padded[:, :, :, RADIUS - k : RADIUS - k + line_depth]
        )
        y_slope = y_slope + first_weights[k] * (jnp.roll(padded, -k, 2) - jnp.roll(padded, k, 2))
    cross_term = jnp.zeros_like(interior)
    for k in range(1, RADIUS + 1):
        cross_term = cross_term + first_weights[k] * (
            y_slope[:, RADIUS + k : RADIUS + k + plane_count]
            - y_slope[:, RADIUS - k : RADIUS - k + plane_count]
        )
    return summed + MIXED_WEIGHT * cross_term


def make_kernel(scale, with_prev, home_count, proj_count, block_rows):
    sw = second_table(RADIUS)
    fw = first_table(RADIUS)

    def kernel(shift_ref, lo_ref, v_ref, hi_ref, pot_ref, pick_ref, place_ref, proj_ref, gain_ref, *rest):
        if with_prev:
            prev_ref, out_ref, up_ref, down_ref, pad_ref, rows_ref = rest
        else:
            out_ref, up_ref, down_ref, pad_ref, rows_ref = rest
        planes, breadth, depth = v_ref.shape
        v = v_ref[...]
        pad_ref[0:RADIUS] = pltpu.roll(lo_ref[...], shift_ref[0], 1)
        pad_ref[RADIUS:RADIUS + planes] = v
        pad_ref[RADIUS + planes:] = pltpu.roll(hi_ref[...], shift_ref[1], 1)

        lines = v.reshape(planes * breadth, depth).astype(jnp.bfloat16)
        picked = jnp.dot(pick_ref[...], lines, preferred_element_type=jnp.float32)

        def one_atom(a, carry):
            base = pl.multiple_of(a * block_rows, block_rows)
            here = picked_ref_load(base)
            acc = jnp.zeros((block_rows, depth), jnp.float32)
            for j in range(proj_count):
                proj = proj_ref[a * proj_count + j].astype(jnp.float32)
                coef = jnp.sum(jnp.sum(proj * here, axis=0, keepdims=True), axis=1, keepdims=True)
                gain = gain_ref[a * proj_count + j]
                scaled = (coef * gain).astype(jnp.bfloat16).astype(jnp.float32)
                acc = acc + proj * scaled
            rows_ref[pl.ds(base, block_rows), :] = acc.astype(jnp.bfloat16)
            return carry

        rows_ref[...] = picked.astype(jnp.bfloat16)

        def picked_ref_load(base):
            return rows_ref[pl.ds(base, block_rows), :].astype(jnp.float32)

        lax.fori_loop(0, home_count, one_atom, 0)
        nonlocal_lines = jnp.dot(place_ref[...], rows_ref[...], preferred_element_type=jnp.float32)
        nonlocal_lines = nonlocal_lines.reshape(planes, breadth, depth)

        lane = lax.broadcasted_iota(jnp.int32, v.shape, 2)
        summed = (3.0 * sw[0]) * v
        for k in range(1, RADIUS + 1):
            xs = pad_ref[RADIUS + k:RADIUS + k + planes] + pad_ref[RADIUS - k:RADIUS - k + planes]
            ys = pltpu.roll(v, breadth - k, 1) + pltpu.roll(v, k, 1)
            zs = (jnp.where(lane < depth - k, pltpu.roll(v, depth - k, 2), 0.0)
                  + jnp.where(lane >= k, pltpu.roll(v, k, 2), 0.0))
            summed = summed + sw[k] * xs + sw[k] * ys + sw[k] * zs
        padded = pad_ref[...]
        slope = fw[1] * (pltpu.roll(padded, breadth - 1, 1) - pltpu.roll(padded, 1, 1))
        for k in range(2, RADIUS + 1):
            slope = slope + fw[k] * (pltpu.roll(padded, breadth - k, 1) - pltpu.roll(padded, k, 1))
        cross = fw[1] * (slope[RADIUS + 1:RADIUS + 1 + planes] - slope[RADIUS - 1:RADIUS - 1 + planes])
        for k in range(2, RADIUS + 1):
            cross = cross + fw[k] * (slope[RADIUS + k:RADIUS + k + planes] - slope[RADIUS - k:RADIUS - k + planes])
        lap = summed + 0.7 * cross
        hv = -0.5 * lap + pot_ref[...] * v + nonlocal_lines
        kv = (hv - 12.0 * v) / 8.0
        if with_prev:
            result = scale * kv - prev_ref[...]
        else:
            result = kv
        out_ref[...] = result
        up_ref[...] = result[planes - RADIUS:]
        down_ref[...] = result[:RADIUS]

    return kernel


def apply_op(shifts, lo, v, hi, pot, pick, place, proj, gain, prev=None, scale=1.0):
    planes, breadth, depth = v.shape
    picked_rows = pick.shape[0]
    home_count = proj.shape[0] // 8
    block_rows = picked_rows // home_count
    args = [shifts, lo, v, hi, pot, pick, place, proj, gain] + ([prev] if prev is not None else [])
    vspec = pl.BlockSpec(memory_space=pltpu.VMEM)
    in_specs = [pl.BlockSpec(memory_space=pltpu.SMEM)] + [vspec] * (len(args) - 1)
    rim_shape = jax.ShapeDtypeStruct((RADIUS, breadth, depth), jnp.float32)
    return pl.pallas_call(
        make_kernel(scale, prev is not None, home_count, proj.shape[0] // home_count, block_rows),
        out_shape=(jax.ShapeDtypeStruct(v.shape, jnp.float32), rim_shape, rim_shape),
        in_specs=in_specs,
        out_specs=(vspec, vspec, vspec),
        scratch_shapes=[
            pltpu.VMEM((planes + 2 * RADIUS, breadth, depth), jnp.float32),
            pltpu.VMEM((picked_rows, depth), jnp.bfloat16),
        ],
    )(*args)


def shards(states_in, potential, projectors, proj_gains, atom_owner, atom_rows, wrap_rows):
    state_count, tile_width, breadth, line_depth = states_in.shape
    n_grid = lax.axis_size("grid")
    n_states = lax.axis_size("states")
    tile_index = lax.axis_index("grid")
    tile_lines = tile_width * breadth
    block_rows = atom_rows.shape[1]
    line_span = block_rows * line_depth
    proj_count = projectors.shape[2]
    home_count = atom_owner.shape[0]
    slot_pairs = projectors.shape[1]
    row_order = jnp.arange(breadth, dtype=jnp.int32)
    unwrap_rows = jnp.sum(
        row_order[None, :] * (wrap_rows[None, :] == row_order[:, None]).astype(jnp.int32), axis=1
    )
    atom_order = jnp.arange(home_count, dtype=jnp.int32)
    same_owner = (atom_owner[:, None] == atom_owner[None, :]) & (
        atom_order[None, :] < atom_order[:, None]
    )
    owner_rank = jnp.sum(same_owner.astype(jnp.int32), axis=1)
    atom_slot = atom_owner * PAIR_CAP + owner_rank
    local_rows = jnp.where(atom_rows >= 0, atom_rows - tile_index * tile_lines, tile_lines)

    gain_lanes = jnp.zeros((1, slot_pairs, proj_count, 128), jnp.bfloat16)
    gain_lanes = gain_lanes.at[..., 0].set(proj_gains)
    packed = jnp.concatenate([projectors, gain_lanes], axis=3)
    pairs = [(o * n_states + t, t * n_states + o) for o in range(n_grid) for t in range(n_states)]
    packed = lax.ppermute(packed, ("grid", "states"), pairs)
    def flip_y(s):
        return s ^ 8

    def flip_x(s):
        return s ^ 2

    def mirror_x(s):
        x = (s // 2) % 4
        return s + (3 - x - x) * 2

    def flip_core(s):
        return s ^ 1

    exchanges = (flip_y, flip_x, mirror_x, flip_core)

    def origins(me, done):
        if not done:
            return [me]
        return origins(me, done[:-1]) + origins(done[-1](me), done[:-1])

    gathered = packed[0]
    for exchange in exchanges:
        partner = lax.ppermute(
            gathered, "states", [(s, exchange(s)) for s in range(n_states)]
        )
        gathered = jnp.concatenate([gathered, partner], axis=0)
    block_owner = jnp.stack(origins(lax.axis_index("states"), exchanges))
    owner_block = jnp.argmax(block_owner[None, :] == atom_owner[:, None], axis=1)
    gathered = gathered.reshape(n_states * slot_pairs, proj_count, line_span + 128)
    atom_slot = owner_block * PAIR_CAP + owner_rank
    atom_pack = jnp.take(gathered, atom_slot, axis=0)
    proj_rows = atom_pack[:, :, :line_span].reshape(home_count * proj_count, line_span)
    atom_gain = atom_pack[:, :, line_span].astype(jnp.float32)
    pick = (
        local_rows.reshape(-1)[:, None] == jnp.arange(tile_lines, dtype=jnp.int32)[None, :]
    ).astype(jnp.bfloat16)
    place = pick.T
    proj_in = proj_rows.reshape(home_count * proj_count, breadth, line_depth)
    gain_in = jnp.broadcast_to(
        atom_gain.reshape(home_count * proj_count, 1, 1), (home_count * proj_count, 1, line_depth)
    )
    skew = wrap_rows[0]
    shifts = jnp.stack(
        [
            jnp.where(tile_index == 0, (breadth - skew) % breadth, 0),
            jnp.where(tile_index == n_grid - 1, skew, 0),
            jnp.zeros((), jnp.int32),
            jnp.zeros((), jnp.int32),
        ]
    ).astype(jnp.int32)
    up = [(i, (i + 1) % n_grid) for i in range(n_grid)]
    down = [(j, i) for i, j in up]

    def step(field, send_up, send_down, prev=None, scale=1.0):
        low_rim = lax.ppermute(send_up, "grid", up)
        high_rim = lax.ppermute(send_down, "grid", down)
        return apply_op(
            shifts, low_rim, field, high_rim, potential, pick, place, proj_in, gain_in, prev, scale
        )

    field = states_in[0]
    first_term = step(field, field[tile_width - RADIUS :], field[:RADIUS])
    second_term = step(*first_term, field, 2.0)
    filtered = step(*second_term, first_term[0], 2.0)
    return filtered[0][None]


def solution(mesh):
    in_specs = (
        P("states", "grid", None, None),
        P("grid", None, None),
        P("grid", "states", None, None),
        P("grid", "states", None),
        P("grid"),
        P("grid", None),
        P(),
    )
    out_specs = P("states", "grid", None, None)
    return jax.shard_map(shards, mesh=mesh, in_specs=in_specs, out_specs=out_specs, check_vma=False)
```

```python
import math

import jax
import jax.numpy as jnp
from jax import lax
from jax.experimental import pallas as pl
from jax.experimental.pallas import tpu as pltpu
from jax.sharding import PartitionSpec as P

RADIUS = 6
PAIR_CAP = 2


MIXED_WEIGHT = 0.7
CENTER = 12.0
HALF_WIDTH = 8.0


def padded_2(shard, sides, width):
    for axis, dim in sides:
        count, length = (lax.axis_size(axis), shard.shape[dim])
        up = [(i, (i + 1) % count) for i in range(count)]
        down = [(j, i) for i, j in up]
        last = lax.slice_in_dim(shard, length - width, length, axis=dim)
        initial = lax.slice_in_dim(shard, 0, width, axis=dim)
        before = lax.ppermute(last, axis, up)
        after = lax.ppermute(initial, axis, down)
        shard = jnp.concatenate([before, shard, after], axis=dim)
    return shard


def second_table(radius):
    weights = [-2.0 * sum((1.0 / (k * k) for k in range(1, radius + 1)))]
    for k in range(1, radius + 1):
        weights.append(
            2.0
            * (-1) ** (k + 1)
            * math.factorial(radius) ** 2
            / (k * k * math.factorial(radius - k) * math.factorial(radius + k))
        )
    return weights


def first_table(radius):
    weights = [0.0]
    for k in range(1, radius + 1):
        weights.append(
            (-1) ** (k + 1)
            * math.factorial(radius) ** 2
            / (k * math.factorial(radius - k) * math.factorial(radius + k))
        )
    return weights


def laplacian(padded, plane_count):
    second_weights = second_table(RADIUS)
    first_weights = first_table(RADIUS)
    interior = padded[:, RADIUS : RADIUS + plane_count]
    line_depth = interior.shape[3]
    z_padded = jnp.pad(interior, ((0, 0), (0, 0), (0, 0), (RADIUS, RADIUS)))
    summed = 3.0 * second_weights[0] * interior
    y_slope = jnp.zeros_like(padded)
    for k in range(1, RADIUS + 1):
        summed = summed + second_weights[k] * (
            padded[:, RADIUS + k : RADIUS + k + plane_count]
            + padded[:, RADIUS - k : RADIUS - k + plane_count]
        )
        summed = summed + second_weights[k] * (jnp.roll(interior, -k, 2) + jnp.roll(interior, k, 2))
        summed = summed + second_weights[k] * (
            z_padded[:, :, :, RADIUS + k : RADIUS + k + line_depth]
            + z_padded[:, :, :, RADIUS - k : RADIUS - k + line_depth]
        )
        y_slope = y_slope + first_weights[k] * (jnp.roll(padded, -k, 2) - jnp.roll(padded, k, 2))
    cross_term = jnp.zeros_like(interior)
    for k in range(1, RADIUS + 1):
        cross_term = cross_term + first_weights[k] * (
            y_slope[:, RADIUS + k : RADIUS + k + plane_count]
            - y_slope[:, RADIUS - k : RADIUS - k + plane_count]
        )
    return summed + MIXED_WEIGHT * cross_term


def make_kernel(scale, with_prev, home_count, proj_count, block_rows):
    sw = second_table(RADIUS)
    fw = first_table(RADIUS)

    def kernel(shift_ref, lo_ref, v_ref, hi_ref, pot_ref, pick_ref, place_ref, proj_ref, *rest):
        if with_prev:
            prev_ref, out_ref, up_ref, down_ref, pad_ref, rows_ref = rest
        else:
            out_ref, up_ref, down_ref, pad_ref, rows_ref = rest
        planes, breadth, depth = v_ref.shape
        v = v_ref[...]
        pad_ref[0:RADIUS] = pltpu.roll(lo_ref[...], shift_ref[0], 1)
        pad_ref[RADIUS:RADIUS + planes] = v
        pad_ref[RADIUS + planes:] = pltpu.roll(hi_ref[...], shift_ref[1], 1)

        lines = v.reshape(planes * breadth, depth).astype(jnp.bfloat16)
        picked = jnp.dot(pick_ref[...], lines, preferred_element_type=jnp.float32)

        def one_atom(a, carry):
            base = pl.multiple_of(a * block_rows, block_rows)
            here = picked_ref_load(base)
            acc = jnp.zeros((block_rows, depth), jnp.float32)
            for j in range(proj_count):
                block = proj_ref[a * proj_count + j].astype(jnp.float32)
                proj = block[:block_rows]
                coef = jnp.sum(jnp.sum(proj * here, axis=0, keepdims=True), axis=1, keepdims=True)
                gain = block[block_rows:]
                scaled = (coef * gain).astype(jnp.bfloat16).astype(jnp.float32)
                acc = acc + proj * scaled
            rows_ref[pl.ds(base, block_rows), :] = acc.astype(jnp.bfloat16)
            return carry

        rows_ref[...] = picked.astype(jnp.bfloat16)

        def picked_ref_load(base):
            return rows_ref[pl.ds(base, block_rows), :].astype(jnp.float32)

        lax.fori_loop(0, home_count, one_atom, 0)
        nonlocal_lines = jnp.dot(place_ref[...], rows_ref[...], preferred_element_type=jnp.float32)
        nonlocal_lines = nonlocal_lines.reshape(planes, breadth, depth)

        lane = lax.broadcasted_iota(jnp.int32, v.shape, 2)
        summed = (3.0 * sw[0]) * v
        for k in range(1, RADIUS + 1):
            xs = pad_ref[RADIUS + k:RADIUS + k + planes] + pad_ref[RADIUS - k:RADIUS - k + planes]
            ys = pltpu.roll(v, breadth - k, 1) + pltpu.roll(v, k, 1)
            zs = (jnp.where(lane < depth - k, pltpu.roll(v, depth - k, 2), 0.0)
                  + jnp.where(lane >= k, pltpu.roll(v, k, 2), 0.0))
            summed = summed + sw[k] * xs + sw[k] * ys + sw[k] * zs
        padded = pad_ref[...]
        slope = fw[1] * (pltpu.roll(padded, breadth - 1, 1) - pltpu.roll(padded, 1, 1))
        for k in range(2, RADIUS + 1):
            slope = slope + fw[k] * (pltpu.roll(padded, breadth - k, 1) - pltpu.roll(padded, k, 1))
        cross = fw[1] * (slope[RADIUS + 1:RADIUS + 1 + planes] - slope[RADIUS - 1:RADIUS - 1 + planes])
        for k in range(2, RADIUS + 1):
            cross = cross + fw[k] * (slope[RADIUS + k:RADIUS + k + planes] - slope[RADIUS - k:RADIUS - k + planes])
        lap = summed + 0.7 * cross
        hv = -0.5 * lap + pot_ref[...] * v + nonlocal_lines
        kv = (hv - 12.0 * v) / 8.0
        if with_prev:
            result = scale * kv - prev_ref[...]
        else:
            result = kv
        out_ref[...] = result
        up_ref[...] = result[planes - RADIUS:]
        down_ref[...] = result[:RADIUS]

    return kernel


def apply_op(shifts, lo, v, hi, pot, pick, place, proj, prev=None, scale=1.0):
    planes, breadth, depth = v.shape
    picked_rows = pick.shape[0]
    home_count = proj.shape[0] // 8
    block_rows = picked_rows // home_count
    args = [shifts, lo, v, hi, pot, pick, place, proj] + ([prev] if prev is not None else [])
    vspec = pl.BlockSpec(memory_space=pltpu.VMEM)
    in_specs = [pl.BlockSpec(memory_space=pltpu.SMEM)] + [vspec] * (len(args) - 1)
    rim_shape = jax.ShapeDtypeStruct((RADIUS, breadth, depth), jnp.float32)
    return pl.pallas_call(
        make_kernel(scale, prev is not None, home_count, proj.shape[0] // home_count, block_rows),
        out_shape=(jax.ShapeDtypeStruct(v.shape, jnp.float32), rim_shape, rim_shape),
        in_specs=in_specs,
        out_specs=(vspec, vspec, vspec),
        scratch_shapes=[
            pltpu.VMEM((planes + 2 * RADIUS, breadth, depth), jnp.float32),
            pltpu.VMEM((picked_rows, depth), jnp.bfloat16),
        ],
    )(*args)


def shards(states_in, potential, projectors, proj_gains, atom_owner, atom_rows, wrap_rows):
    state_count, tile_width, breadth, line_depth = states_in.shape
    n_grid = lax.axis_size("grid")
    n_states = lax.axis_size("states")
    tile_index = lax.axis_index("grid")
    tile_lines = tile_width * breadth
    block_rows = atom_rows.shape[1]
    line_span = block_rows * line_depth
    proj_count = projectors.shape[2]
    home_count = atom_owner.shape[0]
    slot_pairs = projectors.shape[1]
    row_order = jnp.arange(breadth, dtype=jnp.int32)
    unwrap_rows = jnp.sum(
        row_order[None, :] * (wrap_rows[None, :] == row_order[:, None]).astype(jnp.int32), axis=1
    )
    atom_order = jnp.arange(home_count, dtype=jnp.int32)
    same_owner = (atom_owner[:, None] == atom_owner[None, :]) & (
        atom_order[None, :] < atom_order[:, None]
    )
    owner_rank = jnp.sum(same_owner.astype(jnp.int32), axis=1)
    atom_slot = atom_owner * PAIR_CAP + owner_rank
    local_rows = jnp.where(atom_rows >= 0, atom_rows - tile_index * tile_lines, tile_lines)

    gain_row = jnp.broadcast_to(
        proj_gains[..., None, None], (1, slot_pairs, proj_count, 1, line_depth)
    )
    proj_block = projectors.reshape(1, slot_pairs, proj_count, block_rows, line_depth)
    packed = jnp.concatenate([proj_block, gain_row], axis=3)
    pairs = [(o * n_states + t, t * n_states + o) for o in range(n_grid) for t in range(n_states)]
    packed = lax.ppermute(packed, ("grid", "states"), pairs)
    def flip_y(s):
        return s ^ 8

    def flip_x(s):
        return s ^ 2

    def mirror_x(s):
        x = (s // 2) % 4
        return s + (3 - x - x) * 2

    def flip_core(s):
        return s ^ 1

    exchanges = (flip_y, flip_x, mirror_x, flip_core)

    def origins(me, done):
        if not done:
            return [me]
        return origins(me, done[:-1]) + origins(done[-1](me), done[:-1])

    gathered = packed[0]
    for exchange in exchanges:
        partner = lax.ppermute(
            gathered, "states", [(s, exchange(s)) for s in range(n_states)]
        )
        gathered = jnp.concatenate([gathered, partner], axis=0)
    block_owner = jnp.stack(origins(lax.axis_index("states"), exchanges))
    owner_block = jnp.argmax(block_owner[None, :] == atom_owner[:, None], axis=1)
    gathered = gathered.reshape(n_states * slot_pairs, proj_count, block_rows + 1, line_depth)
    atom_slot = owner_block * PAIR_CAP + owner_rank
    atom_pack = jnp.take(gathered, atom_slot, axis=0)
    pick = (
        local_rows.reshape(-1)[:, None] == jnp.arange(tile_lines, dtype=jnp.int32)[None, :]
    ).astype(jnp.bfloat16)
    place = pick.T
    proj_in = atom_pack.reshape(home_count * proj_count, block_rows + 1, line_depth)
    skew = wrap_rows[0]
    shifts = jnp.stack(
        [
            jnp.where(tile_index == 0, (breadth - skew) % breadth, 0),
            jnp.where(tile_index == n_grid - 1, skew, 0),
            jnp.zeros((), jnp.int32),
            jnp.zeros((), jnp.int32),
        ]
    ).astype(jnp.int32)
    up = [(i, (i + 1) % n_grid) for i in range(n_grid)]
    down = [(j, i) for i, j in up]

    def step(field, send_up, send_down, prev=None, scale=1.0):
        low_rim = lax.ppermute(send_up, "grid", up)
        high_rim = lax.ppermute(send_down, "grid", down)
        return apply_op(
            shifts, low_rim, field, high_rim, potential, pick, place, proj_in, prev, scale
        )

    field = states_in[0]
    first_term = step(field, field[tile_width - RADIUS :], field[:RADIUS])
    second_term = step(*first_term, field, 2.0)
    filtered = step(*second_term, first_term[0], 2.0)
    return filtered[0][None]


def solution(mesh):
    in_specs = (
        P("states", "grid", None, None),
        P("grid", None, None),
        P("grid", "states", None, None),
        P("grid", "states", None),
        P("grid"),
        P("grid", None),
        P(),
    )
    out_specs = P("states", "grid", None, None)
    return jax.shard_map(shards, mesh=mesh, in_specs=in_specs, out_specs=out_specs, check_vma=False)
```

```python
import math

import jax
import jax.numpy as jnp
from jax import lax
from jax.experimental import pallas as pl
from jax.experimental.pallas import tpu as pltpu
from jax.sharding import PartitionSpec as P

RADIUS = 6
PAIR_CAP = 2


MIXED_WEIGHT = 0.7
CENTER = 12.0
HALF_WIDTH = 8.0


def padded_2(shard, sides, width):
    for axis, dim in sides:
        count, length = (lax.axis_size(axis), shard.shape[dim])
        up = [(i, (i + 1) % count) for i in range(count)]
        down = [(j, i) for i, j in up]
        last = lax.slice_in_dim(shard, length - width, length, axis=dim)
        initial = lax.slice_in_dim(shard, 0, width, axis=dim)
        before = lax.ppermute(last, axis, up)
        after = lax.ppermute(initial, axis, down)
        shard = jnp.concatenate([before, shard, after], axis=dim)
    return shard


def second_table(radius):
    weights = [-2.0 * sum((1.0 / (k * k) for k in range(1, radius + 1)))]
    for k in range(1, radius + 1):
        weights.append(
            2.0
            * (-1) ** (k + 1)
            * math.factorial(radius) ** 2
            / (k * k * math.factorial(radius - k) * math.factorial(radius + k))
        )
    return weights


def first_table(radius):
    weights = [0.0]
    for k in range(1, radius + 1):
        weights.append(
            (-1) ** (k + 1)
            * math.factorial(radius) ** 2
            / (k * math.factorial(radius - k) * math.factorial(radius + k))
        )
    return weights


def laplacian(padded, plane_count):
    second_weights = second_table(RADIUS)
    first_weights = first_table(RADIUS)
    interior = padded[:, RADIUS : RADIUS + plane_count]
    line_depth = interior.shape[3]
    z_padded = jnp.pad(interior, ((0, 0), (0, 0), (0, 0), (RADIUS, RADIUS)))
    summed = 3.0 * second_weights[0] * interior
    y_slope = jnp.zeros_like(padded)
    for k in range(1, RADIUS + 1):
        summed = summed + second_weights[k] * (
            padded[:, RADIUS + k : RADIUS + k + plane_count]
            + padded[:, RADIUS - k : RADIUS - k + plane_count]
        )
        summed = summed + second_weights[k] * (jnp.roll(interior, -k, 2) + jnp.roll(interior, k, 2))
        summed = summed + second_weights[k] * (
            z_padded[:, :, :, RADIUS + k : RADIUS + k + line_depth]
            + z_padded[:, :, :, RADIUS - k : RADIUS - k + line_depth]
        )
        y_slope = y_slope + first_weights[k] * (jnp.roll(padded, -k, 2) - jnp.roll(padded, k, 2))
    cross_term = jnp.zeros_like(interior)
    for k in range(1, RADIUS + 1):
        cross_term = cross_term + first_weights[k] * (
            y_slope[:, RADIUS + k : RADIUS + k + plane_count]
            - y_slope[:, RADIUS - k : RADIUS - k + plane_count]
        )
    return summed + MIXED_WEIGHT * cross_term


def make_kernel(scale, with_prev, home_count, proj_count, block_rows):
    sw = second_table(RADIUS)
    fw = first_table(RADIUS)

    def kernel(shift_ref, lo_ref, v_ref, hi_ref, pot_ref, pick_ref, place_ref, proj_ref, gain_ref, *rest):
        if with_prev:
            prev_ref, out_ref, up_ref, down_ref, pad_ref, rows_ref = rest
        else:
            out_ref, up_ref, down_ref, pad_ref, rows_ref = rest
        planes, breadth, depth = v_ref.shape
        v = v_ref[...]
        pad_ref[0:RADIUS] = pltpu.roll(lo_ref[...], shift_ref[0], 1)
        pad_ref[RADIUS:RADIUS + planes] = v
        pad_ref[RADIUS + planes:] = pltpu.roll(hi_ref[...], shift_ref[1], 1)

        lines = v.reshape(planes * breadth, depth).astype(jnp.bfloat16)
        picked = jnp.dot(pick_ref[...], lines, preferred_element_type=jnp.float32)

        def one_atom(a, carry):
            base = pl.multiple_of(a * block_rows, block_rows)
            here = picked_ref_load(base)
            acc = jnp.zeros((block_rows, depth), jnp.float32)
            for j in range(proj_count):
                proj = proj_ref[a * proj_count + j].astype(jnp.float32)
                coef = jnp.sum(jnp.sum(proj * here, axis=0, keepdims=True), axis=1, keepdims=True)
                gain = gain_ref[a * proj_count + j]
                scaled = (coef * gain).astype(jnp.bfloat16).astype(jnp.float32)
                acc = acc + proj * scaled
            rows_ref[pl.ds(base, block_rows), :] = acc.astype(jnp.bfloat16)
            return carry

        rows_ref[...] = picked.astype(jnp.bfloat16)

        def picked_ref_load(base):
            return rows_ref[pl.ds(base, block_rows), :].astype(jnp.float32)

        lax.fori_loop(0, home_count, one_atom, 0, unroll=True)
        nonlocal_lines = jnp.dot(place_ref[...], rows_ref[...], preferred_element_type=jnp.float32)
        nonlocal_lines = nonlocal_lines.reshape(planes, breadth, depth)

        lane = lax.broadcasted_iota(jnp.int32, v.shape, 2)
        summed = (3.0 * sw[0]) * v
        for k in range(1, RADIUS + 1):
            xs = pad_ref[RADIUS + k:RADIUS + k + planes] + pad_ref[RADIUS - k:RADIUS - k + planes]
            ys = pltpu.roll(v, breadth - k, 1) + pltpu.roll(v, k, 1)
            zs = (jnp.where(lane < depth - k, pltpu.roll(v, depth - k, 2), 0.0)
                  + jnp.where(lane >= k, pltpu.roll(v, k, 2), 0.0))
            summed = summed + sw[k] * xs + sw[k] * ys + sw[k] * zs
        padded = pad_ref[...]
        slope = fw[1] * (pltpu.roll(padded, breadth - 1, 1) - pltpu.roll(padded, 1, 1))
        for k in range(2, RADIUS + 1):
            slope = slope + fw[k] * (pltpu.roll(padded, breadth - k, 1) - pltpu.roll(padded, k, 1))
        cross = fw[1] * (slope[RADIUS + 1:RADIUS + 1 + planes] - slope[RADIUS - 1:RADIUS - 1 + planes])
        for k in range(2, RADIUS + 1):
            cross = cross + fw[k] * (slope[RADIUS + k:RADIUS + k + planes] - slope[RADIUS - k:RADIUS - k + planes])
        lap = summed + 0.7 * cross
        hv = -0.5 * lap + pot_ref[...] * v + nonlocal_lines
        kv = (hv - 12.0 * v) / 8.0
        if with_prev:
            result = scale * kv - prev_ref[...]
        else:
            result = kv
        out_ref[...] = result
        up_ref[...] = result[planes - RADIUS:]
        down_ref[...] = result[:RADIUS]

    return kernel


def apply_op(shifts, lo, v, hi, pot, pick, place, proj, gain, prev=None, scale=1.0):
    planes, breadth, depth = v.shape
    picked_rows = pick.shape[0]
    home_count = proj.shape[0] // 8
    block_rows = picked_rows // home_count
    args = [shifts, lo, v, hi, pot, pick, place, proj, gain] + ([prev] if prev is not None else [])
    vspec = pl.BlockSpec(memory_space=pltpu.VMEM)
    in_specs = [pl.BlockSpec(memory_space=pltpu.SMEM)] + [vspec] * (len(args) - 1)
    rim_shape = jax.ShapeDtypeStruct((RADIUS, breadth, depth), jnp.float32)
    return pl.pallas_call(
        make_kernel(scale, prev is not None, home_count, proj.shape[0] // home_count, block_rows),
        out_shape=(jax.ShapeDtypeStruct(v.shape, jnp.float32), rim_shape, rim_shape),
        in_specs=in_specs,
        out_specs=(vspec, vspec, vspec),
        scratch_shapes=[
            pltpu.VMEM((planes + 2 * RADIUS, breadth, depth), jnp.float32),
            pltpu.VMEM((picked_rows, depth), jnp.bfloat16),
        ],
    )(*args)


def shards(states_in, potential, projectors, proj_gains, atom_owner, atom_rows, wrap_rows):
    state_count, tile_width, breadth, line_depth = states_in.shape
    n_grid = lax.axis_size("grid")
    n_states = lax.axis_size("states")
    tile_index = lax.axis_index("grid")
    tile_lines = tile_width * breadth
    block_rows = atom_rows.shape[1]
    line_span = block_rows * line_depth
    proj_count = projectors.shape[2]
    home_count = atom_owner.shape[0]
    slot_pairs = projectors.shape[1]
    row_order = jnp.arange(breadth, dtype=jnp.int32)
    unwrap_rows = jnp.sum(
        row_order[None, :] * (wrap_rows[None, :] == row_order[:, None]).astype(jnp.int32), axis=1
    )
    atom_order = jnp.arange(home_count, dtype=jnp.int32)
    same_owner = (atom_owner[:, None] == atom_owner[None, :]) & (
        atom_order[None, :] < atom_order[:, None]
    )
    owner_rank = jnp.sum(same_owner.astype(jnp.int32), axis=1)
    atom_slot = atom_owner * PAIR_CAP + owner_rank
    local_rows = jnp.where(atom_rows >= 0, atom_rows - tile_index * tile_lines, tile_lines)

    gain_lanes = jnp.zeros((1, slot_pairs, proj_count, 128), jnp.bfloat16)
    gain_lanes = gain_lanes.at[..., 0].set(proj_gains)
    packed = jnp.concatenate([projectors, gain_lanes], axis=3)
    pairs = [(o * n_states + t, t * n_states + o) for o in range(n_grid) for t in range(n_states)]
    packed = lax.ppermute(packed, ("grid", "states"), pairs)
    def flip_y(s):
        return s ^ 8

    def flip_x(s):
        return s ^ 2

    def mirror_x(s):
        x = (s // 2) % 4
        return s + (3 - x - x) * 2

    def flip_core(s):
        return s ^ 1

    exchanges = (flip_y, flip_x, mirror_x, flip_core)

    def origins(me, done):
        if not done:
            return [me]
        return origins(me, done[:-1]) + origins(done[-1](me), done[:-1])

    gathered = packed[0]
    for exchange in exchanges:
        partner = lax.ppermute(
            gathered, "states", [(s, exchange(s)) for s in range(n_states)]
        )
        gathered = jnp.concatenate([gathered, partner], axis=0)
    block_owner = jnp.stack(origins(lax.axis_index("states"), exchanges))
    owner_block = jnp.argmax(block_owner[None, :] == atom_owner[:, None], axis=1)
    gathered = gathered.reshape(n_states * slot_pairs, proj_count, line_span + 128)
    atom_slot = owner_block * PAIR_CAP + owner_rank
    atom_pack = jnp.take(gathered, atom_slot, axis=0)
    proj_rows = atom_pack[:, :, :line_span].reshape(home_count * proj_count, line_span)
    atom_gain = atom_pack[:, :, line_span].astype(jnp.float32)
    pick = (
        local_rows.reshape(-1)[:, None] == jnp.arange(tile_lines, dtype=jnp.int32)[None, :]
    ).astype(jnp.bfloat16)
    place = pick.T
    proj_in = proj_rows.reshape(home_count * proj_count, breadth, line_depth)
    gain_in = jnp.broadcast_to(
        atom_gain.reshape(home_count * proj_count, 1, 1), (home_count * proj_count, 1, line_depth)
    )
    skew = wrap_rows[0]
    shifts = jnp.stack(
        [
            jnp.where(tile_index == 0, (breadth - skew) % breadth, 0),
            jnp.where(tile_index == n_grid - 1, skew, 0),
            jnp.zeros((), jnp.int32),
            jnp.zeros((), jnp.int32),
        ]
    ).astype(jnp.int32)
    up = [(i, (i + 1) % n_grid) for i in range(n_grid)]
    down = [(j, i) for i, j in up]

    def step(field, send_up, send_down, prev=None, scale=1.0):
        low_rim = lax.ppermute(send_up, "grid", up)
        high_rim = lax.ppermute(send_down, "grid", down)
        return apply_op(
            shifts, low_rim, field, high_rim, potential, pick, place, proj_in, gain_in, prev, scale
        )

    field = states_in[0]
    first_term = step(field, field[tile_width - RADIUS :], field[:RADIUS])
    second_term = step(*first_term, field, 2.0)
    filtered = step(*second_term, first_term[0], 2.0)
    return filtered[0][None]


def solution(mesh):
    in_specs = (
        P("states", "grid", None, None),
        P("grid", None, None),
        P("grid", "states", None, None),
        P("grid", "states", None),
        P("grid"),
        P("grid", None),
        P(),
    )
    out_specs = P("states", "grid", None, None)
    return jax.shard_map(shards, mesh=mesh, in_specs=in_specs, out_specs=out_specs, check_vma=False)
```

```python
import math

import jax
import jax.numpy as jnp
from jax import lax
from jax.experimental import pallas as pl
from jax.experimental.pallas import tpu as pltpu
from jax.sharding import PartitionSpec as P

RADIUS = 6
PAIR_CAP = 2


MIXED_WEIGHT = 0.7
CENTER = 12.0
HALF_WIDTH = 8.0


def padded_2(shard, sides, width):
    for axis, dim in sides:
        count, length = (lax.axis_size(axis), shard.shape[dim])
        up = [(i, (i + 1) % count) for i in range(count)]
        down = [(j, i) for i, j in up]
        last = lax.slice_in_dim(shard, length - width, length, axis=dim)
        initial = lax.slice_in_dim(shard, 0, width, axis=dim)
        before = lax.ppermute(last, axis, up)
        after = lax.ppermute(initial, axis, down)
        shard = jnp.concatenate([before, shard, after], axis=dim)
    return shard


def second_table(radius):
    weights = [-2.0 * sum((1.0 / (k * k) for k in range(1, radius + 1)))]
    for k in range(1, radius + 1):
        weights.append(
            2.0
            * (-1) ** (k + 1)
            * math.factorial(radius) ** 2
            / (k * k * math.factorial(radius - k) * math.factorial(radius + k))
        )
    return weights


def first_table(radius):
    weights = [0.0]
    for k in range(1, radius + 1):
        weights.append(
            (-1) ** (k + 1)
            * math.factorial(radius) ** 2
            / (k * math.factorial(radius - k) * math.factorial(radius + k))
        )
    return weights


def laplacian(padded, plane_count):
    second_weights = second_table(RADIUS)
    first_weights = first_table(RADIUS)
    interior = padded[:, RADIUS : RADIUS + plane_count]
    line_depth = interior.shape[3]
    z_padded = jnp.pad(interior, ((0, 0), (0, 0), (0, 0), (RADIUS, RADIUS)))
    summed = 3.0 * second_weights[0] * interior
    y_slope = jnp.zeros_like(padded)
    for k in range(1, RADIUS + 1):
        summed = summed + second_weights[k] * (
            padded[:, RADIUS + k : RADIUS + k + plane_count]
            + padded[:, RADIUS - k : RADIUS - k + plane_count]
        )
        summed = summed + second_weights[k] * (jnp.roll(interior, -k, 2) + jnp.roll(interior, k, 2))
        summed = summed + second_weights[k] * (
            z_padded[:, :, :, RADIUS + k : RADIUS + k + line_depth]
            + z_padded[:, :, :, RADIUS - k : RADIUS - k + line_depth]
        )
        y_slope = y_slope + first_weights[k] * (jnp.roll(padded, -k, 2) - jnp.roll(padded, k, 2))
    cross_term = jnp.zeros_like(interior)
    for k in range(1, RADIUS + 1):
        cross_term = cross_term + first_weights[k] * (
            y_slope[:, RADIUS + k : RADIUS + k + plane_count]
            - y_slope[:, RADIUS - k : RADIUS - k + plane_count]
        )
    return summed + MIXED_WEIGHT * cross_term


def make_kernel(scale, with_prev, home_count, proj_count, block_rows):
    sw = second_table(RADIUS)
    fw = first_table(RADIUS)

    def kernel(shift_ref, lo_ref, v_ref, hi_ref, pot_ref, pick_ref, place_ref, proj_ref, gain_ref, *rest):
        if with_prev:
            prev_ref, out_ref, up_ref, down_ref, pad_ref, rows_ref = rest
        else:
            out_ref, up_ref, down_ref, pad_ref, rows_ref = rest
        planes, breadth, depth = v_ref.shape
        v = v_ref[...]
        pad_ref[0:RADIUS] = pltpu.roll(lo_ref[...], shift_ref[0], 1)
        pad_ref[RADIUS:RADIUS + planes] = v
        pad_ref[RADIUS + planes:] = pltpu.roll(hi_ref[...], shift_ref[1], 1)

        lines = v.reshape(planes * breadth, depth).astype(jnp.bfloat16)
        picked = jnp.dot(pick_ref[...], lines, preferred_element_type=jnp.float32)

        def one_atom(a, carry):
            base = pl.multiple_of(a * block_rows, block_rows)
            here = picked_ref_load(base)
            acc = jnp.zeros((block_rows, depth), jnp.float32)
            for j in range(proj_count):
                proj = proj_ref[a * proj_count + j].astype(jnp.float32)
                coef = jnp.sum(jnp.sum(proj * here, axis=0, keepdims=True), axis=1, keepdims=True)
                gain = gain_ref[a * proj_count + j]
                scaled = (coef * gain).astype(jnp.bfloat16).astype(jnp.float32)
                acc = acc + proj * scaled
            rows_ref[pl.ds(base, block_rows), :] = acc.astype(jnp.bfloat16)
            return carry

        rows_ref[...] = picked.astype(jnp.bfloat16)

        def picked_ref_load(base):
            return rows_ref[pl.ds(base, block_rows), :].astype(jnp.float32)

        lax.fori_loop(0, home_count, one_atom, 0, unroll=True)
        nonlocal_lines = jnp.dot(place_ref[...], rows_ref[...], preferred_element_type=jnp.float32)
        nonlocal_lines = nonlocal_lines.reshape(planes, breadth, depth)

        lane = lax.broadcasted_iota(jnp.int32, v.shape, 2)
        summed = (3.0 * sw[0]) * v
        for k in range(1, RADIUS + 1):
            xs = pad_ref[RADIUS + k:RADIUS + k + planes] + pad_ref[RADIUS - k:RADIUS - k + planes]
            ys = pltpu.roll(v, breadth - k, 1) + pltpu.roll(v, k, 1)
            zs = (jnp.where(lane < depth - k, pltpu.roll(v, depth - k, 2), 0.0)
                  + jnp.where(lane >= k, pltpu.roll(v, k, 2), 0.0))
            summed = summed + sw[k] * xs + sw[k] * ys + sw[k] * zs
        x_slope = fw[1] * (pad_ref[RADIUS + 1:RADIUS + 1 + planes] - pad_ref[RADIUS - 1:RADIUS - 1 + planes])
        for k in range(2, RADIUS + 1):
            x_slope = x_slope + fw[k] * (
                pad_ref[RADIUS + k:RADIUS + k + planes] - pad_ref[RADIUS - k:RADIUS - k + planes]
            )
        cross = fw[1] * (pltpu.roll(x_slope, breadth - 1, 1) - pltpu.roll(x_slope, 1, 1))
        for k in range(2, RADIUS + 1):
            cross = cross + fw[k] * (pltpu.roll(x_slope, breadth - k, 1) - pltpu.roll(x_slope, k, 1))
        lap = summed + 0.7 * cross
        hv = -0.5 * lap + pot_ref[...] * v + nonlocal_lines
        kv = (hv - 12.0 * v) / 8.0
        if with_prev:
            result = scale * kv - prev_ref[...]
        else:
            result = kv
        out_ref[...] = result
        up_ref[...] = result[planes - RADIUS:]
        down_ref[...] = result[:RADIUS]

    return kernel


def apply_op(shifts, lo, v, hi, pot, pick, place, proj, gain, prev=None, scale=1.0):
    planes, breadth, depth = v.shape
    picked_rows = pick.shape[0]
    home_count = proj.shape[0] // 8
    block_rows = picked_rows // home_count
    args = [shifts, lo, v, hi, pot, pick, place, proj, gain] + ([prev] if prev is not None else [])
    vspec = pl.BlockSpec(memory_space=pltpu.VMEM)
    in_specs = [pl.BlockSpec(memory_space=pltpu.SMEM)] + [vspec] * (len(args) - 1)
    rim_shape = jax.ShapeDtypeStruct((RADIUS, breadth, depth), jnp.float32)
    return pl.pallas_call(
        make_kernel(scale, prev is not None, home_count, proj.shape[0] // home_count, block_rows),
        out_shape=(jax.ShapeDtypeStruct(v.shape, jnp.float32), rim_shape, rim_shape),
        in_specs=in_specs,
        out_specs=(vspec, vspec, vspec),
        scratch_shapes=[
            pltpu.VMEM((planes + 2 * RADIUS, breadth, depth), jnp.float32),
            pltpu.VMEM((picked_rows, depth), jnp.bfloat16),
        ],
    )(*args)


def shards(states_in, potential, projectors, proj_gains, atom_owner, atom_rows, wrap_rows):
    state_count, tile_width, breadth, line_depth = states_in.shape
    n_grid = lax.axis_size("grid")
    n_states = lax.axis_size("states")
    tile_index = lax.axis_index("grid")
    tile_lines = tile_width * breadth
    block_rows = atom_rows.shape[1]
    line_span = block_rows * line_depth
    proj_count = projectors.shape[2]
    home_count = atom_owner.shape[0]
    slot_pairs = projectors.shape[1]
    row_order = jnp.arange(breadth, dtype=jnp.int32)
    unwrap_rows = jnp.sum(
        row_order[None, :] * (wrap_rows[None, :] == row_order[:, None]).astype(jnp.int32), axis=1
    )
    atom_order = jnp.arange(home_count, dtype=jnp.int32)
    same_owner = (atom_owner[:, None] == atom_owner[None, :]) & (
        atom_order[None, :] < atom_order[:, None]
    )
    owner_rank = jnp.sum(same_owner.astype(jnp.int32), axis=1)
    atom_slot = atom_owner * PAIR_CAP + owner_rank
    local_rows = jnp.where(atom_rows >= 0, atom_rows - tile_index * tile_lines, tile_lines)

    gain_lanes = jnp.zeros((1, slot_pairs, proj_count, 128), jnp.bfloat16)
    gain_lanes = gain_lanes.at[..., 0].set(proj_gains)
    packed = jnp.concatenate([projectors, gain_lanes], axis=3)
    pairs = [(o * n_states + t, t * n_states + o) for o in range(n_grid) for t in range(n_states)]
    packed = lax.ppermute(packed, ("grid", "states"), pairs)
    def flip_y(s):
        return s ^ 8

    def flip_x(s):
        return s ^ 2

    def mirror_x(s):
        x = (s // 2) % 4
        return s + (3 - x - x) * 2

    def flip_core(s):
        return s ^ 1

    exchanges = (flip_y, flip_x, mirror_x, flip_core)

    def origins(me, done):
        if not done:
            return [me]
        return origins(me, done[:-1]) + origins(done[-1](me), done[:-1])

    gathered = packed[0]
    for exchange in exchanges:
        partner = lax.ppermute(
            gathered, "states", [(s, exchange(s)) for s in range(n_states)]
        )
        gathered = jnp.concatenate([gathered, partner], axis=0)
    block_owner = jnp.stack(origins(lax.axis_index("states"), exchanges))
    owner_block = jnp.argmax(block_owner[None, :] == atom_owner[:, None], axis=1)
    gathered = gathered.reshape(n_states * slot_pairs, proj_count, line_span + 128)
    atom_slot = owner_block * PAIR_CAP + owner_rank
    atom_pack = jnp.take(gathered, atom_slot, axis=0)
    proj_rows = atom_pack[:, :, :line_span].reshape(home_count * proj_count, line_span)
    atom_gain = atom_pack[:, :, line_span].astype(jnp.float32)
    pick = (
        local_rows.reshape(-1)[:, None] == jnp.arange(tile_lines, dtype=jnp.int32)[None, :]
    ).astype(jnp.bfloat16)
    place = pick.T
    proj_in = proj_rows.reshape(home_count * proj_count, breadth, line_depth)
    gain_in = jnp.broadcast_to(
        atom_gain.reshape(home_count * proj_count, 1, 1), (home_count * proj_count, 1, line_depth)
    )
    skew = wrap_rows[0]
    shifts = jnp.stack(
        [
            jnp.where(tile_index == 0, (breadth - skew) % breadth, 0),
            jnp.where(tile_index == n_grid - 1, skew, 0),
            jnp.zeros((), jnp.int32),
            jnp.zeros((), jnp.int32),
        ]
    ).astype(jnp.int32)
    up = [(i, (i + 1) % n_grid) for i in range(n_grid)]
    down = [(j, i) for i, j in up]

    def step(field, send_up, send_down, prev=None, scale=1.0):
        low_rim = lax.ppermute(send_up, "grid", up)
        high_rim = lax.ppermute(send_down, "grid", down)
        return apply_op(
            shifts, low_rim, field, high_rim, potential, pick, place, proj_in, gain_in, prev, scale
        )

    field = states_in[0]
    first_term = step(field, field[tile_width - RADIUS :], field[:RADIUS])
    second_term = step(*first_term, field, 2.0)
    filtered = step(*second_term, first_term[0], 2.0)
    return filtered[0][None]


def solution(mesh):
    in_specs = (
        P("states", "grid", None, None),
        P("grid", None, None),
        P("grid", "states", None, None),
        P("grid", "states", None),
        P("grid"),
        P("grid", None),
        P(),
    )
    out_specs = P("states", "grid", None, None)
    return jax.shard_map(shards, mesh=mesh, in_specs=in_specs, out_specs=out_specs, check_vma=False)
```

```python
import math

import jax
import jax.numpy as jnp
from jax import lax
from jax.experimental import pallas as pl
from jax.experimental.pallas import tpu as pltpu
from jax.sharding import PartitionSpec as P

RADIUS = 6
PAIR_CAP = 2


MIXED_WEIGHT = 0.7
CENTER = 12.0
HALF_WIDTH = 8.0


def padded_2(shard, sides, width):
    for axis, dim in sides:
        count, length = (lax.axis_size(axis), shard.shape[dim])
        up = [(i, (i + 1) % count) for i in range(count)]
        down = [(j, i) for i, j in up]
        last = lax.slice_in_dim(shard, length - width, length, axis=dim)
        initial = lax.slice_in_dim(shard, 0, width, axis=dim)
        before = lax.ppermute(last, axis, up)
        after = lax.ppermute(initial, axis, down)
        shard = jnp.concatenate([before, shard, after], axis=dim)
    return shard


def second_table(radius):
    weights = [-2.0 * sum((1.0 / (k * k) for k in range(1, radius + 1)))]
    for k in range(1, radius + 1):
        weights.append(
            2.0
            * (-1) ** (k + 1)
            * math.factorial(radius) ** 2
            / (k * k * math.factorial(radius - k) * math.factorial(radius + k))
        )
    return weights


def first_table(radius):
    weights = [0.0]
    for k in range(1, radius + 1):
        weights.append(
            (-1) ** (k + 1)
            * math.factorial(radius) ** 2
            / (k * math.factorial(radius - k) * math.factorial(radius + k))
        )
    return weights


def laplacian(padded, plane_count):
    second_weights = second_table(RADIUS)
    first_weights = first_table(RADIUS)
    interior = padded[:, RADIUS : RADIUS + plane_count]
    line_depth = interior.shape[3]
    z_padded = jnp.pad(interior, ((0, 0), (0, 0), (0, 0), (RADIUS, RADIUS)))
    summed = 3.0 * second_weights[0] * interior
    y_slope = jnp.zeros_like(padded)
    for k in range(1, RADIUS + 1):
        summed = summed + second_weights[k] * (
            padded[:, RADIUS + k : RADIUS + k + plane_count]
            + padded[:, RADIUS - k : RADIUS - k + plane_count]
        )
        summed = summed + second_weights[k] * (jnp.roll(interior, -k, 2) + jnp.roll(interior, k, 2))
        summed = summed + second_weights[k] * (
            z_padded[:, :, :, RADIUS + k : RADIUS + k + line_depth]
            + z_padded[:, :, :, RADIUS - k : RADIUS - k + line_depth]
        )
        y_slope = y_slope + first_weights[k] * (jnp.roll(padded, -k, 2) - jnp.roll(padded, k, 2))
    cross_term = jnp.zeros_like(interior)
    for k in range(1, RADIUS + 1):
        cross_term = cross_term + first_weights[k] * (
            y_slope[:, RADIUS + k : RADIUS + k + plane_count]
            - y_slope[:, RADIUS - k : RADIUS - k + plane_count]
        )
    return summed + MIXED_WEIGHT * cross_term


def make_kernel(scale, with_prev, home_count, proj_count, block_rows, with_nonlocal=True):
    sw = second_table(RADIUS)
    fw = first_table(RADIUS)

    def nonlocal_of(v, pick_ref, place_ref, proj_ref, gain_ref, rows_ref):
        planes, breadth, depth = v.shape
        lines = v.reshape(planes * breadth, depth).astype(jnp.bfloat16)
        picked = jnp.dot(pick_ref[...], lines, preferred_element_type=jnp.float32)
        rows_ref[...] = picked.astype(jnp.bfloat16)

        def one_atom(a, carry):
            base = pl.multiple_of(a * block_rows, block_rows)
            here = rows_ref[pl.ds(base, block_rows), :].astype(jnp.float32)
            acc = jnp.zeros((block_rows, depth), jnp.float32)
            for j in range(proj_count):
                proj = proj_ref[a * proj_count + j].astype(jnp.float32)
                coef = jnp.sum(jnp.sum(proj * here, axis=0, keepdims=True), axis=1, keepdims=True)
                gain = gain_ref[a * proj_count + j]
                scaled = (coef * gain).astype(jnp.bfloat16).astype(jnp.float32)
                acc = acc + proj * scaled
            rows_ref[pl.ds(base, block_rows), :] = acc.astype(jnp.bfloat16)
            return carry

        lax.fori_loop(0, home_count, one_atom, 0, unroll=True)
        placed = jnp.dot(place_ref[...], rows_ref[...], preferred_element_type=jnp.float32)
        return placed.reshape(planes, breadth, depth)

    if not with_nonlocal and with_prev is None:
        def nonlocal_kernel(v_ref, base_ref, pick_ref, place_ref, proj_ref, gain_ref, out_ref, up_ref, down_ref, rows_ref):
            planes = v_ref.shape[0]
            nonlocal_lines = nonlocal_of(v_ref[...], pick_ref, place_ref, proj_ref, gain_ref, rows_ref)
            result = base_ref[...] + nonlocal_lines / 8.0
            out_ref[...] = result
            up_ref[...] = result[planes - RADIUS:]
            down_ref[...] = result[:RADIUS]

        return nonlocal_kernel

    def kernel(shift_ref, lo_ref, v_ref, hi_ref, pot_ref, *rest):
        if with_nonlocal:
            pick_ref, place_ref, proj_ref, gain_ref = rest[:4]
            rest = rest[4:]
        if with_prev:
            prev_ref, out_ref, up_ref, down_ref, pad_ref, rows_ref = rest
        else:
            out_ref, up_ref, down_ref, pad_ref, rows_ref = rest
        planes, breadth, depth = v_ref.shape
        v = v_ref[...]
        pad_ref[0:RADIUS] = pltpu.roll(lo_ref[...], shift_ref[0], 1)
        pad_ref[RADIUS:RADIUS + planes] = v
        pad_ref[RADIUS + planes:] = pltpu.roll(hi_ref[...], shift_ref[1], 1)

        if with_nonlocal:
            nonlocal_lines = nonlocal_of(v, pick_ref, place_ref, proj_ref, gain_ref, rows_ref)
        else:
            nonlocal_lines = 0.0

        lane = lax.broadcasted_iota(jnp.int32, v.shape, 2)
        summed = (3.0 * sw[0]) * v
        for k in range(1, RADIUS + 1):
            xs = pad_ref[RADIUS + k:RADIUS + k + planes] + pad_ref[RADIUS - k:RADIUS - k + planes]
            ys = pltpu.roll(v, breadth - k, 1) + pltpu.roll(v, k, 1)
            zs = (jnp.where(lane < depth - k, pltpu.roll(v, depth - k, 2), 0.0)
                  + jnp.where(lane >= k, pltpu.roll(v, k, 2), 0.0))
            summed = summed + sw[k] * xs + sw[k] * ys + sw[k] * zs
        padded = pad_ref[...]
        slope = fw[1] * (pltpu.roll(padded, breadth - 1, 1) - pltpu.roll(padded, 1, 1))
        for k in range(2, RADIUS + 1):
            slope = slope + fw[k] * (pltpu.roll(padded, breadth - k, 1) - pltpu.roll(padded, k, 1))
        cross = fw[1] * (slope[RADIUS + 1:RADIUS + 1 + planes] - slope[RADIUS - 1:RADIUS - 1 + planes])
        for k in range(2, RADIUS + 1):
            cross = cross + fw[k] * (slope[RADIUS + k:RADIUS + k + planes] - slope[RADIUS - k:RADIUS - k + planes])
        lap = summed + 0.7 * cross
        hv = -0.5 * lap + pot_ref[...] * v + nonlocal_lines
        kv = (hv - 12.0 * v) / 8.0
        if with_prev:
            result = scale * kv - prev_ref[...]
        else:
            result = kv
        out_ref[...] = result
        up_ref[...] = result[planes - RADIUS:]
        down_ref[...] = result[:RADIUS]

    return kernel


def nonlocal_add(v, base, pick, place, proj, gain):
    planes, breadth, depth = v.shape
    picked_rows = pick.shape[0]
    home_count = proj.shape[0] // 8
    block_rows = picked_rows // home_count
    vspec = pl.BlockSpec(memory_space=pltpu.VMEM)
    rim_shape = jax.ShapeDtypeStruct((RADIUS, breadth, depth), jnp.float32)
    return pl.pallas_call(
        make_kernel(1.0, None, home_count, proj.shape[0] // home_count, block_rows, False),
        out_shape=(jax.ShapeDtypeStruct(v.shape, jnp.float32), rim_shape, rim_shape),
        in_specs=[vspec] * 6,
        out_specs=(vspec, vspec, vspec),
        scratch_shapes=[pltpu.VMEM((picked_rows, depth), jnp.bfloat16)],
    )(v, base, pick, place, proj, gain)


def apply_local(shifts, lo, v, hi, pot):
    planes, breadth, depth = v.shape
    vspec = pl.BlockSpec(memory_space=pltpu.VMEM)
    rim_shape = jax.ShapeDtypeStruct((RADIUS, breadth, depth), jnp.float32)
    return pl.pallas_call(
        make_kernel(1.0, False, 0, 0, 0, False),
        out_shape=(jax.ShapeDtypeStruct(v.shape, jnp.float32), rim_shape, rim_shape),
        in_specs=[pl.BlockSpec(memory_space=pltpu.SMEM)] + [vspec] * 4,
        out_specs=(vspec, vspec, vspec),
        scratch_shapes=[
            pltpu.VMEM((planes + 2 * RADIUS, breadth, depth), jnp.float32),
            pltpu.VMEM((8, depth), jnp.bfloat16),
        ],
    )(shifts, lo, v, hi, pot)


def apply_op(shifts, lo, v, hi, pot, pick, place, proj, gain, prev=None, scale=1.0):
    planes, breadth, depth = v.shape
    picked_rows = pick.shape[0]
    home_count = proj.shape[0] // 8
    block_rows = picked_rows // home_count
    args = [shifts, lo, v, hi, pot, pick, place, proj, gain] + ([prev] if prev is not None else [])
    vspec = pl.BlockSpec(memory_space=pltpu.VMEM)
    in_specs = [pl.BlockSpec(memory_space=pltpu.SMEM)] + [vspec] * (len(args) - 1)
    rim_shape = jax.ShapeDtypeStruct((RADIUS, breadth, depth), jnp.float32)
    return pl.pallas_call(
        make_kernel(scale, prev is not None, home_count, proj.shape[0] // home_count, block_rows),
        out_shape=(jax.ShapeDtypeStruct(v.shape, jnp.float32), rim_shape, rim_shape),
        in_specs=in_specs,
        out_specs=(vspec, vspec, vspec),
        scratch_shapes=[
            pltpu.VMEM((planes + 2 * RADIUS, breadth, depth), jnp.float32),
            pltpu.VMEM((picked_rows, depth), jnp.bfloat16),
        ],
    )(*args)


def shards(states_in, potential, projectors, proj_gains, atom_owner, atom_rows, wrap_rows):
    state_count, tile_width, breadth, line_depth = states_in.shape
    n_grid = lax.axis_size("grid")
    n_states = lax.axis_size("states")
    tile_index = lax.axis_index("grid")
    tile_lines = tile_width * breadth
    block_rows = atom_rows.shape[1]
    line_span = block_rows * line_depth
    proj_count = projectors.shape[2]
    home_count = atom_owner.shape[0]
    slot_pairs = projectors.shape[1]
    row_order = jnp.arange(breadth, dtype=jnp.int32)
    unwrap_rows = jnp.sum(
        row_order[None, :] * (wrap_rows[None, :] == row_order[:, None]).astype(jnp.int32), axis=1
    )
    atom_order = jnp.arange(home_count, dtype=jnp.int32)
    same_owner = (atom_owner[:, None] == atom_owner[None, :]) & (
        atom_order[None, :] < atom_order[:, None]
    )
    owner_rank = jnp.sum(same_owner.astype(jnp.int32), axis=1)
    atom_slot = atom_owner * PAIR_CAP + owner_rank
    local_rows = jnp.where(atom_rows >= 0, atom_rows - tile_index * tile_lines, tile_lines)

    gain_lanes = jnp.zeros((1, slot_pairs, proj_count, 128), jnp.bfloat16)
    gain_lanes = gain_lanes.at[..., 0].set(proj_gains)
    packed = jnp.concatenate([projectors, gain_lanes], axis=3)
    pairs = [(o * n_states + t, t * n_states + o) for o in range(n_grid) for t in range(n_states)]
    packed = lax.ppermute(packed, ("grid", "states"), pairs)
    def flip_y(s):
        return s ^ 8

    def flip_x(s):
        return s ^ 2

    def mirror_x(s):
        x = (s // 2) % 4
        return s + (3 - x - x) * 2

    def flip_core(s):
        return s ^ 1

    exchanges = (flip_y, flip_x, mirror_x, flip_core)

    def origins(me, done):
        if not done:
            return [me]
        return origins(me, done[:-1]) + origins(done[-1](me), done[:-1])

    gathered = packed[0]
    for exchange in exchanges:
        partner = lax.ppermute(
            gathered, "states", [(s, exchange(s)) for s in range(n_states)]
        )
        gathered = jnp.concatenate([gathered, partner], axis=0)
    block_owner = jnp.stack(origins(lax.axis_index("states"), exchanges))
    owner_block = jnp.argmax(block_owner[None, :] == atom_owner[:, None], axis=1)
    gathered = gathered.reshape(n_states * slot_pairs, proj_count, line_span + 128)
    atom_slot = owner_block * PAIR_CAP + owner_rank
    atom_pack = jnp.take(gathered, atom_slot, axis=0)
    proj_rows = atom_pack[:, :, :line_span].reshape(home_count * proj_count, line_span)
    atom_gain = atom_pack[:, :, line_span].astype(jnp.float32)
    pick = (
        local_rows.reshape(-1)[:, None] == jnp.arange(tile_lines, dtype=jnp.int32)[None, :]
    ).astype(jnp.bfloat16)
    place = pick.T
    proj_in = proj_rows.reshape(home_count * proj_count, breadth, line_depth)
    gain_in = jnp.broadcast_to(
        atom_gain.reshape(home_count * proj_count, 1, 1), (home_count * proj_count, 1, line_depth)
    )
    skew = wrap_rows[0]
    shifts = jnp.stack(
        [
            jnp.where(tile_index == 0, (breadth - skew) % breadth, 0),
            jnp.where(tile_index == n_grid - 1, skew, 0),
            jnp.zeros((), jnp.int32),
            jnp.zeros((), jnp.int32),
        ]
    ).astype(jnp.int32)
    up = [(i, (i + 1) % n_grid) for i in range(n_grid)]
    down = [(j, i) for i, j in up]

    def step(field, send_up, send_down, prev=None, scale=1.0):
        low_rim = lax.ppermute(send_up, "grid", up)
        high_rim = lax.ppermute(send_down, "grid", down)
        return apply_op(
            shifts, low_rim, field, high_rim, potential, pick, place, proj_in, gain_in, prev, scale
        )

    field = states_in[0]
    low_rim = lax.ppermute(field[tile_width - RADIUS :], "grid", up)
    high_rim = lax.ppermute(field[:RADIUS], "grid", down)
    local_part = apply_local(shifts, low_rim, field, high_rim, potential)[0]
    first_term = nonlocal_add(field, local_part, pick, place, proj_in, gain_in)
    second_term = step(*first_term, field, 2.0)
    filtered = step(*second_term, first_term[0], 2.0)
    return filtered[0][None]


def solution(mesh):
    in_specs = (
        P("states", "grid", None, None),
        P("grid", None, None),
        P("grid", "states", None, None),
        P("grid", "states", None),
        P("grid"),
        P("grid", None),
        P(),
    )
    out_specs = P("states", "grid", None, None)
    return jax.shard_map(shards, mesh=mesh, in_specs=in_specs, out_specs=out_specs, check_vma=False)
```

```python
import math

import jax
import jax.numpy as jnp
from jax import lax
from jax.experimental import pallas as pl
from jax.experimental.pallas import tpu as pltpu
from jax.sharding import PartitionSpec as P

RADIUS = 6
PAIR_CAP = 2


MIXED_WEIGHT = 0.7
CENTER = 12.0
HALF_WIDTH = 8.0


def padded_2(shard, sides, width):
    for axis, dim in sides:
        count, length = (lax.axis_size(axis), shard.shape[dim])
        up = [(i, (i + 1) % count) for i in range(count)]
        down = [(j, i) for i, j in up]
        last = lax.slice_in_dim(shard, length - width, length, axis=dim)
        initial = lax.slice_in_dim(shard, 0, width, axis=dim)
        before = lax.ppermute(last, axis, up)
        after = lax.ppermute(initial, axis, down)
        shard = jnp.concatenate([before, shard, after], axis=dim)
    return shard


def second_table(radius):
    weights = [-2.0 * sum((1.0 / (k * k) for k in range(1, radius + 1)))]
    for k in range(1, radius + 1):
        weights.append(
            2.0
            * (-1) ** (k + 1)
            * math.factorial(radius) ** 2
            / (k * k * math.factorial(radius - k) * math.factorial(radius + k))
        )
    return weights


def first_table(radius):
    weights = [0.0]
    for k in range(1, radius + 1):
        weights.append(
            (-1) ** (k + 1)
            * math.factorial(radius) ** 2
            / (k * math.factorial(radius - k) * math.factorial(radius + k))
        )
    return weights


def laplacian(padded, plane_count):
    second_weights = second_table(RADIUS)
    first_weights = first_table(RADIUS)
    interior = padded[:, RADIUS : RADIUS + plane_count]
    line_depth = interior.shape[3]
    z_padded = jnp.pad(interior, ((0, 0), (0, 0), (0, 0), (RADIUS, RADIUS)))
    summed = 3.0 * second_weights[0] * interior
    y_slope = jnp.zeros_like(padded)
    for k in range(1, RADIUS + 1):
        summed = summed + second_weights[k] * (
            padded[:, RADIUS + k : RADIUS + k + plane_count]
            + padded[:, RADIUS - k : RADIUS - k + plane_count]
        )
        summed = summed + second_weights[k] * (jnp.roll(interior, -k, 2) + jnp.roll(interior, k, 2))
        summed = summed + second_weights[k] * (
            z_padded[:, :, :, RADIUS + k : RADIUS + k + line_depth]
            + z_padded[:, :, :, RADIUS - k : RADIUS - k + line_depth]
        )
        y_slope = y_slope + first_weights[k] * (jnp.roll(padded, -k, 2) - jnp.roll(padded, k, 2))
    cross_term = jnp.zeros_like(interior)
    for k in range(1, RADIUS + 1):
        cross_term = cross_term + first_weights[k] * (
            y_slope[:, RADIUS + k : RADIUS + k + plane_count]
            - y_slope[:, RADIUS - k : RADIUS - k + plane_count]
        )
    return summed + MIXED_WEIGHT * cross_term


def make_kernel(scale, with_prev, home_count, proj_count, block_rows):
    sw = second_table(RADIUS)
    fw = first_table(RADIUS)

    def kernel(shift_ref, lo_ref, v_ref, hi_ref, pot_ref, pick_ref, place_ref, proj_ref, gain_ref, *rest):
        if with_prev:
            prev_ref, out_ref, up_ref, down_ref, pad_ref, rows_ref = rest
        else:
            out_ref, up_ref, down_ref, pad_ref, rows_ref = rest
        planes, breadth, depth = v_ref.shape
        v = v_ref[...]
        pad_ref[0:RADIUS] = pltpu.roll(lo_ref[...], shift_ref[0], 1)
        pad_ref[RADIUS:RADIUS + planes] = v
        pad_ref[RADIUS + planes:] = pltpu.roll(hi_ref[...], shift_ref[1], 1)

        lines = v.reshape(planes * breadth, depth).astype(jnp.bfloat16)
        picked = jnp.dot(pick_ref[...], lines, preferred_element_type=jnp.float32)

        def one_atom(a, carry):
            base = pl.multiple_of(a * block_rows, block_rows)
            here = picked_ref_load(base)
            acc = jnp.zeros((block_rows, depth), jnp.float32)
            for j in range(proj_count):
                proj = proj_ref[a * proj_count + j].astype(jnp.float32)
                coef = jnp.sum(jnp.sum(proj * here, axis=0, keepdims=True), axis=1, keepdims=True)
                gain = gain_ref[a * proj_count + j]
                scaled = (coef * gain).astype(jnp.bfloat16).astype(jnp.float32)
                acc = acc + proj * scaled
            rows_ref[pl.ds(base, block_rows), :] = acc.astype(jnp.bfloat16)
            return carry

        rows_ref[...] = picked.astype(jnp.bfloat16)

        def picked_ref_load(base):
            return rows_ref[pl.ds(base, block_rows), :].astype(jnp.float32)

        lax.fori_loop(0, home_count, one_atom, 0, unroll=True)
        nonlocal_lines = jnp.dot(place_ref[...], rows_ref[...], preferred_element_type=jnp.float32)
        nonlocal_lines = nonlocal_lines.reshape(planes, breadth, depth)

        lane = lax.broadcasted_iota(jnp.int32, v.shape, 2)
        summed = (3.0 * sw[0]) * v
        for k in range(1, RADIUS + 1):
            xs = pad_ref[RADIUS + k:RADIUS + k + planes] + pad_ref[RADIUS - k:RADIUS - k + planes]
            ys = pltpu.roll(v, breadth - k, 1) + pltpu.roll(v, k, 1)
            zs = (jnp.where(lane < depth - k, pltpu.roll(v, depth - k, 2), 0.0)
                  + jnp.where(lane >= k, pltpu.roll(v, k, 2), 0.0))
            summed = summed + sw[k] * xs + sw[k] * ys + sw[k] * zs
        padded = pad_ref[...]
        slope = fw[1] * (pltpu.roll(padded, breadth - 1, 1) - pltpu.roll(padded, 1, 1))
        for k in range(2, RADIUS + 1):
            slope = slope + fw[k] * (pltpu.roll(padded, breadth - k, 1) - pltpu.roll(padded, k, 1))
        cross = fw[1] * (slope[RADIUS + 1:RADIUS + 1 + planes] - slope[RADIUS - 1:RADIUS - 1 + planes])
        for k in range(2, RADIUS + 1):
            cross = cross + fw[k] * (slope[RADIUS + k:RADIUS + k + planes] - slope[RADIUS - k:RADIUS - k + planes])
        lap = summed + 0.7 * cross
        hv = -0.5 * lap + pot_ref[...] * v + nonlocal_lines
        kv = (hv - 12.0 * v) / 8.0
        if with_prev:
            result = scale * kv - prev_ref[...]
        else:
            result = kv
        out_ref[...] = result
        up_ref[...] = result[planes - RADIUS:]
        down_ref[...] = result[:RADIUS]

    return kernel


def apply_op(shifts, lo, v, hi, pot, pick, place, proj, gain, prev=None, scale=1.0):
    planes, breadth, depth = v.shape
    picked_rows = pick.shape[0]
    home_count = proj.shape[0] // 8
    block_rows = picked_rows // home_count
    args = [shifts, lo, v, hi, pot, pick, place, proj, gain] + ([prev] if prev is not None else [])
    vspec = pl.BlockSpec(memory_space=pltpu.VMEM)
    sspec = pl.BlockSpec(memory_space=pltpu.SMEM)
    in_specs = [sspec] + [vspec] * 7 + [sspec] + [vspec] * (len(args) - 9)
    rim_shape = jax.ShapeDtypeStruct((RADIUS, breadth, depth), jnp.float32)
    return pl.pallas_call(
        make_kernel(scale, prev is not None, home_count, proj.shape[0] // home_count, block_rows),
        out_shape=(jax.ShapeDtypeStruct(v.shape, jnp.float32), rim_shape, rim_shape),
        in_specs=in_specs,
        out_specs=(vspec, vspec, vspec),
        scratch_shapes=[
            pltpu.VMEM((planes + 2 * RADIUS, breadth, depth), jnp.float32),
            pltpu.VMEM((picked_rows, depth), jnp.bfloat16),
        ],
    )(*args)


def shards(states_in, potential, projectors, proj_gains, atom_owner, atom_rows, wrap_rows):
    state_count, tile_width, breadth, line_depth = states_in.shape
    n_grid = lax.axis_size("grid")
    n_states = lax.axis_size("states")
    tile_index = lax.axis_index("grid")
    tile_lines = tile_width * breadth
    block_rows = atom_rows.shape[1]
    line_span = block_rows * line_depth
    proj_count = projectors.shape[2]
    home_count = atom_owner.shape[0]
    slot_pairs = projectors.shape[1]
    row_order = jnp.arange(breadth, dtype=jnp.int32)
    unwrap_rows = jnp.sum(
        row_order[None, :] * (wrap_rows[None, :] == row_order[:, None]).astype(jnp.int32), axis=1
    )
    atom_order = jnp.arange(home_count, dtype=jnp.int32)
    same_owner = (atom_owner[:, None] == atom_owner[None, :]) & (
        atom_order[None, :] < atom_order[:, None]
    )
    owner_rank = jnp.sum(same_owner.astype(jnp.int32), axis=1)
    atom_slot = atom_owner * PAIR_CAP + owner_rank
    local_rows = jnp.where(atom_rows >= 0, atom_rows - tile_index * tile_lines, tile_lines)

    gain_lanes = jnp.zeros((1, slot_pairs, proj_count, 128), jnp.bfloat16)
    gain_lanes = gain_lanes.at[..., 0].set(proj_gains)
    packed = jnp.concatenate([projectors, gain_lanes], axis=3)
    pairs = [(o * n_states + t, t * n_states + o) for o in range(n_grid) for t in range(n_states)]
    packed = lax.ppermute(packed, ("grid", "states"), pairs)
    def flip_y(s):
        return s ^ 8

    def flip_x(s):
        return s ^ 2

    def mirror_x(s):
        x = (s // 2) % 4
        return s + (3 - x - x) * 2

    def flip_core(s):
        return s ^ 1

    exchanges = (flip_y, flip_x, mirror_x, flip_core)

    def origins(me, done):
        if not done:
            return [me]
        return origins(me, done[:-1]) + origins(done[-1](me), done[:-1])

    gathered = packed[0]
    for exchange in exchanges:
        partner = lax.ppermute(
            gathered, "states", [(s, exchange(s)) for s in range(n_states)]
        )
        gathered = jnp.concatenate([gathered, partner], axis=0)
    block_owner = jnp.stack(origins(lax.axis_index("states"), exchanges))
    owner_block = jnp.argmax(block_owner[None, :] == atom_owner[:, None], axis=1)
    gathered = gathered.reshape(n_states * slot_pairs, proj_count, line_span + 128)
    atom_slot = owner_block * PAIR_CAP + owner_rank
    atom_pack = jnp.take(gathered, atom_slot, axis=0)
    proj_rows = atom_pack[:, :, :line_span].reshape(home_count * proj_count, line_span)
    atom_gain = atom_pack[:, :, line_span].astype(jnp.float32)
    pick = (
        local_rows.reshape(-1)[:, None] == jnp.arange(tile_lines, dtype=jnp.int32)[None, :]
    ).astype(jnp.bfloat16)
    place = pick.T
    proj_in = proj_rows.reshape(home_count * proj_count, breadth, line_depth)
    gain_in = atom_gain.reshape(home_count * proj_count)
    skew = wrap_rows[0]
    shifts = jnp.stack(
        [
            jnp.where(tile_index == 0, (breadth - skew) % breadth, 0),
            jnp.where(tile_index == n_grid - 1, skew, 0),
            jnp.zeros((), jnp.int32),
            jnp.zeros((), jnp.int32),
        ]
    ).astype(jnp.int32)
    up = [(i, (i + 1) % n_grid) for i in range(n_grid)]
    down = [(j, i) for i, j in up]

    def step(field, send_up, send_down, prev=None, scale=1.0):
        low_rim = lax.ppermute(send_up, "grid", up)
        high_rim = lax.ppermute(send_down, "grid", down)
        return apply_op(
            shifts, low_rim, field, high_rim, potential, pick, place, proj_in, gain_in, prev, scale
        )

    field = states_in[0]
    first_term = step(field, field[tile_width - RADIUS :], field[:RADIUS])
    second_term = step(*first_term, field, 2.0)
    filtered = step(*second_term, first_term[0], 2.0)
    return filtered[0][None]


def solution(mesh):
    in_specs = (
        P("states", "grid", None, None),
        P("grid", None, None),
        P("grid", "states", None, None),
        P("grid", "states", None),
        P("grid"),
        P("grid", None),
        P(),
    )
    out_specs = P("states", "grid", None, None)
    return jax.shard_map(shards, mesh=mesh, in_specs=in_specs, out_specs=out_specs, check_vma=False)
```

```python
import math

import jax
import jax.numpy as jnp
from jax import lax
from jax.experimental import pallas as pl
from jax.experimental.pallas import tpu as pltpu
from jax.sharding import PartitionSpec as P

RADIUS = 6
PAIR_CAP = 2


MIXED_WEIGHT = 0.7
CENTER = 12.0
HALF_WIDTH = 8.0


def padded_2(shard, sides, width):
    for axis, dim in sides:
        count, length = (lax.axis_size(axis), shard.shape[dim])
        up = [(i, (i + 1) % count) for i in range(count)]
        down = [(j, i) for i, j in up]
        last = lax.slice_in_dim(shard, length - width, length, axis=dim)
        initial = lax.slice_in_dim(shard, 0, width, axis=dim)
        before = lax.ppermute(last, axis, up)
        after = lax.ppermute(initial, axis, down)
        shard = jnp.concatenate([before, shard, after], axis=dim)
    return shard


def second_table(radius):
    weights = [-2.0 * sum((1.0 / (k * k) for k in range(1, radius + 1)))]
    for k in range(1, radius + 1):
        weights.append(
            2.0
            * (-1) ** (k + 1)
            * math.factorial(radius) ** 2
            / (k * k * math.factorial(radius - k) * math.factorial(radius + k))
        )
    return weights


def first_table(radius):
    weights = [0.0]
    for k in range(1, radius + 1):
        weights.append(
            (-1) ** (k + 1)
            * math.factorial(radius) ** 2
            / (k * math.factorial(radius - k) * math.factorial(radius + k))
        )
    return weights


def laplacian(padded, plane_count):
    second_weights = second_table(RADIUS)
    first_weights = first_table(RADIUS)
    interior = padded[:, RADIUS : RADIUS + plane_count]
    line_depth = interior.shape[3]
    z_padded = jnp.pad(interior, ((0, 0), (0, 0), (0, 0), (RADIUS, RADIUS)))
    summed = 3.0 * second_weights[0] * interior
    y_slope = jnp.zeros_like(padded)
    for k in range(1, RADIUS + 1):
        summed = summed + second_weights[k] * (
            padded[:, RADIUS + k : RADIUS + k + plane_count]
            + padded[:, RADIUS - k : RADIUS - k + plane_count]
        )
        summed = summed + second_weights[k] * (jnp.roll(interior, -k, 2) + jnp.roll(interior, k, 2))
        summed = summed + second_weights[k] * (
            z_padded[:, :, :, RADIUS + k : RADIUS + k + line_depth]
            + z_padded[:, :, :, RADIUS - k : RADIUS - k + line_depth]
        )
        y_slope = y_slope + first_weights[k] * (jnp.roll(padded, -k, 2) - jnp.roll(padded, k, 2))
    cross_term = jnp.zeros_like(interior)
    for k in range(1, RADIUS + 1):
        cross_term = cross_term + first_weights[k] * (
            y_slope[:, RADIUS + k : RADIUS + k + plane_count]
            - y_slope[:, RADIUS - k : RADIUS - k + plane_count]
        )
    return summed + MIXED_WEIGHT * cross_term


def make_kernel(scale, with_prev, home_count, proj_count, block_rows):
    sw = second_table(RADIUS)
    fw = first_table(RADIUS)

    def kernel(shift_ref, lo_ref, v_ref, hi_ref, pot_ref, pick_ref, place_ref, proj_ref, gain_ref, *rest):
        if with_prev:
            prev_ref, out_ref, up_ref, down_ref, pad_ref, rows_ref = rest
        else:
            out_ref, up_ref, down_ref, pad_ref, rows_ref = rest
        planes, breadth, depth = v_ref.shape
        v = v_ref[...]
        even = shift_ref[2].astype(jnp.float32)
        odd = 1.0 - even
        first_swap = lo_ref[...]
        second_swap = hi_ref[...]
        low_rim = even * second_swap + odd * first_swap
        high_rim = even * first_swap + odd * second_swap
        pad_ref[0:RADIUS] = pltpu.roll(low_rim, shift_ref[0], 1)
        pad_ref[RADIUS:RADIUS + planes] = v
        pad_ref[RADIUS + planes:] = pltpu.roll(high_rim, shift_ref[1], 1)

        lines = v.reshape(planes * breadth, depth).astype(jnp.bfloat16)
        picked = jnp.dot(pick_ref[...], lines, preferred_element_type=jnp.float32)

        def one_atom(a, carry):
            base = pl.multiple_of(a * block_rows, block_rows)
            here = picked_ref_load(base)
            acc = jnp.zeros((block_rows, depth), jnp.float32)
            for j in range(proj_count):
                proj = proj_ref[a * proj_count + j].astype(jnp.float32)
                coef = jnp.sum(jnp.sum(proj * here, axis=0, keepdims=True), axis=1, keepdims=True)
                gain = gain_ref[a * proj_count + j]
                scaled = (coef * gain).astype(jnp.bfloat16).astype(jnp.float32)
                acc = acc + proj * scaled
            rows_ref[pl.ds(base, block_rows), :] = acc.astype(jnp.bfloat16)
            return carry

        rows_ref[...] = picked.astype(jnp.bfloat16)

        def picked_ref_load(base):
            return rows_ref[pl.ds(base, block_rows), :].astype(jnp.float32)

        lax.fori_loop(0, home_count, one_atom, 0, unroll=True)
        nonlocal_lines = jnp.dot(place_ref[...], rows_ref[...], preferred_element_type=jnp.float32)
        nonlocal_lines = nonlocal_lines.reshape(planes, breadth, depth)

        lane = lax.broadcasted_iota(jnp.int32, v.shape, 2)
        summed = (3.0 * sw[0]) * v
        for k in range(1, RADIUS + 1):
            xs = pad_ref[RADIUS + k:RADIUS + k + planes] + pad_ref[RADIUS - k:RADIUS - k + planes]
            ys = pltpu.roll(v, breadth - k, 1) + pltpu.roll(v, k, 1)
            zs = (jnp.where(lane < depth - k, pltpu.roll(v, depth - k, 2), 0.0)
                  + jnp.where(lane >= k, pltpu.roll(v, k, 2), 0.0))
            summed = summed + sw[k] * xs + sw[k] * ys + sw[k] * zs
        padded = pad_ref[...]
        slope = fw[1] * (pltpu.roll(padded, breadth - 1, 1) - pltpu.roll(padded, 1, 1))
        for k in range(2, RADIUS + 1):
            slope = slope + fw[k] * (pltpu.roll(padded, breadth - k, 1) - pltpu.roll(padded, k, 1))
        cross = fw[1] * (slope[RADIUS + 1:RADIUS + 1 + planes] - slope[RADIUS - 1:RADIUS - 1 + planes])
        for k in range(2, RADIUS + 1):
            cross = cross + fw[k] * (slope[RADIUS + k:RADIUS + k + planes] - slope[RADIUS - k:RADIUS - k + planes])
        lap = summed + 0.7 * cross
        hv = -0.5 * lap + pot_ref[...] * v + nonlocal_lines
        kv = (hv - 12.0 * v) / 8.0
        if with_prev:
            result = scale * kv - prev_ref[...]
        else:
            result = kv
        out_ref[...] = result
        top = result[planes - RADIUS:]
        bottom = result[:RADIUS]
        up_ref[...] = even * top + odd * bottom
        down_ref[...] = even * bottom + odd * top

    return kernel


def apply_op(shifts, lo, v, hi, pot, pick, place, proj, gain, prev=None, scale=1.0):
    planes, breadth, depth = v.shape
    picked_rows = pick.shape[0]
    home_count = proj.shape[0] // 8
    block_rows = picked_rows // home_count
    args = [shifts, lo, v, hi, pot, pick, place, proj, gain] + ([prev] if prev is not None else [])
    vspec = pl.BlockSpec(memory_space=pltpu.VMEM)
    in_specs = [pl.BlockSpec(memory_space=pltpu.SMEM)] + [vspec] * (len(args) - 1)
    rim_shape = jax.ShapeDtypeStruct((RADIUS, breadth, depth), jnp.float32)
    return pl.pallas_call(
        make_kernel(scale, prev is not None, home_count, proj.shape[0] // home_count, block_rows),
        out_shape=(jax.ShapeDtypeStruct(v.shape, jnp.float32), rim_shape, rim_shape),
        in_specs=in_specs,
        out_specs=(vspec, vspec, vspec),
        scratch_shapes=[
            pltpu.VMEM((planes + 2 * RADIUS, breadth, depth), jnp.float32),
            pltpu.VMEM((picked_rows, depth), jnp.bfloat16),
        ],
    )(*args)


def shards(states_in, potential, projectors, proj_gains, atom_owner, atom_rows, wrap_rows):
    state_count, tile_width, breadth, line_depth = states_in.shape
    n_grid = lax.axis_size("grid")
    n_states = lax.axis_size("states")
    tile_index = lax.axis_index("grid")
    tile_lines = tile_width * breadth
    block_rows = atom_rows.shape[1]
    line_span = block_rows * line_depth
    proj_count = projectors.shape[2]
    home_count = atom_owner.shape[0]
    slot_pairs = projectors.shape[1]
    row_order = jnp.arange(breadth, dtype=jnp.int32)
    unwrap_rows = jnp.sum(
        row_order[None, :] * (wrap_rows[None, :] == row_order[:, None]).astype(jnp.int32), axis=1
    )
    atom_order = jnp.arange(home_count, dtype=jnp.int32)
    same_owner = (atom_owner[:, None] == atom_owner[None, :]) & (
        atom_order[None, :] < atom_order[:, None]
    )
    owner_rank = jnp.sum(same_owner.astype(jnp.int32), axis=1)
    atom_slot = atom_owner * PAIR_CAP + owner_rank
    local_rows = jnp.where(atom_rows >= 0, atom_rows - tile_index * tile_lines, tile_lines)

    gain_lanes = jnp.zeros((1, slot_pairs, proj_count, 128), jnp.bfloat16)
    gain_lanes = gain_lanes.at[..., 0].set(proj_gains)
    packed = jnp.concatenate([projectors, gain_lanes], axis=3)
    pairs = [(o * n_states + t, t * n_states + o) for o in range(n_grid) for t in range(n_states)]
    packed = lax.ppermute(packed, ("grid", "states"), pairs)
    def flip_y(s):
        return s ^ 8

    def flip_x(s):
        return s ^ 2

    def mirror_x(s):
        x = (s // 2) % 4
        return s + (3 - x - x) * 2

    def flip_core(s):
        return s ^ 1

    exchanges = (flip_y, flip_x, mirror_x, flip_core)

    def origins(me, done):
        if not done:
            return [me]
        return origins(me, done[:-1]) + origins(done[-1](me), done[:-1])

    gathered = packed[0]
    for exchange in exchanges:
        partner = lax.ppermute(
            gathered, "states", [(s, exchange(s)) for s in range(n_states)]
        )
        gathered = jnp.concatenate([gathered, partner], axis=0)
    block_owner = jnp.stack(origins(lax.axis_index("states"), exchanges))
    owner_block = jnp.argmax(block_owner[None, :] == atom_owner[:, None], axis=1)
    gathered = gathered.reshape(n_states * slot_pairs, proj_count, line_span + 128)
    atom_slot = owner_block * PAIR_CAP + owner_rank
    atom_pack = jnp.take(gathered, atom_slot, axis=0)
    proj_rows = atom_pack[:, :, :line_span].reshape(home_count * proj_count, line_span)
    atom_gain = atom_pack[:, :, line_span].astype(jnp.float32)
    pick = (
        local_rows.reshape(-1)[:, None] == jnp.arange(tile_lines, dtype=jnp.int32)[None, :]
    ).astype(jnp.bfloat16)
    place = pick.T
    proj_in = proj_rows.reshape(home_count * proj_count, breadth, line_depth)
    gain_in = jnp.broadcast_to(
        atom_gain.reshape(home_count * proj_count, 1, 1), (home_count * proj_count, 1, line_depth)
    )
    skew = wrap_rows[0]
    shifts = jnp.stack(
        [
            jnp.where(tile_index == 0, (breadth - skew) % breadth, 0),
            jnp.where(tile_index == n_grid - 1, skew, 0),
            (tile_index % 2 == 0).astype(jnp.int32),
            jnp.zeros((), jnp.int32),
        ]
    ).astype(jnp.int32)
    up = [(i, (i + 1) % n_grid) for i in range(n_grid)]
    down = [(j, i) for i, j in up]

    first_pairs = [(g, g ^ 1) for g in range(n_grid)]
    second_pairs = [(g, (g + 1) % n_grid if g % 2 else (g - 1) % n_grid) for g in range(n_grid)]

    def step(field, send_first, send_second, prev=None, scale=1.0):
        low_rim = lax.ppermute(send_first, "grid", first_pairs)
        high_rim = lax.ppermute(send_second, "grid", second_pairs)
        return apply_op(
            shifts, low_rim, field, high_rim, potential, pick, place, proj_in, gain_in, prev, scale
        )

    field = states_in[0]
    is_even = tile_index % 2 == 0
    top, bottom = field[tile_width - RADIUS :], field[:RADIUS]
    first_term = step(
        field, jnp.where(is_even, top, bottom), jnp.where(is_even, bottom, top)
    )
    second_term = step(*first_term, field, 2.0)
    filtered = step(*second_term, first_term[0], 2.0)
    return filtered[0][None]


def solution(mesh):
    in_specs = (
        P("states", "grid", None, None),
        P("grid", None, None),
        P("grid", "states", None, None),
        P("grid", "states", None),
        P("grid"),
        P("grid", None),
        P(),
    )
    out_specs = P("states", "grid", None, None)
    return jax.shard_map(shards, mesh=mesh, in_specs=in_specs, out_specs=out_specs, check_vma=False)
```

```python
import math

import jax
import jax.numpy as jnp
from jax import lax
from jax.experimental import pallas as pl
from jax.experimental.pallas import tpu as pltpu
from jax.sharding import PartitionSpec as P

RADIUS = 6
PAIR_CAP = 2


MIXED_WEIGHT = 0.7
CENTER = 12.0
HALF_WIDTH = 8.0


def padded_2(shard, sides, width):
    for axis, dim in sides:
        count, length = (lax.axis_size(axis), shard.shape[dim])
        up = [(i, (i + 1) % count) for i in range(count)]
        down = [(j, i) for i, j in up]
        last = lax.slice_in_dim(shard, length - width, length, axis=dim)
        initial = lax.slice_in_dim(shard, 0, width, axis=dim)
        before = lax.ppermute(last, axis, up)
        after = lax.ppermute(initial, axis, down)
        shard = jnp.concatenate([before, shard, after], axis=dim)
    return shard


def second_table(radius):
    weights = [-2.0 * sum((1.0 / (k * k) for k in range(1, radius + 1)))]
    for k in range(1, radius + 1):
        weights.append(
            2.0
            * (-1) ** (k + 1)
            * math.factorial(radius) ** 2
            / (k * k * math.factorial(radius - k) * math.factorial(radius + k))
        )
    return weights


def first_table(radius):
    weights = [0.0]
    for k in range(1, radius + 1):
        weights.append(
            (-1) ** (k + 1)
            * math.factorial(radius) ** 2
            / (k * math.factorial(radius - k) * math.factorial(radius + k))
        )
    return weights


def laplacian(padded, plane_count):
    second_weights = second_table(RADIUS)
    first_weights = first_table(RADIUS)
    interior = padded[:, RADIUS : RADIUS + plane_count]
    line_depth = interior.shape[3]
    z_padded = jnp.pad(interior, ((0, 0), (0, 0), (0, 0), (RADIUS, RADIUS)))
    summed = 3.0 * second_weights[0] * interior
    y_slope = jnp.zeros_like(padded)
    for k in range(1, RADIUS + 1):
        summed = summed + second_weights[k] * (
            padded[:, RADIUS + k : RADIUS + k + plane_count]
            + padded[:, RADIUS - k : RADIUS - k + plane_count]
        )
        summed = summed + second_weights[k] * (jnp.roll(interior, -k, 2) + jnp.roll(interior, k, 2))
        summed = summed + second_weights[k] * (
            z_padded[:, :, :, RADIUS + k : RADIUS + k + line_depth]
            + z_padded[:, :, :, RADIUS - k : RADIUS - k + line_depth]
        )
        y_slope = y_slope + first_weights[k] * (jnp.roll(padded, -k, 2) - jnp.roll(padded, k, 2))
    cross_term = jnp.zeros_like(interior)
    for k in range(1, RADIUS + 1):
        cross_term = cross_term + first_weights[k] * (
            y_slope[:, RADIUS + k : RADIUS + k + plane_count]
            - y_slope[:, RADIUS - k : RADIUS - k + plane_count]
        )
    return summed + MIXED_WEIGHT * cross_term


def make_kernel(scale, with_prev, home_count, proj_count, block_rows):
    sw = second_table(RADIUS)
    fw = first_table(RADIUS)

    def kernel(shift_ref, lo_ref, v_ref, hi_ref, pot_ref, pick_ref, place_ref, proj_ref, gain_ref, *rest):
        if with_prev:
            prev_ref, out_ref, up_ref, down_ref, pad_ref, rows_ref = rest
        else:
            out_ref, up_ref, down_ref, pad_ref, rows_ref = rest
        planes, breadth, depth = v_ref.shape
        v = v_ref[...]
        pad_ref[0:RADIUS] = pltpu.roll(lo_ref[...], shift_ref[0], 1)
        pad_ref[RADIUS:RADIUS + planes] = v
        pad_ref[RADIUS + planes:] = pltpu.roll(hi_ref[...], shift_ref[1], 1)

        lines = v.reshape(planes * breadth, depth).astype(jnp.bfloat16)
        picked = jnp.dot(pick_ref[...], lines, preferred_element_type=jnp.float32)

        def one_atom(a, carry):
            base = pl.multiple_of(a * block_rows, block_rows)
            here = picked_ref_load(base)
            acc = jnp.zeros((block_rows, depth), jnp.float32)
            for j in range(proj_count):
                proj = proj_ref[a * proj_count + j].astype(jnp.float32)
                coef = jnp.sum(jnp.sum(proj * here, axis=0, keepdims=True), axis=1, keepdims=True)
                gain = gain_ref[a * proj_count + j]
                scaled = (coef * gain).astype(jnp.bfloat16).astype(jnp.float32)
                acc = acc + proj * scaled
            rows_ref[pl.ds(base, block_rows), :] = acc.astype(jnp.bfloat16)
            return carry

        rows_ref[...] = picked.astype(jnp.bfloat16)

        def picked_ref_load(base):
            return rows_ref[pl.ds(base, block_rows), :].astype(jnp.float32)

        lax.fori_loop(0, home_count, one_atom, 0, unroll=True)
        nonlocal_lines = jnp.dot(place_ref[...], rows_ref[...], preferred_element_type=jnp.float32)
        nonlocal_lines = nonlocal_lines.reshape(planes, breadth, depth)

        lane = lax.broadcasted_iota(jnp.int32, v.shape, 2)
        summed = (3.0 * sw[0]) * v
        for k in range(1, RADIUS + 1):
            xs = pad_ref[RADIUS + k:RADIUS + k + planes] + pad_ref[RADIUS - k:RADIUS - k + planes]
            ys = pltpu.roll(v, breadth - k, 1) + pltpu.roll(v, k, 1)
            zs = (jnp.where(lane < depth - k, pltpu.roll(v, depth - k, 2), 0.0)
                  + jnp.where(lane >= k, pltpu.roll(v, k, 2), 0.0))
            summed = summed + sw[k] * xs + sw[k] * ys + sw[k] * zs
        x_slope = fw[1] * (pad_ref[RADIUS + 1:RADIUS + 1 + planes] - pad_ref[RADIUS - 1:RADIUS - 1 + planes])
        for k in range(2, RADIUS + 1):
            x_slope = x_slope + fw[k] * (
                pad_ref[RADIUS + k:RADIUS + k + planes] - pad_ref[RADIUS - k:RADIUS - k + planes]
            )
        cross = fw[1] * (pltpu.roll(x_slope, breadth - 1, 1) - pltpu.roll(x_slope, 1, 1))
        for k in range(2, RADIUS + 1):
            cross = cross + fw[k] * (pltpu.roll(x_slope, breadth - k, 1) - pltpu.roll(x_slope, k, 1))
        lap = summed + 0.7 * cross
        hv = -0.5 * lap + pot_ref[...] * v + nonlocal_lines
        kv = (hv - 12.0 * v) / 8.0
        if with_prev:
            result = scale * kv - prev_ref[...]
        else:
            result = kv
        out_ref[...] = result
        up_ref[...] = result[planes - RADIUS:]
        down_ref[...] = result[:RADIUS]

    return kernel


def apply_op(shifts, lo, v, hi, pot, pick, place, proj, gain, prev=None, scale=1.0):
    planes, breadth, depth = v.shape
    picked_rows = pick.shape[0]
    home_count = proj.shape[0] // 8
    block_rows = picked_rows // home_count
    args = [shifts, lo, v, hi, pot, pick, place, proj, gain] + ([prev] if prev is not None else [])
    vspec = pl.BlockSpec(memory_space=pltpu.VMEM)
    sspec = pl.BlockSpec(memory_space=pltpu.SMEM)
    in_specs = [sspec] + [vspec] * 7 + [sspec] + [vspec] * (len(args) - 9)
    rim_shape = jax.ShapeDtypeStruct((RADIUS, breadth, depth), jnp.float32)
    return pl.pallas_call(
        make_kernel(scale, prev is not None, home_count, proj.shape[0] // home_count, block_rows),
        out_shape=(jax.ShapeDtypeStruct(v.shape, jnp.float32), rim_shape, rim_shape),
        in_specs=in_specs,
        out_specs=(vspec, vspec, vspec),
        scratch_shapes=[
            pltpu.VMEM((planes + 2 * RADIUS, breadth, depth), jnp.float32),
            pltpu.VMEM((picked_rows, depth), jnp.bfloat16),
        ],
    )(*args)


def shards(states_in, potential, projectors, proj_gains, atom_owner, atom_rows, wrap_rows):
    state_count, tile_width, breadth, line_depth = states_in.shape
    n_grid = lax.axis_size("grid")
    n_states = lax.axis_size("states")
    tile_index = lax.axis_index("grid")
    tile_lines = tile_width * breadth
    block_rows = atom_rows.shape[1]
    line_span = block_rows * line_depth
    proj_count = projectors.shape[2]
    home_count = atom_owner.shape[0]
    slot_pairs = projectors.shape[1]
    row_order = jnp.arange(breadth, dtype=jnp.int32)
    unwrap_rows = jnp.sum(
        row_order[None, :] * (wrap_rows[None, :] == row_order[:, None]).astype(jnp.int32), axis=1
    )
    atom_order = jnp.arange(home_count, dtype=jnp.int32)
    same_owner = (atom_owner[:, None] == atom_owner[None, :]) & (
        atom_order[None, :] < atom_order[:, None]
    )
    owner_rank = jnp.sum(same_owner.astype(jnp.int32), axis=1)
    atom_slot = atom_owner * PAIR_CAP + owner_rank
    local_rows = jnp.where(atom_rows >= 0, atom_rows - tile_index * tile_lines, tile_lines)

    gain_lanes = jnp.zeros((1, slot_pairs, proj_count, 128), jnp.bfloat16)
    gain_lanes = gain_lanes.at[..., 0].set(proj_gains)
    packed = jnp.concatenate([projectors, gain_lanes], axis=3)
    pairs = [(o * n_states + t, t * n_states + o) for o in range(n_grid) for t in range(n_states)]
    packed = lax.ppermute(packed, ("grid", "states"), pairs)
    def flip_y(s):
        return s ^ 8

    def flip_x(s):
        return s ^ 2

    def mirror_x(s):
        x = (s // 2) % 4
        return s + (3 - x - x) * 2

    def flip_core(s):
        return s ^ 1

    exchanges = (flip_y, flip_x, mirror_x, flip_core)

    def origins(me, done):
        if not done:
            return [me]
        return origins(me, done[:-1]) + origins(done[-1](me), done[:-1])

    gathered = packed[0]
    for exchange in exchanges:
        partner = lax.ppermute(
            gathered, "states", [(s, exchange(s)) for s in range(n_states)]
        )
        gathered = jnp.concatenate([gathered, partner], axis=0)
    block_owner = jnp.stack(origins(lax.axis_index("states"), exchanges))
    owner_block = jnp.argmax(block_owner[None, :] == atom_owner[:, None], axis=1)
    gathered = gathered.reshape(n_states * slot_pairs, proj_count, line_span + 128)
    atom_slot = owner_block * PAIR_CAP + owner_rank
    atom_pack = jnp.take(gathered, atom_slot, axis=0)
    proj_rows = atom_pack[:, :, :line_span].reshape(home_count * proj_count, line_span)
    atom_gain = atom_pack[:, :, line_span].astype(jnp.float32)
    pick = (
        local_rows.reshape(-1)[:, None] == jnp.arange(tile_lines, dtype=jnp.int32)[None, :]
    ).astype(jnp.bfloat16)
    place = pick.T
    proj_in = proj_rows.reshape(home_count * proj_count, breadth, line_depth)
    gain_in = atom_gain.reshape(home_count * proj_count)
    skew = wrap_rows[0]
    shifts = jnp.stack(
        [
            jnp.where(tile_index == 0, (breadth - skew) % breadth, 0),
            jnp.where(tile_index == n_grid - 1, skew, 0),
            jnp.zeros((), jnp.int32),
            jnp.zeros((), jnp.int32),
        ]
    ).astype(jnp.int32)
    up = [(i, (i + 1) % n_grid) for i in range(n_grid)]
    down = [(j, i) for i, j in up]

    def step(field, send_up, send_down, prev=None, scale=1.0):
        low_rim = lax.ppermute(send_up, "grid", up)
        high_rim = lax.ppermute(send_down, "grid", down)
        return apply_op(
            shifts, low_rim, field, high_rim, potential, pick, place, proj_in, gain_in, prev, scale
        )

    field = states_in[0]
    first_term = step(field, field[tile_width - RADIUS :], field[:RADIUS])
    second_term = step(*first_term, field, 2.0)
    filtered = step(*second_term, first_term[0], 2.0)
    return filtered[0][None]


def solution(mesh):
    in_specs = (
        P("states", "grid", None, None),
        P("grid", None, None),
        P("grid", "states", None, None),
        P("grid", "states", None),
        P("grid"),
        P("grid", None),
        P(),
    )
    out_specs = P("states", "grid", None, None)
    return jax.shard_map(shards, mesh=mesh, in_specs=in_specs, out_specs=out_specs, check_vma=False)
```

```python
import math

import jax
import jax.numpy as jnp
from jax import lax
from jax.experimental import pallas as pl
from jax.experimental.pallas import tpu as pltpu
from jax.sharding import PartitionSpec as P

RADIUS = 6
PAIR_CAP = 2


MIXED_WEIGHT = 0.7
CENTER = 12.0
HALF_WIDTH = 8.0


def padded_2(shard, sides, width):
    for axis, dim in sides:
        count, length = (lax.axis_size(axis), shard.shape[dim])
        up = [(i, (i + 1) % count) for i in range(count)]
        down = [(j, i) for i, j in up]
        last = lax.slice_in_dim(shard, length - width, length, axis=dim)
        initial = lax.slice_in_dim(shard, 0, width, axis=dim)
        before = lax.ppermute(last, axis, up)
        after = lax.ppermute(initial, axis, down)
        shard = jnp.concatenate([before, shard, after], axis=dim)
    return shard


def second_table(radius):
    weights = [-2.0 * sum((1.0 / (k * k) for k in range(1, radius + 1)))]
    for k in range(1, radius + 1):
        weights.append(
            2.0
            * (-1) ** (k + 1)
            * math.factorial(radius) ** 2
            / (k * k * math.factorial(radius - k) * math.factorial(radius + k))
        )
    return weights


def first_table(radius):
    weights = [0.0]
    for k in range(1, radius + 1):
        weights.append(
            (-1) ** (k + 1)
            * math.factorial(radius) ** 2
            / (k * math.factorial(radius - k) * math.factorial(radius + k))
        )
    return weights


def laplacian(padded, plane_count):
    second_weights = second_table(RADIUS)
    first_weights = first_table(RADIUS)
    interior = padded[:, RADIUS : RADIUS + plane_count]
    line_depth = interior.shape[3]
    z_padded = jnp.pad(interior, ((0, 0), (0, 0), (0, 0), (RADIUS, RADIUS)))
    summed = 3.0 * second_weights[0] * interior
    y_slope = jnp.zeros_like(padded)
    for k in range(1, RADIUS + 1):
        summed = summed + second_weights[k] * (
            padded[:, RADIUS + k : RADIUS + k + plane_count]
            + padded[:, RADIUS - k : RADIUS - k + plane_count]
        )
        summed = summed + second_weights[k] * (jnp.roll(interior, -k, 2) + jnp.roll(interior, k, 2))
        summed = summed + second_weights[k] * (
            z_padded[:, :, :, RADIUS + k : RADIUS + k + line_depth]
            + z_padded[:, :, :, RADIUS - k : RADIUS - k + line_depth]
        )
        y_slope = y_slope + first_weights[k] * (jnp.roll(padded, -k, 2) - jnp.roll(padded, k, 2))
    cross_term = jnp.zeros_like(interior)
    for k in range(1, RADIUS + 1):
        cross_term = cross_term + first_weights[k] * (
            y_slope[:, RADIUS + k : RADIUS + k + plane_count]
            - y_slope[:, RADIUS - k : RADIUS - k + plane_count]
        )
    return summed + MIXED_WEIGHT * cross_term


def make_kernel(scale, with_prev, home_count, proj_count, block_rows):
    sw = second_table(RADIUS)
    fw = first_table(RADIUS)

    def kernel(shift_ref, lo_ref, v_ref, hi_ref, pot_ref, pick_ref, place_ref, proj_ref, gain_ref, *rest):
        if with_prev:
            prev_ref, out_ref, up_ref, down_ref, pad_ref, rows_ref = rest
        else:
            out_ref, up_ref, down_ref, pad_ref, rows_ref = rest
        planes, breadth, depth = v_ref.shape
        v = v_ref[...]
        pad_ref[0:RADIUS] = pltpu.roll(lo_ref[...], shift_ref[0], 1)
        pad_ref[RADIUS:RADIUS + planes] = v
        pad_ref[RADIUS + planes:] = pltpu.roll(hi_ref[...], shift_ref[1], 1)

        lines = v.reshape(planes * breadth, depth).astype(jnp.bfloat16)
        picked = jnp.dot(pick_ref[...], lines, preferred_element_type=jnp.float32)

        def one_atom(a, carry):
            base = pl.multiple_of(a * block_rows, block_rows)
            here = picked_ref_load(base)
            acc = jnp.zeros((block_rows, depth), jnp.float32)
            for j in range(proj_count):
                proj = proj_ref[a * proj_count + j].astype(jnp.float32)
                coef = jnp.sum(jnp.sum(proj * here, axis=0, keepdims=True), axis=1, keepdims=True)
                gain = gain_ref[a * proj_count + j]
                scaled = (coef * gain).astype(jnp.bfloat16).astype(jnp.float32)
                acc = acc + proj * scaled
            rows_ref[pl.ds(base, block_rows), :] = acc.astype(jnp.bfloat16)
            return carry

        rows_ref[...] = picked.astype(jnp.bfloat16)

        def picked_ref_load(base):
            return rows_ref[pl.ds(base, block_rows), :].astype(jnp.float32)

        lax.fori_loop(0, home_count, one_atom, 0, unroll=True)
        nonlocal_lines = jnp.dot(place_ref[...], rows_ref[...], preferred_element_type=jnp.float32)
        nonlocal_lines = nonlocal_lines.reshape(planes, breadth, depth)

        lane = lax.broadcasted_iota(jnp.int32, v.shape, 2)
        summed = (3.0 * sw[0]) * v
        for k in range(1, RADIUS + 1):
            xs = pad_ref[RADIUS + k:RADIUS + k + planes] + pad_ref[RADIUS - k:RADIUS - k + planes]
            ys = pltpu.roll(v, breadth - k, 1) + pltpu.roll(v, k, 1)
            zs = (jnp.where(lane < depth - k, pltpu.roll(v, depth - k, 2), 0.0)
                  + jnp.where(lane >= k, pltpu.roll(v, k, 2), 0.0))
            summed = summed + sw[k] * xs + sw[k] * ys + sw[k] * zs
        padded = pad_ref[...]
        slope = fw[1] * (pltpu.roll(padded, breadth - 1, 1) - pltpu.roll(padded, 1, 1))
        for k in range(2, RADIUS + 1):
            slope = slope + fw[k] * (pltpu.roll(padded, breadth - k, 1) - pltpu.roll(padded, k, 1))
        cross = fw[1] * (slope[RADIUS + 1:RADIUS + 1 + planes] - slope[RADIUS - 1:RADIUS - 1 + planes])
        for k in range(2, RADIUS + 1):
            cross = cross + fw[k] * (slope[RADIUS + k:RADIUS + k + planes] - slope[RADIUS - k:RADIUS - k + planes])
        lap = summed + 0.7 * cross
        hv = -0.5 * lap + pot_ref[...] * v + nonlocal_lines
        kv = (hv - 12.0 * v) / 8.0
        if with_prev:
            result = scale * kv - prev_ref[...]
        else:
            result = kv
        out_ref[...] = result
        up_ref[...] = result[planes - RADIUS:]
        down_ref[...] = result[:RADIUS]

    return kernel


def apply_op(shifts, lo, v, hi, pot, pick, place, proj, gain, prev=None, scale=1.0):
    planes, breadth, depth = v.shape
    picked_rows = pick.shape[0]
    home_count = proj.shape[0] // 8
    block_rows = picked_rows // home_count
    args = [shifts, lo, v, hi, pot, pick, place, proj, gain] + ([prev] if prev is not None else [])
    vspec = pl.BlockSpec(memory_space=pltpu.VMEM)
    in_specs = [pl.BlockSpec(memory_space=pltpu.SMEM)] + [vspec] * (len(args) - 1)
    rim_shape = jax.ShapeDtypeStruct((RADIUS, breadth, depth), jnp.float32)
    return pl.pallas_call(
        make_kernel(scale, prev is not None, home_count, proj.shape[0] // home_count, block_rows),
        out_shape=(jax.ShapeDtypeStruct(v.shape, jnp.float32), rim_shape, rim_shape),
        in_specs=in_specs,
        out_specs=(vspec, vspec, vspec),
        scratch_shapes=[
            pltpu.VMEM((planes + 2 * RADIUS, breadth, depth), jnp.float32),
            pltpu.VMEM((picked_rows, depth), jnp.bfloat16),
        ],
    )(*args)


def shards(states_in, potential, projectors, proj_gains, atom_owner, atom_rows, wrap_rows):
    state_count, tile_width, breadth, line_depth = states_in.shape
    n_grid = lax.axis_size("grid")
    n_states = lax.axis_size("states")
    tile_index = lax.axis_index("grid")
    tile_lines = tile_width * breadth
    block_rows = atom_rows.shape[1]
    line_span = block_rows * line_depth
    proj_count = projectors.shape[2]
    home_count = atom_owner.shape[0]
    slot_pairs = projectors.shape[1]
    row_order = jnp.arange(breadth, dtype=jnp.int32)
    unwrap_rows = jnp.sum(
        row_order[None, :] * (wrap_rows[None, :] == row_order[:, None]).astype(jnp.int32), axis=1
    )
    atom_order = jnp.arange(home_count, dtype=jnp.int32)
    same_owner = (atom_owner[:, None] == atom_owner[None, :]) & (
        atom_order[None, :] < atom_order[:, None]
    )
    owner_rank = jnp.sum(same_owner.astype(jnp.int32), axis=1)
    atom_slot = atom_owner * PAIR_CAP + owner_rank
    local_rows = jnp.where(atom_rows >= 0, atom_rows - tile_index * tile_lines, tile_lines)

    gain_lanes = jnp.zeros((1, slot_pairs, proj_count, 128), jnp.bfloat16)
    gain_lanes = gain_lanes.at[..., 0].set(proj_gains)
    packed = jnp.concatenate([projectors, gain_lanes], axis=3)
    pairs = [(o * n_states + t, t * n_states + o) for o in range(n_grid) for t in range(n_states)]
    packed = lax.ppermute(packed, ("grid", "states"), pairs)
    def flip_y(s):
        return s ^ 8

    def flip_x(s):
        return s ^ 2

    def mirror_x(s):
        x = (s // 2) % 4
        return s + (3 - x - x) * 2

    def flip_core(s):
        return s ^ 1

    exchanges = (flip_y, flip_x, mirror_x, flip_core)

    def origins(me, done):
        if not done:
            return [me]
        return origins(me, done[:-1]) + origins(done[-1](me), done[:-1])

    gathered = packed[0]
    for exchange in exchanges:
        partner = lax.ppermute(
            gathered, "states", [(s, exchange(s)) for s in range(n_states)]
        )
        gathered = jnp.concatenate([gathered, partner], axis=0)
    block_owner = jnp.stack(origins(lax.axis_index("states"), exchanges))
    owner_block = jnp.argmax(block_owner[None, :] == atom_owner[:, None], axis=1)
    gathered = gathered.reshape(n_states * slot_pairs, proj_count, line_span + 128)
    atom_slot = owner_block * PAIR_CAP + owner_rank
    atom_pack = jnp.take(gathered, atom_slot, axis=0)
    proj_rows = atom_pack[:, :, :line_span].reshape(home_count * proj_count, line_span)
    atom_gain = atom_pack[:, :, line_span].astype(jnp.float32)
    pick = (
        local_rows.reshape(-1)[:, None] == jnp.arange(tile_lines, dtype=jnp.int32)[None, :]
    ).astype(jnp.bfloat16)
    place = pick.T
    proj_in = proj_rows.reshape(home_count * proj_count, breadth, line_depth)
    gain_in = jnp.broadcast_to(
        atom_gain.reshape(home_count * proj_count, 1, 1), (home_count * proj_count, 1, line_depth)
    )
    skew = wrap_rows[0]
    shifts = jnp.stack(
        [
            jnp.where(tile_index == 0, (breadth - skew) % breadth, 0),
            jnp.where(tile_index == n_grid - 1, skew, 0),
            jnp.zeros((), jnp.int32),
            jnp.zeros((), jnp.int32),
        ]
    ).astype(jnp.int32)
    up = [(i, (i + 1) % n_grid) for i in range(n_grid)]
    down = [(j, i) for i, j in up]

    def step(field, send_up, send_down, prev=None, scale=1.0):
        high_rim = lax.ppermute(send_down, "grid", down)
        low_rim = lax.ppermute(send_up, "grid", up)
        return apply_op(
            shifts, low_rim, field, high_rim, potential, pick, place, proj_in, gain_in, prev, scale
        )

    field = states_in[0]
    first_term = step(field, field[tile_width - RADIUS :], field[:RADIUS])
    second_term = step(*first_term, field, 2.0)
    filtered = step(*second_term, first_term[0], 2.0)
    return filtered[0][None]


def solution(mesh):
    in_specs = (
        P("states", "grid", None, None),
        P("grid", None, None),
        P("grid", "states", None, None),
        P("grid", "states", None),
        P("grid"),
        P("grid", None),
        P(),
    )
    out_specs = P("states", "grid", None, None)
    return jax.shard_map(shards, mesh=mesh, in_specs=in_specs, out_specs=out_specs, check_vma=False)
```
